32 devices in a mesh: rep: 4 (over z), sy: 2 (over y), sx: 4 (over x, core).
Axes of the slice: x: 2, y: 2, z: 4, core: 2. Of those that a mesh axis runs over, the one named last changes fastest.
Arguments:
- features: bfloat16 [4, 32, 64, 256], P('rep', 'sy', 'sx'), may hold values from -1.5 to 1.5
- cotangent: bfloat16 [4, 32, 64, 256], P('rep', 'sy', 'sx'), may hold values from -15 to 15
- gain_conv: float32 [256], replicated, may hold values from 0.25 to 1.75
- expand_weight: bfloat16 [256, 1024], replicated, may hold values from -0.375 to 0.375
- dw_kernel: float32 [1024, 9], replicated, may hold values from -2 to 2
- project_weight: bfloat16 [1024, 256], replicated, may hold values from -0.1875 to 0.1875
- gain_block: float32 [256], replicated, may hold values from 0.25 to 1.75
- block_inward: bfloat16 [256, 768], replicated, may hold values from -0.375 to 0.375
- block_outward: bfloat16 [256, 256], replicated, may hold values from -0.375 to 0.375
- gain_grid: float32 [256], replicated, may hold values from 0.25 to 1.75
- grid_inward: bfloat16 [256, 768], replicated, may hold values from -0.375 to 0.375
- grid_outward: bfloat16 [256, 256], replicated, may hold values from -0.375 to 0.375
Outputs:
- output_tokens: bfloat16 [4, 32, 64, 256], P('rep', 'sy', 'sx')
- token_grads: bfloat16 [4, 32, 64, 256], P('rep', 'sy', 'sx')
- grad_conv_gain: float32 [256], P('rep')
- grad_expand: float32 [256, 1024], P('rep')
- grad_kernel: float32 [1024, 9], P('rep')
- grad_project: float32 [1024, 256], P('rep')
- grad_block_gain: float32 [256], P('rep')
- grad_block_inward: float32 [256, 768], P('rep')
- grad_block_outward: float32 [256, 256], P('rep')
- grad_grid_gain: float32 [256], P('rep')
- grad_grid_inward: float32 [256, 768], P('rep')
- grad_grid_outward: float32 [256, 256], P('rep')
The draws below stay inside these ranges and needn't reach their ends.
All inputs are finite; a program needn't handle non-finite values.
Results may differ from the reference program's by a relative error of at most 0.018.
Values may be sent and summed in bfloat16 or wider, within the bound.
No kernel may reach another device: no remote copies, remote signals or barrier semaphores. Data moves between devices by JAX's collectives and lax.ppermute only.
A program may use at most 64 MiB of HBM per device.

```python
import math
import jax
import jax.numpy as jnp
from jax import lax

DIM = 256
HEADS = 8
EXPAND = 1024
WIN = 8
SAMPLES = 4
GRID_H = 32
GRID_W = 64


def draw_cotangent(key, part):
    normal_part = jax.random.normal(key, (SAMPLES, GRID_H, GRID_W, DIM), jnp.float32)
    row_place = jnp.arange(GRID_H, dtype=jnp.float32) / max(GRID_H - 1, 1)
    col_place = jnp.arange(GRID_W, dtype=jnp.float32) / max(GRID_W - 1, 1)
    cell_scale = jnp.exp(math.log(3.0) * (row_place[:, None] + col_place[None, :] - 1.0))
    bounded = jnp.clip(normal_part, -5.0, 5.0)
    return (bounded * cell_scale[None, :, :, None]).astype(jnp.bfloat16)


def block_levels(rng, dims, split, smallest, top_value):
    level, own = 1.0, jax.random.fold_in(rng, 6)
    for position, shards_of in split:
        draws = jnp.exp(jax.random.uniform(jax.random.fold_in(own, position), (shards_of,), jnp.float32, smallest / len(split), top_value / len(split)))
        level = level * jnp.repeat(draws, dims[position] // shards_of).reshape([-1 if axis == position else 1 for axis in range(len(dims))])
    return level


def noise(rng, shape, scale, limit, cuts=(), kind=jnp.bfloat16):
    loudness = block_levels(rng, shape, cuts, -0.22, 0.18) if cuts else 1.0
    values = jax.random.normal(rng, shape, jnp.float32) * scale * loudness
    return jnp.minimum(jnp.maximum(values, -limit), limit).astype(kind)


def setup_inputs(seed: int = 0) -> dict:
    key_list = jax.random.split(jax.random.key(seed), 13)
    return {
        "features": noise(key_list[0], (SAMPLES, GRID_H, GRID_W, DIM), 0.25, 1.5, ((0, 4), (1, 2), (2, 4))),
        "cotangent": draw_cotangent(jax.random.fold_in(key_list[12], 71), 0),
        "gain_conv": jnp.clip(1.0 + 0.15 * jax.random.normal(key_list[2], (DIM,), jnp.float32), 0.25, 1.75),
        "expand_weight": noise(key_list[3], (DIM, EXPAND), DIM ** -0.5, 0.375),
        "dw_kernel": noise(key_list[4], (EXPAND, 9), 9 ** -0.5, 2.0, (), jnp.float32),
        "project_weight": noise(key_list[5], (EXPAND, DIM), EXPAND ** -0.5, 0.1875),
        "gain_block": jnp.clip(1.0 + 0.15 * jax.random.normal(key_list[6], (DIM,), jnp.float32), 0.25, 1.75),
        "block_inward": noise(key_list[7], (DIM, 3 * DIM), DIM ** -0.5, 0.375),
        "block_outward": noise(key_list[8], (DIM, DIM), DIM ** -0.5, 0.375),
        "gain_grid": jnp.clip(1.0 + 0.15 * jax.random.normal(key_list[9], (DIM,), jnp.float32), 0.25, 1.75),
        "grid_inward": noise(key_list[10], (DIM, 3 * DIM), DIM ** -0.5, 0.375),
        "grid_outward": noise(key_list[11], (DIM, DIM), DIM ** -0.5, 0.375),
    }


EPSILON = 1e-05

def widen(values):
    return lax.optimization_barrier(values).astype(jnp.float32)

def layer_norm(values, gain):
    row_mean = lax.optimization_barrier(jnp.mean(values, axis=-1, keepdims=True))
    centred = values - row_mean
    variance = lax.optimization_barrier(jnp.mean(centred * centred, axis=-1, keepdims=True))
    return centred * lax.rsqrt(variance + EPSILON) * gain

def project_rows(values, weight):
    leading = values.shape[:-1]
    flattened = values.reshape(-1, values.shape[-1])
    product = jnp.dot(flattened, weight, preferred_element_type=jnp.float32)
    return product.reshape(leading + (weight.shape[1],))

def outer_sum(left_side, right_side):
    left_flat = left_side.reshape(-1, left_side.shape[-1])
    right_flat = right_side.reshape(-1, right_side.shape[-1]).astype(jnp.bfloat16)
    return lax.dot_general(left_flat, right_flat, (((0,), (0,)), ((), ())), preferred_element_type=jnp.float32)

def to_windows(image, side):
    height, breadth, channels = image.shape
    blocks = image.reshape(height // side, side, breadth // side, side, channels)
    return blocks.transpose(0, 2, 1, 3, 4).reshape(-1, side * side, channels)

def from_windows(windows, height, breadth, side):
    channels = windows.shape[-1]
    blocks = windows.reshape(height // side, breadth // side, side, side, channels)
    return blocks.transpose(0, 2, 1, 3, 4).reshape(height, breadth, channels)

def to_grid(image, side):
    height, breadth, channels = image.shape
    blocks = image.reshape(side, height // side, side, breadth // side, channels)
    return blocks.transpose(1, 3, 0, 2, 4).reshape(-1, side * side, channels)

def from_grid(windows, height, breadth, side):
    channels = windows.shape[-1]
    blocks = windows.reshape(height // side, breadth // side, side, side, channels)
    return blocks.transpose(2, 0, 3, 1, 4).reshape(height, breadth, channels)

def window_attention(windows, weight, tap_in, heads):
    count, members, channels = windows.shape
    head_width = channels // heads
    qkv_rows = widen((project_rows(windows, weight) + tap_in).astype(jnp.bfloat16))
    queries = qkv_rows[..., :channels].reshape(count, members, heads, head_width)
    key_rows = qkv_rows[..., channels:2 * channels].reshape(count, members, heads, head_width)
    value_rows = qkv_rows[..., 2 * channels:].reshape(count, members, heads, head_width)
    scores = jnp.einsum('wqhd,wkhd->whqk', queries, key_rows, precision=lax.Precision.HIGHEST) * head_width ** (-0.5)
    softmax_out = widen(jax.nn.softmax(scores, axis=-1).astype(jnp.bfloat16))
    attended = jnp.einsum('whqk,wkhd->wqhd', softmax_out, value_rows, precision=lax.Precision.HIGHEST)
    return attended.astype(jnp.bfloat16).reshape(count, members, channels)

def depthwise(inner, kernel):
    height, breadth = (inner.shape[0], inner.shape[1])
    padded = jnp.pad(widen(inner), ((1, 1), (1, 1), (0, 0)))
    summed = jnp.zeros(inner.shape, jnp.float32)
    for tap_index in range(9):
        row_step, col_step = divmod(tap_index, 3)
        summed = summed + padded[row_step:row_step + height, col_step:col_step + breadth] * kernel[:, tap_index]
    return summed

def reference(features, cotangent, gain_conv, expand_weight, dw_kernel, project_weight, gain_block, block_inward, block_outward, gain_grid, grid_inward, grid_outward):

    def one_image(paired):
        image, image_cot = paired
        height, breadth, channels = image.shape
        expand_units = expand_weight.shape[1]
        window_count = height * breadth // (WIN * WIN)

        def forward(widened, gain_one, kernel_in, gain_two, gain_three, tap_list):
            tap_expand, tap_project, tap_block_in, tap_block_out, tap_grid_in, tap_grid_out = tap_list
            normed = layer_norm(widened, gain_one).astype(jnp.bfloat16)
            inner = jax.nn.gelu(project_rows(normed, expand_weight) + tap_expand).astype(jnp.bfloat16)
            conv_out = depthwise(inner, kernel_in)
            activated = jax.nn.gelu(conv_out).astype(jnp.bfloat16)
            stream_one = widened + project_rows(activated, project_weight) + tap_project
            normed_two = layer_norm(stream_one, gain_two).astype(jnp.bfloat16)
            block_windows = to_windows(normed_two, WIN)
            block_home = from_windows(window_attention(block_windows, block_inward, tap_block_in, HEADS), height, breadth, WIN)
            stream_two = stream_one + project_rows(block_home, block_outward) + tap_block_out
            normed_three = layer_norm(stream_two, gain_three).astype(jnp.bfloat16)
            grid_windows = to_grid(normed_three, WIN)
            grid_home = from_grid(window_attention(grid_windows, grid_inward, tap_grid_in, HEADS), height, breadth, WIN)
            result = (stream_two + project_rows(grid_home, grid_outward) + tap_grid_out).astype(jnp.bfloat16)
            return (result, (normed, activated, block_windows, block_home, grid_windows, grid_home))
        tap_list = (jnp.zeros((height, breadth, expand_units), jnp.float32), jnp.zeros((height, breadth, channels), jnp.float32), jnp.zeros((window_count, WIN * WIN, 3 * channels), jnp.float32), jnp.zeros((height, breadth, channels), jnp.float32), jnp.zeros((window_count, WIN * WIN, 3 * channels), jnp.float32), jnp.zeros((height, breadth, channels), jnp.float32))
        widened = image.astype(jnp.float32)
        result, backward, saved = jax.vjp(forward, widened, gain_conv, dw_kernel, gain_block, gain_grid, tap_list, has_aux=True)
        d_wide, d_gain_one, d_kernel, d_gain_two, d_gain_three, d_taps = backward(image_cot)
        gradients = (d_gain_one, outer_sum(saved[0], d_taps[0]), d_kernel, outer_sum(saved[1], d_taps[1]), d_gain_two, outer_sum(saved[2], d_taps[2]), outer_sum(saved[3], d_taps[3]), d_gain_three, outer_sum(saved[4], d_taps[4]), outer_sum(saved[5], d_taps[5]))
        return (result, d_wide.astype(jnp.bfloat16), gradients)
    results, token_grads, stacked = lax.map(one_image, (features, cotangent))
    return (results, token_grads, lax.optimization_barrier(jnp.sum(stacked[0], axis=0)), lax.optimization_barrier(jnp.sum(stacked[1], axis=0)), lax.optimization_barrier(jnp.sum(stacked[2], axis=0)), lax.optimization_barrier(jnp.sum(stacked[3], axis=0)), lax.optimization_barrier(jnp.sum(stacked[4], axis=0)), lax.optimization_barrier(jnp.sum(stacked[5], axis=0)), lax.optimization_barrier(jnp.sum(stacked[6], axis=0)), lax.optimization_barrier(jnp.sum(stacked[7], axis=0)), lax.optimization_barrier(jnp.sum(stacked[8], axis=0)), lax.optimization_barrier(jnp.sum(stacked[9], axis=0)))
```

```python
import jax
import jax.numpy as jnp
from jax import lax
from jax.sharding import PartitionSpec as P

HEADS = 8
WIN = 8


EPSILON = 1e-05


def as_sent(value):

    def short(part):
        return part.astype(jnp.bfloat16) if part.dtype == jnp.float32 else part

    return jax.tree.map(short, value)


def extended_2(cells, sides, width):
    for axis, dim in sides:
        count = lax.axis_size(axis)
        ends = count - 1
        head = lax.slice_in_dim(cells, 0, width, axis=dim)
        tail = lax.slice_in_dim(cells, cells.shape[dim] - width, cells.shape[dim], axis=dim)
        cells = jnp.concatenate(
            [
                lax.ppermute(tail, axis, [(i, (i + 1) % count) for i in range(ends)]),
                cells,
                lax.ppermute(head, axis, [((i + 1) % count, i) for i in range(ends)]),
            ],
            axis=dim,
        )
    return cells


def widen(values):
    return lax.optimization_barrier(values).astype(jnp.float32)


def layer_norm(values, gain):
    row_mean = jnp.mean(values, axis=-1, keepdims=True)
    centred = values - row_mean
    variance = jnp.mean(centred * centred, axis=-1, keepdims=True)
    return centred * lax.rsqrt(variance + EPSILON) * gain


def project_rows(values, weight):
    leading = values.shape[:-1]
    flattened = values.reshape(-1, values.shape[-1])
    product = jnp.dot(flattened, weight, preferred_element_type=jnp.float32)
    return product.reshape(leading + (weight.shape[1],))


def outer_sum(left_side, right_side):
    left_flat = left_side.reshape(-1, left_side.shape[-1])
    right_flat = right_side.reshape(-1, right_side.shape[-1]).astype(jnp.bfloat16)
    return lax.dot_general(
        left_flat, right_flat, (((0,), (0,)), ((), ())), preferred_element_type=jnp.float32
    )


def to_windows(image, side):
    height, breadth, channels = image.shape
    blocks = image.reshape(height // side, side, breadth // side, side, channels)
    return blocks.transpose(0, 2, 1, 3, 4).reshape(-1, side * side, channels)


def from_windows(windows, height, breadth, side):
    channels = windows.shape[-1]
    blocks = windows.reshape(height // side, breadth // side, side, side, channels)
    return blocks.transpose(0, 2, 1, 3, 4).reshape(height, breadth, channels)


def to_grid(image, side):
    height, breadth, channels = image.shape
    blocks = image.reshape(side, height // side, side, breadth // side, channels)
    return blocks.transpose(1, 3, 0, 2, 4).reshape(-1, side * side, channels)


def from_grid(windows, height, breadth, side):
    channels = windows.shape[-1]
    blocks = windows.reshape(height // side, breadth // side, side, side, channels)
    return blocks.transpose(2, 0, 3, 1, 4).reshape(height, breadth, channels)


def window_attention(windows, weight, tap_in, heads):
    count, members, channels = windows.shape
    head_width = channels // heads
    qkv_rows = (project_rows(windows, weight) + tap_in).astype(jnp.bfloat16)
    queries = qkv_rows[..., :channels].reshape(count, members, heads, head_width)
    key_rows = qkv_rows[..., channels : 2 * channels].reshape(count, members, heads, head_width)
    value_rows = qkv_rows[..., 2 * channels :].reshape(count, members, heads, head_width)
    scores = jnp.einsum(
        "wqhd,wkhd->whqk", queries, key_rows, preferred_element_type=jnp.float32
    ) * head_width ** (-0.5)
    softmax_out = jax.nn.softmax(scores, axis=-1).astype(jnp.bfloat16)
    attended = jnp.einsum(
        "whqk,wkhd->wqhd", softmax_out, value_rows, preferred_element_type=jnp.float32
    )
    return attended.astype(jnp.bfloat16).reshape(count, members, channels)


def depthwise(extended, kernel):
    height = extended.shape[0] - 2
    breadth = extended.shape[1] - 2
    widened = widen(extended)
    summed = jnp.zeros((height, breadth, extended.shape[2]), jnp.float32)
    for tap_index in range(9):
        row_step, col_step = divmod(tap_index, 3)
        summed = (
            summed
            + widened[row_step : row_step + height, col_step : col_step + breadth]
            * kernel[:, tap_index]
        )
    return summed


def depthwise_back(grad_ext, kernel):
    height = grad_ext.shape[0] - 2
    breadth = grad_ext.shape[1] - 2
    summed = jnp.zeros((height, breadth, grad_ext.shape[2]), jnp.float32)
    for tap_index in range(9):
        row_step, col_step = divmod(tap_index, 3)
        summed = (
            summed
            + grad_ext[2 - row_step : 2 - row_step + height, 2 - col_step : 2 - col_step + breadth]
            * kernel[:, tap_index]
        )
    return summed


def swap_blocks(blocks):
    sy_count, sx_count, row_part, col_part, channels = blocks.shape
    flattened = blocks.reshape(sy_count * sx_count, row_part, col_part, channels)
    moved = lax.all_to_all(
        as_sent(flattened), ("sy", "sx"), split_axis=0, concat_axis=0, tiled=True
    ).astype(flattened.dtype)
    return moved.reshape(blocks.shape)


def to_exchanged(image):
    height, breadth, channels = image.shape
    sy_count = lax.axis_size("sy")
    sx_count = lax.axis_size("sx")
    blocks = image.reshape(height // sy_count, sy_count, breadth // sx_count, sx_count, channels)
    moved = swap_blocks(blocks.transpose(1, 3, 0, 2, 4))
    return moved.transpose(0, 2, 1, 3, 4).reshape(height, breadth, channels)


def to_home(image):
    height, breadth, channels = image.shape
    sy_count = lax.axis_size("sy")
    sx_count = lax.axis_size("sx")
    blocks = image.reshape(sy_count, height // sy_count, sx_count, breadth // sx_count, channels)
    moved = swap_blocks(blocks.transpose(0, 2, 1, 3, 4))
    return moved.transpose(2, 0, 3, 1, 4).reshape(height, breadth, channels)


def reduce_grads(grads, groups):
    parts = lax.axis_size("rep")
    results = [None] * len(grads)
    for group in groups:
        pieces = [grads[i].reshape(parts, -1) for i in group]
        sizes = [piece.shape[1] for piece in pieces]
        width = sum(sizes)
        padded = -(-width // 1024) * 1024
        packed = jnp.concatenate(pieces + [jnp.zeros((parts, padded - width), jnp.float32)], axis=1)
        whole = lax.psum(packed, ("rep", "sy", "sx"))
        total = lax.dynamic_index_in_dim(whole, lax.axis_index("rep"), 0, keepdims=False)
        offset = 0
        for index, size in zip(group, sizes):
            shape = (grads[index].shape[0] // parts,) + grads[index].shape[1:]
            results[index] = total[offset : offset + size].reshape(shape)
            offset += size
    return tuple(results)


def body(
    features,
    cotangent,
    gain_conv,
    expand_weight,
    dw_kernel,
    project_weight,
    gain_block,
    block_inward,
    block_outward,
    gain_grid,
    grid_inward,
    grid_outward,
):
    image = features[0]
    height, breadth, channels = image.shape
    expand_units = expand_weight.shape[1]
    window_count = height * breadth // (WIN * WIN)
    zero_width = jnp.zeros((height, breadth, channels), jnp.float32)
    zero_expand = jnp.zeros((height, breadth, expand_units), jnp.float32)
    zero_qkv = jnp.zeros((window_count, WIN * WIN, 3 * channels), jnp.float32)
    widened = image.astype(jnp.float32)

    def conv_front(wide_in, gain_in):
        return layer_norm(wide_in, gain_in).astype(jnp.bfloat16)

    normed, front_back = jax.vjp(conv_front, widened, gain_conv)

    def expand_fn(normed_in, tap_in):
        return jax.nn.gelu(project_rows(normed_in, expand_weight) + tap_in).astype(jnp.bfloat16)

    inner, expand_back = jax.vjp(expand_fn, normed, zero_expand)
    inner_ext = extended_2(inner, (("sy", 0), ("sx", 1)), 1)

    def conv_only(kernel_in):
        return depthwise(inner_ext, kernel_in)

    conv_out, kernel_back = jax.vjp(conv_only, dw_kernel)

    def conv_tail(conv_in, wide_in, tap_in):
        activated_in = jax.nn.gelu(conv_in).astype(jnp.bfloat16)
        return (wide_in + project_rows(activated_in, project_weight) + tap_in, activated_in)

    stream_one, tail_back, activated = jax.vjp(
        conv_tail, conv_out, widened, zero_width, has_aux=True
    )

    def block_layer(stream_in, gain_in, tap_in, tap_out):
        normed_two = layer_norm(stream_in, gain_in).astype(jnp.bfloat16)
        windows = to_windows(normed_two, WIN)
        attended = window_attention(windows, block_inward, tap_in, HEADS)
        attended_home = from_windows(attended, height, breadth, WIN)
        return (
            stream_in + project_rows(attended_home, block_outward) + tap_out,
            (windows, attended_home),
        )

    stream_two, block_back, block_saved = jax.vjp(
        block_layer, stream_one, gain_block, zero_qkv, zero_width, has_aux=True
    )

    def grid_front(stream_in, gain_in):
        return layer_norm(stream_in, gain_in).astype(jnp.bfloat16)

    normed_three, grid_front_back = jax.vjp(grid_front, stream_two, gain_grid)
    grid_windows = to_grid(to_exchanged(normed_three), WIN)

    def grid_core(windows_in, tap_in):
        return window_attention(windows_in, grid_inward, tap_in, HEADS)

    grid_attended, grid_core_back = jax.vjp(grid_core, grid_windows, zero_qkv)
    grid_home = to_home(from_grid(grid_attended, height, breadth, WIN))

    def grid_tail(stream_in, attended_in, tap_in):
        return (stream_in + project_rows(attended_in, grid_outward) + tap_in).astype(jnp.bfloat16)

    output_tile, grid_tail_back = jax.vjp(grid_tail, stream_two, grid_home, zero_width)
    d_stream_two, d_grid_home, tap_grid_out = grid_tail_back(cotangent[0])
    d_grid_attended = to_grid(to_exchanged(d_grid_home), WIN)
    d_grid_windows, tap_grid_in = grid_core_back(d_grid_attended)
    d_normed_three = to_home(from_grid(d_grid_windows, height, breadth, WIN))
    d_stream_extra, d_gain_grid = grid_front_back(d_normed_three)
    d_stream_two = d_stream_two + d_stream_extra
    d_stream_one, d_gain_block, tap_block_in, tap_block_out = block_back(d_stream_two)
    d_conv, d_wide_tail, tap_project = tail_back(d_stream_one)
    d_conv_ext = extended_2(d_conv, (("sy", 0), ("sx", 1)), 1)
    d_kernel = kernel_back(d_conv)[0]
    d_inner = depthwise_back(d_conv_ext, dw_kernel).astype(jnp.bfloat16)
    d_normed, tap_expand = expand_back(d_inner)
    d_wide_front, d_gain_conv = front_back(d_normed)
    token_grad = (d_wide_tail + d_wide_front).astype(jnp.bfloat16)
    local_grads = (
        d_gain_conv,
        outer_sum(normed, tap_expand),
        d_kernel,
        outer_sum(activated, tap_project),
        d_gain_block,
        outer_sum(block_saved[0], tap_block_in),
        outer_sum(block_saved[1], tap_block_out),
        d_gain_grid,
        outer_sum(grid_windows, tap_grid_in),
        outer_sum(grid_home, tap_grid_out),
    )
    summed = reduce_grads(local_grads, ((0, 1, 2, 3, 4, 5, 6, 7, 8, 9),))
    return (
        output_tile[None],
        token_grad[None],
        summed[0],
        summed[1],
        summed[2],
        summed[3],
        summed[4],
        summed[5],
        summed[6],
        summed[7],
        summed[8],
        summed[9],
    )


def solution(mesh):
    return jax.shard_map(
        body,
        mesh=mesh,
        in_specs=(
            P("rep", "sy", "sx", None),
            P("rep", "sy", "sx", None),
            P(),
            P(),
            P(),
            P(),
            P(),
            P(),
            P(),
            P(),
            P(),
            P(),
        ),
        out_specs=(
            P("rep", "sy", "sx", None),
            P("rep", "sy", "sx", None),
            P("rep"),
            P("rep", None),
            P("rep", None),
            P("rep", None),
            P("rep"),
            P("rep", None),
            P("rep", None),
            P("rep"),
            P("rep", None),
            P("rep", None),
        ),
        check_vma=False,
    )
```

```python
import jax
import jax.numpy as jnp
from jax import lax
from jax.sharding import PartitionSpec as P

HEADS = 8
WIN = 8


EPSILON = 1e-05


def as_sent(value):

    def short(part):
        return part.astype(jnp.bfloat16) if part.dtype == jnp.float32 else part

    return jax.tree.map(short, value)


def extended_2(cells, sides, width):
    for axis, dim in sides:
        count = lax.axis_size(axis)
        ends = count - 1
        head = lax.slice_in_dim(cells, 0, width, axis=dim)
        tail = lax.slice_in_dim(cells, cells.shape[dim] - width, cells.shape[dim], axis=dim)
        cells = jnp.concatenate(
            [
                lax.ppermute(tail, axis, [(i, (i + 1) % count) for i in range(ends)]),
                cells,
                lax.ppermute(head, axis, [((i + 1) % count, i) for i in range(ends)]),
            ],
            axis=dim,
        )
    return cells


def widen(values):
    return lax.optimization_barrier(values).astype(jnp.float32)


def layer_norm(values, gain):
    row_mean = jnp.mean(values, axis=-1, keepdims=True)
    centred = values - row_mean
    variance = jnp.mean(centred * centred, axis=-1, keepdims=True)
    return centred * lax.rsqrt(variance + EPSILON) * gain


def project_rows(values, weight):
    leading = values.shape[:-1]
    flattened = values.reshape(-1, values.shape[-1])
    product = jnp.dot(flattened, weight, preferred_element_type=jnp.float32)
    return product.reshape(leading + (weight.shape[1],))


def outer_sum(left_side, right_side):
    left_flat = left_side.reshape(-1, left_side.shape[-1])
    right_flat = right_side.reshape(-1, right_side.shape[-1]).astype(jnp.bfloat16)
    return lax.dot_general(
        left_flat, right_flat, (((0,), (0,)), ((), ())), preferred_element_type=jnp.float32
    )


def to_windows(image, side):
    height, breadth, channels = image.shape
    blocks = image.reshape(height // side, side, breadth // side, side, channels)
    return blocks.transpose(0, 2, 1, 3, 4).reshape(-1, side * side, channels)


def from_windows(windows, height, breadth, side):
    channels = windows.shape[-1]
    blocks = windows.reshape(height // side, breadth // side, side, side, channels)
    return blocks.transpose(0, 2, 1, 3, 4).reshape(height, breadth, channels)


def to_grid(image, side):
    height, breadth, channels = image.shape
    blocks = image.reshape(side, height // side, side, breadth // side, channels)
    return blocks.transpose(1, 3, 0, 2, 4).reshape(-1, side * side, channels)


def from_grid(windows, height, breadth, side):
    channels = windows.shape[-1]
    blocks = windows.reshape(height // side, breadth // side, side, side, channels)
    return blocks.transpose(2, 0, 3, 1, 4).reshape(height, breadth, channels)


def window_attention(windows, weight, tap_in, heads):
    count, members, channels = windows.shape
    head_width = channels // heads
    qkv_rows = (project_rows(windows, weight) + tap_in).astype(jnp.bfloat16)
    queries = qkv_rows[..., :channels].reshape(count, members, heads, head_width)
    key_rows = qkv_rows[..., channels : 2 * channels].reshape(count, members, heads, head_width)
    value_rows = qkv_rows[..., 2 * channels :].reshape(count, members, heads, head_width)
    scores = jnp.einsum(
        "wqhd,wkhd->whqk", queries, key_rows, preferred_element_type=jnp.float32
    ) * head_width ** (-0.5)
    softmax_out = jax.nn.softmax(scores, axis=-1).astype(jnp.bfloat16)
    attended = jnp.einsum(
        "whqk,wkhd->wqhd", softmax_out, value_rows, preferred_element_type=jnp.float32
    )
    return attended.astype(jnp.bfloat16).reshape(count, members, channels)


def depthwise(extended, kernel):
    height = extended.shape[0] - 2
    breadth = extended.shape[1] - 2
    widened = widen(extended)
    summed = jnp.zeros((height, breadth, extended.shape[2]), jnp.float32)
    for tap_index in range(9):
        row_step, col_step = divmod(tap_index, 3)
        summed = (
            summed
            + widened[row_step : row_step + height, col_step : col_step + breadth]
            * kernel[:, tap_index]
        )
    return summed


def depthwise_back(grad_ext, kernel):
    height = grad_ext.shape[0] - 2
    breadth = grad_ext.shape[1] - 2
    summed = jnp.zeros((height, breadth, grad_ext.shape[2]), jnp.float32)
    for tap_index in range(9):
        row_step, col_step = divmod(tap_index, 3)
        summed = (
            summed
            + grad_ext[2 - row_step : 2 - row_step + height, 2 - col_step : 2 - col_step + breadth]
            * kernel[:, tap_index]
        )
    return summed


def swap_blocks(blocks):
    sy_count, sx_count, row_part, col_part, channels = blocks.shape
    flattened = blocks.reshape(sy_count * sx_count, row_part, col_part, channels)
    moved = lax.all_to_all(
        as_sent(flattened), ("sy", "sx"), split_axis=0, concat_axis=0, tiled=True
    ).astype(flattened.dtype)
    return moved.reshape(blocks.shape)


def to_exchanged(image):
    height, breadth, channels = image.shape
    sy_count = lax.axis_size("sy")
    sx_count = lax.axis_size("sx")
    blocks = image.reshape(height // sy_count, sy_count, breadth // sx_count, sx_count, channels)
    moved = swap_blocks(blocks.transpose(1, 3, 0, 2, 4))
    return moved.transpose(0, 2, 1, 3, 4).reshape(height, breadth, channels)


def to_home(image):
    height, breadth, channels = image.shape
    sy_count = lax.axis_size("sy")
    sx_count = lax.axis_size("sx")
    blocks = image.reshape(sy_count, height // sy_count, sx_count, breadth // sx_count, channels)
    moved = swap_blocks(blocks.transpose(0, 2, 1, 3, 4))
    return moved.transpose(2, 0, 3, 1, 4).reshape(height, breadth, channels)


def reduce_grads(grads, groups):
    parts = lax.axis_size("rep")
    results = [None] * len(grads)
    for group in groups:
        pieces = [grads[i].reshape(parts, -1) for i in group]
        sizes = [piece.shape[1] for piece in pieces]
        width = sum(sizes)
        padded = -(-width // 8192) * 8192
        packed = jnp.concatenate(pieces + [jnp.zeros((parts, padded - width), jnp.float32)], axis=1)
        tiles = lax.axis_size(("sy", "sx"))
        local = packed.reshape(parts, tiles, padded // tiles).transpose(1, 0, 2)
        local = local.reshape(tiles * parts * 8, padded // tiles // 8)
        local = lax.psum_scatter(local, ("sy", "sx"), scatter_dimension=0, tiled=True)
        local = lax.psum_scatter(local, "rep", scatter_dimension=0, tiled=True)
        total = lax.all_gather(local, ("sy", "sx"), axis=0, tiled=True).reshape(-1)
        offset = 0
        for index, size in zip(group, sizes):
            shape = (grads[index].shape[0] // parts,) + grads[index].shape[1:]
            results[index] = total[offset : offset + size].reshape(shape)
            offset += size
    return tuple(results)


def body(
    features,
    cotangent,
    gain_conv,
    expand_weight,
    dw_kernel,
    project_weight,
    gain_block,
    block_inward,
    block_outward,
    gain_grid,
    grid_inward,
    grid_outward,
):
    image = features[0]
    height, breadth, channels = image.shape
    expand_units = expand_weight.shape[1]
    window_count = height * breadth // (WIN * WIN)
    zero_width = jnp.zeros((height, breadth, channels), jnp.float32)
    zero_expand = jnp.zeros((height, breadth, expand_units), jnp.float32)
    zero_qkv = jnp.zeros((window_count, WIN * WIN, 3 * channels), jnp.float32)
    widened = image.astype(jnp.float32)

    def conv_front(wide_in, gain_in):
        return layer_norm(wide_in, gain_in).astype(jnp.bfloat16)

    normed, front_back = jax.vjp(conv_front, widened, gain_conv)

    def expand_fn(normed_in, tap_in):
        return jax.nn.gelu(project_rows(normed_in, expand_weight) + tap_in).astype(jnp.bfloat16)

    inner, expand_back = jax.vjp(expand_fn, normed, zero_expand)
    inner_ext = extended_2(inner, (("sy", 0), ("sx", 1)), 1)

    def conv_only(kernel_in):
        return depthwise(inner_ext, kernel_in)

    conv_out, kernel_back = jax.vjp(conv_only, dw_kernel)

    def conv_tail(conv_in, wide_in, tap_in):
        activated_in = jax.nn.gelu(conv_in).astype(jnp.bfloat16)
        return (wide_in + project_rows(activated_in, project_weight) + tap_in, activated_in)

    stream_one, tail_back, activated = jax.vjp(
        conv_tail, conv_out, widened, zero_width, has_aux=True
    )

    def block_layer(stream_in, gain_in, tap_in, tap_out):
        normed_two = layer_norm(stream_in, gain_in).astype(jnp.bfloat16)
        windows = to_windows(normed_two, WIN)
        attended = window_attention(windows, block_inward, tap_in, HEADS)
        attended_home = from_windows(attended, height, breadth, WIN)
        return (
            stream_in + project_rows(attended_home, block_outward) + tap_out,
            (windows, attended_home),
        )

    stream_two, block_back, block_saved = jax.vjp(
        block_layer, stream_one, gain_block, zero_qkv, zero_width, has_aux=True
    )

    def grid_front(stream_in, gain_in):
        return layer_norm(stream_in, gain_in).astype(jnp.bfloat16)

    normed_three, grid_front_back = jax.vjp(grid_front, stream_two, gain_grid)
    grid_windows = to_grid(to_exchanged(normed_three), WIN)

    def grid_core(windows_in, tap_in):
        return window_attention(windows_in, grid_inward, tap_in, HEADS)

    grid_attended, grid_core_back = jax.vjp(grid_core, grid_windows, zero_qkv)
    grid_home = to_home(from_grid(grid_attended, height, breadth, WIN))

    def grid_tail(stream_in, attended_in, tap_in):
        return (stream_in + project_rows(attended_in, grid_outward) + tap_in).astype(jnp.bfloat16)

    output_tile, grid_tail_back = jax.vjp(grid_tail, stream_two, grid_home, zero_width)
    d_stream_two, d_grid_home, tap_grid_out = grid_tail_back(cotangent[0])
    d_grid_attended = to_grid(to_exchanged(d_grid_home), WIN)
    d_grid_windows, tap_grid_in = grid_core_back(d_grid_attended)
    d_normed_three = to_home(from_grid(d_grid_windows, height, breadth, WIN))
    d_stream_extra, d_gain_grid = grid_front_back(d_normed_three)
    d_stream_two = d_stream_two + d_stream_extra
    d_stream_one, d_gain_block, tap_block_in, tap_block_out = block_back(d_stream_two)
    d_conv, d_wide_tail, tap_project = tail_back(d_stream_one)
    d_conv_ext = extended_2(d_conv, (("sy", 0), ("sx", 1)), 1)
    d_kernel = kernel_back(d_conv)[0]
    d_inner = depthwise_back(d_conv_ext, dw_kernel).astype(jnp.bfloat16)
    d_normed, tap_expand = expand_back(d_inner)
    d_wide_front, d_gain_conv = front_back(d_normed)
    token_grad = (d_wide_tail + d_wide_front).astype(jnp.bfloat16)
    local_grads = (
        d_gain_conv,
        outer_sum(normed, tap_expand),
        d_kernel,
        outer_sum(activated, tap_project),
        d_gain_block,
        outer_sum(block_saved[0], tap_block_in),
        outer_sum(block_saved[1], tap_block_out),
        d_gain_grid,
        outer_sum(grid_windows, tap_grid_in),
        outer_sum(grid_home, tap_grid_out),
    )
    summed = reduce_grads(local_grads, ((0, 1, 2, 3, 4, 5, 6, 7, 8, 9),))
    return (
        output_tile[None],
        token_grad[None],
        summed[0],
        summed[1],
        summed[2],
        summed[3],
        summed[4],
        summed[5],
        summed[6],
        summed[7],
        summed[8],
        summed[9],
    )


def solution(mesh):
    return jax.shard_map(
        body,
        mesh=mesh,
        in_specs=(
            P("rep", "sy", "sx", None),
            P("rep", "sy", "sx", None),
            P(),
            P(),
            P(),
            P(),
            P(),
            P(),
            P(),
            P(),
            P(),
            P(),
        ),
        out_specs=(
            P("rep", "sy", "sx", None),
            P("rep", "sy", "sx", None),
            P("rep"),
            P("rep", None),
            P("rep", None),
            P("rep", None),
            P("rep"),
            P("rep", None),
            P("rep", None),
            P("rep"),
            P("rep", None),
            P("rep", None),
        ),
        check_vma=False,
    )
```

```python
import jax
import jax.numpy as jnp
from jax import lax
from jax.sharding import PartitionSpec as P

HEADS = 8
WIN = 8


EPSILON = 1e-05


def as_sent(value):

    def short(part):
        return part.astype(jnp.bfloat16) if part.dtype == jnp.float32 else part

    return jax.tree.map(short, value)


def extended_2(cells, sides, width):
    for axis, dim in sides:
        count = lax.axis_size(axis)
        ends = count - 1
        head = lax.slice_in_dim(cells, 0, width, axis=dim)
        tail = lax.slice_in_dim(cells, cells.shape[dim] - width, cells.shape[dim], axis=dim)
        cells = jnp.concatenate(
            [
                lax.ppermute(tail, axis, [(i, (i + 1) % count) for i in range(ends)]),
                cells,
                lax.ppermute(head, axis, [((i + 1) % count, i) for i in range(ends)]),
            ],
            axis=dim,
        )
    return cells


def widen(values):
    return lax.optimization_barrier(values).astype(jnp.float32)


def layer_norm(values, gain):
    row_mean = jnp.mean(values, axis=-1, keepdims=True)
    centred = values - row_mean
    variance = jnp.mean(centred * centred, axis=-1, keepdims=True)
    return centred * lax.rsqrt(variance + EPSILON) * gain


def project_rows(values, weight):
    leading = values.shape[:-1]
    flattened = values.reshape(-1, values.shape[-1])
    product = jnp.dot(flattened, weight, preferred_element_type=jnp.float32)
    return product.reshape(leading + (weight.shape[1],))


def outer_sum(left_side, right_side):
    left_flat = left_side.reshape(-1, left_side.shape[-1])
    right_flat = right_side.reshape(-1, right_side.shape[-1]).astype(jnp.bfloat16)
    return lax.dot_general(
        left_flat, right_flat, (((0,), (0,)), ((), ())), preferred_element_type=jnp.float32
    )


def to_windows(image, side):
    height, breadth, channels = image.shape
    blocks = image.reshape(height // side, side, breadth // side, side, channels)
    return blocks.transpose(0, 2, 1, 3, 4).reshape(-1, side * side, channels)


def from_windows(windows, height, breadth, side):
    channels = windows.shape[-1]
    blocks = windows.reshape(height // side, breadth // side, side, side, channels)
    return blocks.transpose(0, 2, 1, 3, 4).reshape(height, breadth, channels)


def to_grid(image, side):
    height, breadth, channels = image.shape
    blocks = image.reshape(side, height // side, side, breadth // side, channels)
    return blocks.transpose(1, 3, 0, 2, 4).reshape(-1, side * side, channels)


def from_grid(windows, height, breadth, side):
    channels = windows.shape[-1]
    blocks = windows.reshape(height // side, breadth // side, side, side, channels)
    return blocks.transpose(2, 0, 3, 1, 4).reshape(height, breadth, channels)


def window_attention(windows, weight, tap_in, heads):
    count, members, channels = windows.shape
    head_width = channels // heads
    qkv_rows = (project_rows(windows, weight) + tap_in).astype(jnp.bfloat16)
    queries = qkv_rows[..., :channels].reshape(count, members, heads, head_width)
    key_rows = qkv_rows[..., channels : 2 * channels].reshape(count, members, heads, head_width)
    value_rows = qkv_rows[..., 2 * channels :].reshape(count, members, heads, head_width)
    scores = jnp.einsum(
        "wqhd,wkhd->whqk", queries, key_rows, preferred_element_type=jnp.float32
    ) * head_width ** (-0.5)
    softmax_out = jax.nn.softmax(scores, axis=-1).astype(jnp.bfloat16)
    attended = jnp.einsum(
        "whqk,wkhd->wqhd", softmax_out, value_rows, preferred_element_type=jnp.float32
    )
    return attended.astype(jnp.bfloat16).reshape(count, members, channels)


def depthwise(extended, kernel):
    height = extended.shape[0] - 2
    breadth = extended.shape[1] - 2
    widened = widen(extended)
    summed = jnp.zeros((height, breadth, extended.shape[2]), jnp.float32)
    for tap_index in range(9):
        row_step, col_step = divmod(tap_index, 3)
        summed = (
            summed
            + widened[row_step : row_step + height, col_step : col_step + breadth]
            * kernel[:, tap_index]
        )
    return summed


def depthwise_back(grad_ext, kernel):
    height = grad_ext.shape[0] - 2
    breadth = grad_ext.shape[1] - 2
    summed = jnp.zeros((height, breadth, grad_ext.shape[2]), jnp.float32)
    for tap_index in range(9):
        row_step, col_step = divmod(tap_index, 3)
        summed = (
            summed
            + grad_ext[2 - row_step : 2 - row_step + height, 2 - col_step : 2 - col_step + breadth]
            * kernel[:, tap_index]
        )
    return summed


def swap_blocks(blocks):
    sy_count, sx_count, row_part, col_part, channels = blocks.shape
    flattened = blocks.reshape(sy_count * sx_count, row_part, col_part, channels)
    moved = lax.all_to_all(
        as_sent(flattened), ("sy", "sx"), split_axis=0, concat_axis=0, tiled=True
    ).astype(flattened.dtype)
    return moved.reshape(blocks.shape)


def to_exchanged(image):
    height, breadth, channels = image.shape
    sy_count = lax.axis_size("sy")
    sx_count = lax.axis_size("sx")
    blocks = image.reshape(height // sy_count, sy_count, breadth // sx_count, sx_count, channels)
    moved = swap_blocks(blocks.transpose(1, 3, 0, 2, 4))
    return moved.transpose(0, 2, 1, 3, 4).reshape(height, breadth, channels)


def to_home(image):
    height, breadth, channels = image.shape
    sy_count = lax.axis_size("sy")
    sx_count = lax.axis_size("sx")
    blocks = image.reshape(sy_count, height // sy_count, sx_count, breadth // sx_count, channels)
    moved = swap_blocks(blocks.transpose(0, 2, 1, 3, 4))
    return moved.transpose(2, 0, 3, 1, 4).reshape(height, breadth, channels)


def exchange_sum(values, axes, axis):
    moved = lax.all_to_all(values.astype(jnp.bfloat16), axes, split_axis=axis, concat_axis=axis, tiled=True)
    return moved.astype(jnp.float32).sum(axis)


def reduce_grads(grads):
    parts = lax.axis_size("rep")
    tiles = lax.axis_size(("sy", "sx"))
    channels = grads[0].shape[0]
    small = jnp.concatenate(
        [grads[2].reshape(channels, -1), grads[0][:, None], grads[4][:, None], grads[7][:, None]], axis=1
    )
    small_width = small.shape[1]
    small = jnp.pad(small, ((0, 0), (0, -small_width % 128)))
    wide = [grads[1], grads[5], grads[6], grads[8], grads[9], grads[3].reshape(channels, -1), small]
    widths = [piece.shape[1] for piece in wide]
    packed = jnp.concatenate(wide, axis=1)
    width = packed.shape[1]
    rows = channels // parts
    piece = rows // tiles
    local = exchange_sum(packed.reshape(parts, tiles, piece, width), ("sy", "sx"), 1)
    local = exchange_sum(local, "rep", 0)
    spread = jnp.broadcast_to(local[None], (tiles, piece, width))
    total = lax.all_to_all(spread, ("sy", "sx"), split_axis=0, concat_axis=0, tiled=True)
    total = total.reshape(rows, width)
    cuts = []
    offset = 0
    for size in widths:
        cuts.append(total[:, offset : offset + size])
        offset += size
    small = cuts[6]
    kernel_cols = grads[2].shape[1] * grads[2].shape[0] // channels
    return (
        small[:, kernel_cols],
        cuts[0],
        small[:, :kernel_cols].reshape(-1, grads[2].shape[1]),
        cuts[5].reshape(-1, grads[3].shape[1]),
        small[:, kernel_cols + 1],
        cuts[1],
        cuts[2],
        small[:, kernel_cols + 2],
        cuts[3],
        cuts[4],
    )

def body(
    features,
    cotangent,
    gain_conv,
    expand_weight,
    dw_kernel,
    project_weight,
    gain_block,
    block_inward,
    block_outward,
    gain_grid,
    grid_inward,
    grid_outward,
):
    image = features[0]
    height, breadth, channels = image.shape
    expand_units = expand_weight.shape[1]
    window_count = height * breadth // (WIN * WIN)
    zero_width = jnp.zeros((height, breadth, channels), jnp.float32)
    zero_expand = jnp.zeros((height, breadth, expand_units), jnp.float32)
    zero_qkv = jnp.zeros((window_count, WIN * WIN, 3 * channels), jnp.float32)
    widened = image.astype(jnp.float32)

    def conv_front(wide_in, gain_in):
        return layer_norm(wide_in, gain_in).astype(jnp.bfloat16)

    normed, front_back = jax.vjp(conv_front, widened, gain_conv)

    def expand_fn(normed_in, tap_in):
        return jax.nn.gelu(project_rows(normed_in, expand_weight) + tap_in).astype(jnp.bfloat16)

    inner, expand_back = jax.vjp(expand_fn, normed, zero_expand)
    inner_ext = extended_2(inner, (("sy", 0), ("sx", 1)), 1)

    def conv_only(kernel_in):
        return depthwise(inner_ext, kernel_in)

    conv_out, kernel_back = jax.vjp(conv_only, dw_kernel)

    def conv_tail(conv_in, wide_in, tap_in):
        activated_in = jax.nn.gelu(conv_in).astype(jnp.bfloat16)
        return (wide_in + project_rows(activated_in, project_weight) + tap_in, activated_in)

    stream_one, tail_back, activated = jax.vjp(
        conv_tail, conv_out, widened, zero_width, has_aux=True
    )

    def block_layer(stream_in, gain_in, tap_in, tap_out):
        normed_two = layer_norm(stream_in, gain_in).astype(jnp.bfloat16)
        windows = to_windows(normed_two, WIN)
        attended = window_attention(windows, block_inward, tap_in, HEADS)
        attended_home = from_windows(attended, height, breadth, WIN)
        return (
            stream_in + project_rows(attended_home, block_outward) + tap_out,
            (windows, attended_home),
        )

    stream_two, block_back, block_saved = jax.vjp(
        block_layer, stream_one, gain_block, zero_qkv, zero_width, has_aux=True
    )

    def grid_front(stream_in, gain_in):
        return layer_norm(stream_in, gain_in).astype(jnp.bfloat16)

    normed_three, grid_front_back = jax.vjp(grid_front, stream_two, gain_grid)
    grid_windows = to_grid(to_exchanged(normed_three), WIN)

    def grid_core(windows_in, tap_in):
        return window_attention(windows_in, grid_inward, tap_in, HEADS)

    grid_attended, grid_core_back = jax.vjp(grid_core, grid_windows, zero_qkv)
    grid_home = to_home(from_grid(grid_attended, height, breadth, WIN))

    def grid_tail(stream_in, attended_in, tap_in):
        return (stream_in + project_rows(attended_in, grid_outward) + tap_in).astype(jnp.bfloat16)

    output_tile, grid_tail_back = jax.vjp(grid_tail, stream_two, grid_home, zero_width)
    d_stream_two, d_grid_home, tap_grid_out = grid_tail_back(cotangent[0])
    d_grid_attended = to_grid(to_exchanged(d_grid_home), WIN)
    d_grid_windows, tap_grid_in = grid_core_back(d_grid_attended)
    d_normed_three = to_home(from_grid(d_grid_windows, height, breadth, WIN))
    d_stream_extra, d_gain_grid = grid_front_back(d_normed_three)
    d_stream_two = d_stream_two + d_stream_extra
    d_stream_one, d_gain_block, tap_block_in, tap_block_out = block_back(d_stream_two)
    d_conv, d_wide_tail, tap_project = tail_back(d_stream_one)
    d_conv_ext = extended_2(d_conv, (("sy", 0), ("sx", 1)), 1)
    d_kernel = kernel_back(d_conv)[0]
    d_inner = depthwise_back(d_conv_ext, dw_kernel).astype(jnp.bfloat16)
    d_normed, tap_expand = expand_back(d_inner)
    d_wide_front, d_gain_conv = front_back(d_normed)
    token_grad = (d_wide_tail + d_wide_front).astype(jnp.bfloat16)
    local_grads = (
        d_gain_conv,
        outer_sum(normed, tap_expand),
        d_kernel,
        outer_sum(activated, tap_project),
        d_gain_block,
        outer_sum(block_saved[0], tap_block_in),
        outer_sum(block_saved[1], tap_block_out),
        d_gain_grid,
        outer_sum(grid_windows, tap_grid_in),
        outer_sum(grid_home, tap_grid_out),
    )
    summed = reduce_grads(local_grads)
    return (
        output_tile[None],
        token_grad[None],
        summed[0],
        summed[1],
        summed[2],
        summed[3],
        summed[4],
        summed[5],
        summed[6],
        summed[7],
        summed[8],
        summed[9],
    )


def solution(mesh):
    return jax.shard_map(
        body,
        mesh=mesh,
        in_specs=(
            P("rep", "sy", "sx", None),
            P("rep", "sy", "sx", None),
            P(),
            P(),
            P(),
            P(),
            P(),
            P(),
            P(),
            P(),
            P(),
            P(),
        ),
        out_specs=(
            P("rep", "sy", "sx", None),
            P("rep", "sy", "sx", None),
            P("rep"),
            P("rep", None),
            P("rep", None),
            P("rep", None),
            P("rep"),
            P("rep", None),
            P("rep", None),
            P("rep"),
            P("rep", None),
            P("rep", None),
        ),
        check_vma=False,
    )
```

```python
import jax
import jax.numpy as jnp
from jax import lax
from jax.sharding import PartitionSpec as P

HEADS = 8
WIN = 8


EPSILON = 1e-05


def as_sent(value):

    def short(part):
        return part.astype(jnp.bfloat16) if part.dtype == jnp.float32 else part

    return jax.tree.map(short, value)


def extended_2(cells, sides, width):
    for axis, dim in sides:
        count = lax.axis_size(axis)
        ends = count - 1
        head = lax.slice_in_dim(cells, 0, width, axis=dim)
        tail = lax.slice_in_dim(cells, cells.shape[dim] - width, cells.shape[dim], axis=dim)
        cells = jnp.concatenate(
            [
                lax.ppermute(tail, axis, [(i, (i + 1) % count) for i in range(ends)]),
                cells,
                lax.ppermute(head, axis, [((i + 1) % count, i) for i in range(ends)]),
            ],
            axis=dim,
        )
    return cells


def widen(values):
    return lax.optimization_barrier(values).astype(jnp.float32)


def layer_norm(values, gain):
    row_mean = jnp.mean(values, axis=-1, keepdims=True)
    centred = values - row_mean
    variance = jnp.mean(centred * centred, axis=-1, keepdims=True)
    return centred * lax.rsqrt(variance + EPSILON) * gain


def project_rows(values, weight):
    leading = values.shape[:-1]
    flattened = values.reshape(-1, values.shape[-1])
    product = jnp.dot(flattened, weight, preferred_element_type=jnp.float32)
    return product.reshape(leading + (weight.shape[1],))


def outer_sum(left_side, right_side):
    left_flat = left_side.reshape(-1, left_side.shape[-1])
    right_flat = right_side.reshape(-1, right_side.shape[-1]).astype(jnp.bfloat16)
    return lax.dot_general(
        left_flat, right_flat, (((0,), (0,)), ((), ())), preferred_element_type=jnp.float32
    )


def to_windows(image, side):
    height, breadth, channels = image.shape
    blocks = image.reshape(height // side, side, breadth // side, side, channels)
    return blocks.transpose(0, 2, 1, 3, 4).reshape(-1, side * side, channels)


def from_windows(windows, height, breadth, side):
    channels = windows.shape[-1]
    blocks = windows.reshape(height // side, breadth // side, side, side, channels)
    return blocks.transpose(0, 2, 1, 3, 4).reshape(height, breadth, channels)


def to_grid(image, side):
    height, breadth, channels = image.shape
    blocks = image.reshape(side, height // side, side, breadth // side, channels)
    return blocks.transpose(1, 3, 0, 2, 4).reshape(-1, side * side, channels)


def from_grid(windows, height, breadth, side):
    channels = windows.shape[-1]
    blocks = windows.reshape(height // side, breadth // side, side, side, channels)
    return blocks.transpose(2, 0, 3, 1, 4).reshape(height, breadth, channels)


def window_attention(windows, weight, tap_in, heads):
    count, members, channels = windows.shape
    head_width = channels // heads
    qkv_rows = (project_rows(windows, weight) + tap_in).astype(jnp.bfloat16)
    queries = qkv_rows[..., :channels].reshape(count, members, heads, head_width)
    key_rows = qkv_rows[..., channels : 2 * channels].reshape(count, members, heads, head_width)
    value_rows = qkv_rows[..., 2 * channels :].reshape(count, members, heads, head_width)
    scores = jnp.einsum(
        "wqhd,wkhd->whqk", queries, key_rows, preferred_element_type=jnp.float32
    ) * head_width ** (-0.5)
    softmax_out = jax.nn.softmax(scores, axis=-1).astype(jnp.bfloat16)
    attended = jnp.einsum(
        "whqk,wkhd->wqhd", softmax_out, value_rows, preferred_element_type=jnp.float32
    )
    return attended.astype(jnp.bfloat16).reshape(count, members, channels)


def depthwise(extended, kernel):
    height = extended.shape[0] - 2
    breadth = extended.shape[1] - 2
    widened = widen(extended)
    summed = jnp.zeros((height, breadth, extended.shape[2]), jnp.float32)
    for tap_index in range(9):
        row_step, col_step = divmod(tap_index, 3)
        summed = (
            summed
            + widened[row_step : row_step + height, col_step : col_step + breadth]
            * kernel[:, tap_index]
        )
    return summed


def depthwise_back(grad_ext, kernel):
    height = grad_ext.shape[0] - 2
    breadth = grad_ext.shape[1] - 2
    summed = jnp.zeros((height, breadth, grad_ext.shape[2]), jnp.float32)
    for tap_index in range(9):
        row_step, col_step = divmod(tap_index, 3)
        summed = (
            summed
            + grad_ext[2 - row_step : 2 - row_step + height, 2 - col_step : 2 - col_step + breadth]
            * kernel[:, tap_index]
        )
    return summed


def swap_blocks(blocks):
    sy_count, sx_count, row_part, col_part, channels = blocks.shape
    flattened = blocks.reshape(sy_count * sx_count, row_part, col_part, channels)
    moved = lax.all_to_all(
        as_sent(flattened), ("sy", "sx"), split_axis=0, concat_axis=0, tiled=True
    ).astype(flattened.dtype)
    return moved.reshape(blocks.shape)


def to_exchanged(image):
    height, breadth, channels = image.shape
    sy_count = lax.axis_size("sy")
    sx_count = lax.axis_size("sx")
    blocks = image.reshape(height // sy_count, sy_count, breadth // sx_count, sx_count, channels)
    moved = swap_blocks(blocks.transpose(1, 3, 0, 2, 4))
    return moved.transpose(0, 2, 1, 3, 4).reshape(height, breadth, channels)


def to_home(image):
    height, breadth, channels = image.shape
    sy_count = lax.axis_size("sy")
    sx_count = lax.axis_size("sx")
    blocks = image.reshape(sy_count, height // sy_count, sx_count, breadth // sx_count, channels)
    moved = swap_blocks(blocks.transpose(0, 2, 1, 3, 4))
    return moved.transpose(2, 0, 3, 1, 4).reshape(height, breadth, channels)


def exchange_sum(values, axes, axis):
    moved = lax.all_to_all(values.astype(jnp.bfloat16), axes, split_axis=axis, concat_axis=axis, tiled=True)
    return moved.astype(jnp.float32).sum(axis)


def reduce_packed(wide):
    parts = lax.axis_size("rep")
    tiles = lax.axis_size(("sy", "sx"))
    widths = [piece.shape[1] for piece in wide]
    packed = jnp.concatenate(wide, axis=1)
    channels, width = packed.shape
    rows = channels // parts
    piece = rows // tiles
    local = exchange_sum(packed.reshape(parts, tiles, piece, width), ("sy", "sx"), 1)
    local = exchange_sum(local, "rep", 0)
    spread = jnp.broadcast_to(local[None].astype(jnp.bfloat16), (tiles, piece, width))
    total = lax.all_to_all(spread, ("sy", "sx"), split_axis=0, concat_axis=0, tiled=True)
    total = total.astype(jnp.float32).reshape(rows, width)
    cuts = []
    offset = 0
    for size in widths:
        cuts.append(total[:, offset : offset + size])
        offset += size
    return cuts


def pad_lanes(columns):
    joined = jnp.concatenate(columns, axis=1)
    return jnp.pad(joined, ((0, 0), (0, -joined.shape[1] % 128)))


def reduce_grads(grads):
    channels = grads[0].shape[0]
    taps = grads[2].shape[1]
    kernel_cols = taps * grads[2].shape[0] // channels
    attention = reduce_packed(
        [grads[5], grads[6], grads[8], grads[9], pad_lanes([grads[4][:, None], grads[7][:, None]])]
    )
    conv = reduce_packed(
        [grads[1], grads[3].reshape(channels, -1), pad_lanes([grads[2].reshape(channels, -1), grads[0][:, None]])]
    )
    return (
        conv[2][:, kernel_cols],
        conv[0],
        conv[2][:, :kernel_cols].reshape(-1, taps),
        conv[1].reshape(-1, grads[3].shape[1]),
        attention[4][:, 0],
        attention[0],
        attention[1],
        attention[4][:, 1],
        attention[2],
        attention[3],
    )

def body(
    features,
    cotangent,
    gain_conv,
    expand_weight,
    dw_kernel,
    project_weight,
    gain_block,
    block_inward,
    block_outward,
    gain_grid,
    grid_inward,
    grid_outward,
):
    image = features[0]
    height, breadth, channels = image.shape
    expand_units = expand_weight.shape[1]
    window_count = height * breadth // (WIN * WIN)
    zero_width = jnp.zeros((height, breadth, channels), jnp.float32)
    zero_expand = jnp.zeros((height, breadth, expand_units), jnp.float32)
    zero_qkv = jnp.zeros((window_count, WIN * WIN, 3 * channels), jnp.float32)
    widened = image.astype(jnp.float32)

    def conv_front(wide_in, gain_in):
        return layer_norm(wide_in, gain_in).astype(jnp.bfloat16)

    normed, front_back = jax.vjp(conv_front, widened, gain_conv)

    def expand_fn(normed_in, tap_in):
        return jax.nn.gelu(project_rows(normed_in, expand_weight) + tap_in).astype(jnp.bfloat16)

    inner, expand_back = jax.vjp(expand_fn, normed, zero_expand)
    inner_ext = extended_2(inner, (("sy", 0), ("sx", 1)), 1)

    def conv_only(kernel_in):
        return depthwise(inner_ext, kernel_in)

    conv_out, kernel_back = jax.vjp(conv_only, dw_kernel)

    def conv_tail(conv_in, wide_in, tap_in):
        activated_in = jax.nn.gelu(conv_in).astype(jnp.bfloat16)
        return (wide_in + project_rows(activated_in, project_weight) + tap_in, activated_in)

    stream_one, tail_back, activated = jax.vjp(
        conv_tail, conv_out, widened, zero_width, has_aux=True
    )

    def block_layer(stream_in, gain_in, tap_in, tap_out):
        normed_two = layer_norm(stream_in, gain_in).astype(jnp.bfloat16)
        windows = to_windows(normed_two, WIN)
        attended = window_attention(windows, block_inward, tap_in, HEADS)
        attended_home = from_windows(attended, height, breadth, WIN)
        return (
            stream_in + project_rows(attended_home, block_outward) + tap_out,
            (windows, attended_home),
        )

    stream_two, block_back, block_saved = jax.vjp(
        block_layer, stream_one, gain_block, zero_qkv, zero_width, has_aux=True
    )

    def grid_front(stream_in, gain_in):
        return layer_norm(stream_in, gain_in).astype(jnp.bfloat16)

    normed_three, grid_front_back = jax.vjp(grid_front, stream_two, gain_grid)
    grid_windows = to_grid(to_exchanged(normed_three), WIN)

    def grid_core(windows_in, tap_in):
        return window_attention(windows_in, grid_inward, tap_in, HEADS)

    grid_attended, grid_core_back = jax.vjp(grid_core, grid_windows, zero_qkv)
    grid_home = to_home(from_grid(grid_attended, height, breadth, WIN))

    def grid_tail(stream_in, attended_in, tap_in):
        return (stream_in + project_rows(attended_in, grid_outward) + tap_in).astype(jnp.bfloat16)

    output_tile, grid_tail_back = jax.vjp(grid_tail, stream_two, grid_home, zero_width)
    d_stream_two, d_grid_home, tap_grid_out = grid_tail_back(cotangent[0])
    d_grid_attended = to_grid(to_exchanged(d_grid_home), WIN)
    d_grid_windows, tap_grid_in = grid_core_back(d_grid_attended)
    d_normed_three = to_home(from_grid(d_grid_windows, height, breadth, WIN))
    d_stream_extra, d_gain_grid = grid_front_back(d_normed_three)
    d_stream_two = d_stream_two + d_stream_extra
    d_stream_one, d_gain_block, tap_block_in, tap_block_out = block_back(d_stream_two)
    d_conv, d_wide_tail, tap_project = tail_back(d_stream_one)
    d_conv_ext = extended_2(d_conv, (("sy", 0), ("sx", 1)), 1)
    d_kernel = kernel_back(d_conv)[0]
    d_inner = depthwise_back(d_conv_ext, dw_kernel).astype(jnp.bfloat16)
    d_normed, tap_expand = expand_back(d_inner)
    d_wide_front, d_gain_conv = front_back(d_normed)
    token_grad = (d_wide_tail + d_wide_front).astype(jnp.bfloat16)
    local_grads = (
        d_gain_conv,
        outer_sum(normed, tap_expand),
        d_kernel,
        outer_sum(activated, tap_project),
        d_gain_block,
        outer_sum(block_saved[0], tap_block_in),
        outer_sum(block_saved[1], tap_block_out),
        d_gain_grid,
        outer_sum(grid_windows, tap_grid_in),
        outer_sum(grid_home, tap_grid_out),
    )
    summed = reduce_grads(local_grads)
    return (
        output_tile[None],
        token_grad[None],
        summed[0],
        summed[1],
        summed[2],
        summed[3],
        summed[4],
        summed[5],
        summed[6],
        summed[7],
        summed[8],
        summed[9],
    )


def solution(mesh):
    return jax.shard_map(
        body,
        mesh=mesh,
        in_specs=(
            P("rep", "sy", "sx", None),
            P("rep", "sy", "sx", None),
            P(),
            P(),
            P(),
            P(),
            P(),
            P(),
            P(),
            P(),
            P(),
            P(),
        ),
        out_specs=(
            P("rep", "sy", "sx", None),
            P("rep", "sy", "sx", None),
            P("rep"),
            P("rep", None),
            P("rep", None),
            P("rep", None),
            P("rep"),
            P("rep", None),
            P("rep", None),
            P("rep"),
            P("rep", None),
            P("rep", None),
        ),
        check_vma=False,
    )
```

```python
import jax
import jax.numpy as jnp
from jax import lax
from jax.sharding import PartitionSpec as P

HEADS = 8
WIN = 8


EPSILON = 1e-05


def as_sent(value):

    def short(part):
        return part.astype(jnp.bfloat16) if part.dtype == jnp.float32 else part

    return jax.tree.map(short, value)


def extended_2(cells, sides, width):
    for axis, dim in sides:
        count = lax.axis_size(axis)
        ends = count - 1
        head = lax.slice_in_dim(cells, 0, width, axis=dim)
        tail = lax.slice_in_dim(cells, cells.shape[dim] - width, cells.shape[dim], axis=dim)
        cells = jnp.concatenate(
            [
                lax.ppermute(tail, axis, [(i, (i + 1) % count) for i in range(ends)]),
                cells,
                lax.ppermute(head, axis, [((i + 1) % count, i) for i in range(ends)]),
            ],
            axis=dim,
        )
    return cells


def widen(values):
    return lax.optimization_barrier(values).astype(jnp.float32)


def layer_norm(values, gain):
    row_mean = jnp.mean(values, axis=-1, keepdims=True)
    centred = values - row_mean
    variance = jnp.mean(centred * centred, axis=-1, keepdims=True)
    return centred * lax.rsqrt(variance + EPSILON) * gain


def project_rows(values, weight):
    leading = values.shape[:-1]
    flattened = values.reshape(-1, values.shape[-1])
    product = jnp.dot(flattened, weight, preferred_element_type=jnp.float32)
    return product.reshape(leading + (weight.shape[1],))


def outer_sum(left_side, right_side):
    left_flat = left_side.reshape(-1, left_side.shape[-1])
    right_flat = right_side.reshape(-1, right_side.shape[-1]).astype(jnp.bfloat16)
    return lax.dot_general(
        left_flat, right_flat, (((0,), (0,)), ((), ())), preferred_element_type=jnp.float32
    )


def to_windows(image, side):
    height, breadth, channels = image.shape
    blocks = image.reshape(height // side, side, breadth // side, side, channels)
    return blocks.transpose(0, 2, 1, 3, 4).reshape(-1, side * side, channels)


def from_windows(windows, height, breadth, side):
    channels = windows.shape[-1]
    blocks = windows.reshape(height // side, breadth // side, side, side, channels)
    return blocks.transpose(0, 2, 1, 3, 4).reshape(height, breadth, channels)


def to_grid(image, side):
    height, breadth, channels = image.shape
    blocks = image.reshape(side, height // side, side, breadth // side, channels)
    return blocks.transpose(1, 3, 0, 2, 4).reshape(-1, side * side, channels)


def from_grid(windows, height, breadth, side):
    channels = windows.shape[-1]
    blocks = windows.reshape(height // side, breadth // side, side, side, channels)
    return blocks.transpose(2, 0, 3, 1, 4).reshape(height, breadth, channels)


def window_attention(windows, weight, tap_in, heads):
    count, members, channels = windows.shape
    head_width = channels // heads
    qkv_rows = (project_rows(windows, weight) + tap_in).astype(jnp.bfloat16)
    queries = qkv_rows[..., :channels].reshape(count, members, heads, head_width)
    key_rows = qkv_rows[..., channels : 2 * channels].reshape(count, members, heads, head_width)
    value_rows = qkv_rows[..., 2 * channels :].reshape(count, members, heads, head_width)
    scores = jnp.einsum(
        "wqhd,wkhd->whqk", queries, key_rows, preferred_element_type=jnp.float32
    ) * head_width ** (-0.5)
    softmax_out = jax.nn.softmax(scores, axis=-1).astype(jnp.bfloat16)
    attended = jnp.einsum(
        "whqk,wkhd->wqhd", softmax_out, value_rows, preferred_element_type=jnp.float32
    )
    return attended.astype(jnp.bfloat16).reshape(count, members, channels)


def depthwise(extended, kernel):
    height = extended.shape[0] - 2
    breadth = extended.shape[1] - 2
    widened = widen(extended)
    summed = jnp.zeros((height, breadth, extended.shape[2]), jnp.float32)
    for tap_index in range(9):
        row_step, col_step = divmod(tap_index, 3)
        summed = (
            summed
            + widened[row_step : row_step + height, col_step : col_step + breadth]
            * kernel[:, tap_index]
        )
    return summed


def depthwise_back(grad_ext, kernel):
    height = grad_ext.shape[0] - 2
    breadth = grad_ext.shape[1] - 2
    summed = jnp.zeros((height, breadth, grad_ext.shape[2]), jnp.float32)
    for tap_index in range(9):
        row_step, col_step = divmod(tap_index, 3)
        summed = (
            summed
            + grad_ext[2 - row_step : 2 - row_step + height, 2 - col_step : 2 - col_step + breadth]
            * kernel[:, tap_index]
        )
    return summed


def swap_blocks(blocks):
    sy_count, sx_count, row_part, col_part, channels = blocks.shape
    flattened = blocks.reshape(sy_count * sx_count, row_part, col_part, channels)
    moved = lax.all_to_all(
        as_sent(flattened), ("sy", "sx"), split_axis=0, concat_axis=0, tiled=True
    ).astype(flattened.dtype)
    return moved.reshape(blocks.shape)


def to_exchanged(image):
    height, breadth, channels = image.shape
    sy_count = lax.axis_size("sy")
    sx_count = lax.axis_size("sx")
    blocks = image.reshape(height // sy_count, sy_count, breadth // sx_count, sx_count, channels)
    moved = swap_blocks(blocks.transpose(1, 3, 0, 2, 4))
    return moved.transpose(0, 2, 1, 3, 4).reshape(height, breadth, channels)


def to_home(image):
    height, breadth, channels = image.shape
    sy_count = lax.axis_size("sy")
    sx_count = lax.axis_size("sx")
    blocks = image.reshape(sy_count, height // sy_count, sx_count, breadth // sx_count, channels)
    moved = swap_blocks(blocks.transpose(0, 2, 1, 3, 4))
    return moved.transpose(2, 0, 3, 1, 4).reshape(height, breadth, channels)


def exchange_sum(values, axes, axis):
    moved = lax.all_to_all(values.astype(jnp.bfloat16), axes, split_axis=axis, concat_axis=axis, tiled=True)
    return moved.astype(jnp.float32).sum(axis)


def reduce_packed(wide):
    parts = lax.axis_size("rep")
    tiles = lax.axis_size(("sy", "sx"))
    widths = [piece.shape[1] for piece in wide]
    packed = jnp.concatenate(wide, axis=1)
    channels, width = packed.shape
    rows = channels // parts
    piece = rows // tiles
    local = exchange_sum(packed.reshape(parts, tiles, piece, width), ("sy", "sx"), 1)
    local = exchange_sum(local, "rep", 0)
    spread = jnp.broadcast_to(local[None].astype(jnp.bfloat16), (tiles, piece, width))
    total = lax.all_to_all(spread, ("sy", "sx"), split_axis=0, concat_axis=0, tiled=True)
    total = total.astype(jnp.float32).reshape(rows, width)
    cuts = []
    offset = 0
    for size in widths:
        cuts.append(total[:, offset : offset + size])
        offset += size
    return cuts


def pad_lanes(columns):
    joined = jnp.concatenate(columns, axis=1)
    return jnp.pad(joined, ((0, 0), (0, -joined.shape[1] % 128)))


def reduce_grads(grads):
    channels = grads[0].shape[0]
    taps = grads[2].shape[1]
    kernel_cols = taps * grads[2].shape[0] // channels
    small = pad_lanes([grads[2].reshape(channels, -1), grads[0][:, None], grads[4][:, None], grads[7][:, None]])
    cuts = reduce_packed([grads[1], grads[5], grads[6], grads[8], grads[9], grads[3].reshape(channels, -1), small])
    small = cuts[6]
    return (
        small[:, kernel_cols],
        cuts[0],
        small[:, :kernel_cols].reshape(-1, taps),
        cuts[5].reshape(-1, grads[3].shape[1]),
        small[:, kernel_cols + 1],
        cuts[1],
        cuts[2],
        small[:, kernel_cols + 2],
        cuts[3],
        cuts[4],
    )

def body(
    features,
    cotangent,
    gain_conv,
    expand_weight,
    dw_kernel,
    project_weight,
    gain_block,
    block_inward,
    block_outward,
    gain_grid,
    grid_inward,
    grid_outward,
):
    image = features[0]
    height, breadth, channels = image.shape
    expand_units = expand_weight.shape[1]
    window_count = height * breadth // (WIN * WIN)
    zero_width = jnp.zeros((height, breadth, channels), jnp.float32)
    zero_expand = jnp.zeros((height, breadth, expand_units), jnp.float32)
    zero_qkv = jnp.zeros((window_count, WIN * WIN, 3 * channels), jnp.float32)
    widened = image.astype(jnp.float32)

    def conv_front(wide_in, gain_in):
        return layer_norm(wide_in, gain_in).astype(jnp.bfloat16)

    normed, front_back = jax.vjp(conv_front, widened, gain_conv)

    def expand_fn(normed_in, tap_in):
        return jax.nn.gelu(project_rows(normed_in, expand_weight) + tap_in).astype(jnp.bfloat16)

    inner, expand_back = jax.vjp(expand_fn, normed, zero_expand)
    inner_ext = extended_2(inner, (("sy", 0), ("sx", 1)), 1)

    def conv_only(kernel_in):
        return depthwise(inner_ext, kernel_in)

    conv_out, kernel_back = jax.vjp(conv_only, dw_kernel)

    def conv_tail(conv_in, wide_in, tap_in):
        activated_in = jax.nn.gelu(conv_in).astype(jnp.bfloat16)
        return (wide_in + project_rows(activated_in, project_weight) + tap_in, activated_in)

    stream_one, tail_back, activated = jax.vjp(
        conv_tail, conv_out, widened, zero_width, has_aux=True
    )

    def block_layer(stream_in, gain_in, tap_in, tap_out):
        normed_two = layer_norm(stream_in, gain_in).astype(jnp.bfloat16)
        windows = to_windows(normed_two, WIN)
        attended = window_attention(windows, block_inward, tap_in, HEADS)
        attended_home = from_windows(attended, height, breadth, WIN)
        return (
            stream_in + project_rows(attended_home, block_outward) + tap_out,
            (windows, attended_home),
        )

    stream_two, block_back, block_saved = jax.vjp(
        block_layer, stream_one, gain_block, zero_qkv, zero_width, has_aux=True
    )

    def grid_front(stream_in, gain_in):
        return layer_norm(stream_in, gain_in).astype(jnp.bfloat16)

    normed_three, grid_front_back = jax.vjp(grid_front, stream_two, gain_grid)
    grid_windows = to_grid(to_exchanged(normed_three), WIN)

    def grid_core(windows_in, tap_in):
        return window_attention(windows_in, grid_inward, tap_in, HEADS)

    grid_attended, grid_core_back = jax.vjp(grid_core, grid_windows, zero_qkv)
    grid_home = to_home(from_grid(grid_attended, height, breadth, WIN))

    def grid_tail(stream_in, attended_in, tap_in):
        return (stream_in + project_rows(attended_in, grid_outward) + tap_in).astype(jnp.bfloat16)

    output_tile, grid_tail_back = jax.vjp(grid_tail, stream_two, grid_home, zero_width)
    d_stream_two, d_grid_home, tap_grid_out = grid_tail_back(cotangent[0])
    d_grid_attended = to_grid(to_exchanged(d_grid_home), WIN)
    d_grid_windows, tap_grid_in = grid_core_back(d_grid_attended)
    d_normed_three = to_home(from_grid(d_grid_windows, height, breadth, WIN))
    d_stream_extra, d_gain_grid = grid_front_back(d_normed_three)
    d_stream_two = d_stream_two + d_stream_extra
    d_stream_one, d_gain_block, tap_block_in, tap_block_out = block_back(d_stream_two)
    d_conv, d_wide_tail, tap_project = tail_back(d_stream_one)
    d_conv_ext = extended_2(d_conv, (("sy", 0), ("sx", 1)), 1)
    d_kernel = kernel_back(d_conv)[0]
    d_inner = depthwise_back(d_conv_ext, dw_kernel).astype(jnp.bfloat16)
    d_normed, tap_expand = expand_back(d_inner)
    d_wide_front, d_gain_conv = front_back(d_normed)
    token_grad = (d_wide_tail + d_wide_front).astype(jnp.bfloat16)
    local_grads = (
        d_gain_conv,
        outer_sum(normed, tap_expand),
        d_kernel,
        outer_sum(activated, tap_project),
        d_gain_block,
        outer_sum(block_saved[0], tap_block_in),
        outer_sum(block_saved[1], tap_block_out),
        d_gain_grid,
        outer_sum(grid_windows, tap_grid_in),
        outer_sum(grid_home, tap_grid_out),
    )
    summed = reduce_grads(local_grads)
    return (
        output_tile[None],
        token_grad[None],
        summed[0],
        summed[1],
        summed[2],
        summed[3],
        summed[4],
        summed[5],
        summed[6],
        summed[7],
        summed[8],
        summed[9],
    )


def solution(mesh):
    return jax.shard_map(
        body,
        mesh=mesh,
        in_specs=(
            P("rep", "sy", "sx", None),
            P("rep", "sy", "sx", None),
            P(),
            P(),
            P(),
            P(),
            P(),
            P(),
            P(),
            P(),
            P(),
            P(),
        ),
        out_specs=(
            P("rep", "sy", "sx", None),
            P("rep", "sy", "sx", None),
            P("rep"),
            P("rep", None),
            P("rep", None),
            P("rep", None),
            P("rep"),
            P("rep", None),
            P("rep", None),
            P("rep"),
            P("rep", None),
            P("rep", None),
        ),
        check_vma=False,
    )
```

```python
import jax
import jax.numpy as jnp
from jax import lax
from jax.sharding import PartitionSpec as P

HEADS = 8
WIN = 8


EPSILON = 1e-05


def as_sent(value):

    def short(part):
        return part.astype(jnp.bfloat16) if part.dtype == jnp.float32 else part

    return jax.tree.map(short, value)


def extended_2(cells, sides, width):
    for axis, dim in sides:
        count = lax.axis_size(axis)
        ends = count - 1
        head = lax.slice_in_dim(cells, 0, width, axis=dim)
        tail = lax.slice_in_dim(cells, cells.shape[dim] - width, cells.shape[dim], axis=dim)
        cells = jnp.concatenate(
            [
                lax.ppermute(tail, axis, [(i, (i + 1) % count) for i in range(ends)]),
                cells,
                lax.ppermute(head, axis, [((i + 1) % count, i) for i in range(ends)]),
            ],
            axis=dim,
        )
    return cells


def widen(values):
    return lax.optimization_barrier(values).astype(jnp.float32)


def layer_norm(values, gain):
    row_mean = jnp.mean(values, axis=-1, keepdims=True)
    centred = values - row_mean
    variance = jnp.mean(centred * centred, axis=-1, keepdims=True)
    return centred * lax.rsqrt(variance + EPSILON) * gain


def project_rows(values, weight):
    leading = values.shape[:-1]
    flattened = values.reshape(-1, values.shape[-1])
    product = jnp.dot(flattened, weight, preferred_element_type=jnp.float32)
    return product.reshape(leading + (weight.shape[1],))


def outer_sum(left_side, right_side):
    left_flat = left_side.reshape(-1, left_side.shape[-1])
    right_flat = right_side.reshape(-1, right_side.shape[-1]).astype(jnp.bfloat16)
    return lax.dot_general(
        left_flat, right_flat, (((0,), (0,)), ((), ())), preferred_element_type=jnp.float32
    )


def to_windows(image, side):
    height, breadth, channels = image.shape
    blocks = image.reshape(height // side, side, breadth // side, side, channels)
    return blocks.transpose(0, 2, 1, 3, 4).reshape(-1, side * side, channels)


def from_windows(windows, height, breadth, side):
    channels = windows.shape[-1]
    blocks = windows.reshape(height // side, breadth // side, side, side, channels)
    return blocks.transpose(0, 2, 1, 3, 4).reshape(height, breadth, channels)


def to_grid(image, side):
    height, breadth, channels = image.shape
    blocks = image.reshape(side, height // side, side, breadth // side, channels)
    return blocks.transpose(1, 3, 0, 2, 4).reshape(-1, side * side, channels)


def from_grid(windows, height, breadth, side):
    channels = windows.shape[-1]
    blocks = windows.reshape(height // side, breadth // side, side, side, channels)
    return blocks.transpose(2, 0, 3, 1, 4).reshape(height, breadth, channels)


def window_attention(windows, weight, tap_in, heads):
    count, members, channels = windows.shape
    head_width = channels // heads
    qkv_rows = (project_rows(windows, weight) + tap_in).astype(jnp.bfloat16)
    queries = qkv_rows[..., :channels]
    key_rows = qkv_rows[..., channels : 2 * channels]
    value_rows = qkv_rows[..., 2 * channels :]
    owner = lax.broadcasted_iota(jnp.int32, (heads, channels), 1) // head_width
    mask = (owner == lax.broadcasted_iota(jnp.int32, (heads, channels), 0)).astype(jnp.bfloat16)
    masked = queries[:, None, :, :] * mask[None, :, None, :]
    scores = jnp.einsum(
        "whqc,wkc->whqk", masked, key_rows, preferred_element_type=jnp.float32
    ) * head_width ** (-0.5)
    softmax_out = jax.nn.softmax(scores, axis=-1).astype(jnp.bfloat16)
    spread = jnp.einsum(
        "whqk,wkc->whqc", softmax_out, value_rows, preferred_element_type=jnp.float32
    )
    attended = (spread * mask[None, :, None, :].astype(jnp.float32)).sum(axis=1)
    return attended.astype(jnp.bfloat16)

def depthwise(extended, kernel):
    height = extended.shape[0] - 2
    breadth = extended.shape[1] - 2
    widened = widen(extended)
    summed = jnp.zeros((height, breadth, extended.shape[2]), jnp.float32)
    for tap_index in range(9):
        row_step, col_step = divmod(tap_index, 3)
        summed = (
            summed
            + widened[row_step : row_step + height, col_step : col_step + breadth]
            * kernel[:, tap_index]
        )
    return summed


def depthwise_back(grad_ext, kernel):
    height = grad_ext.shape[0] - 2
    breadth = grad_ext.shape[1] - 2
    summed = jnp.zeros((height, breadth, grad_ext.shape[2]), jnp.float32)
    for tap_index in range(9):
        row_step, col_step = divmod(tap_index, 3)
        summed = (
            summed
            + grad_ext[2 - row_step : 2 - row_step + height, 2 - col_step : 2 - col_step + breadth]
            * kernel[:, tap_index]
        )
    return summed


def swap_blocks(blocks):
    sy_count, sx_count, row_part, col_part, channels = blocks.shape
    flattened = blocks.reshape(sy_count * sx_count, row_part, col_part, channels)
    moved = lax.all_to_all(
        as_sent(flattened), ("sy", "sx"), split_axis=0, concat_axis=0, tiled=True
    ).astype(flattened.dtype)
    return moved.reshape(blocks.shape)


def to_exchanged(image):
    height, breadth, channels = image.shape
    sy_count = lax.axis_size("sy")
    sx_count = lax.axis_size("sx")
    blocks = image.reshape(height // sy_count, sy_count, breadth // sx_count, sx_count, channels)
    moved = swap_blocks(blocks.transpose(1, 3, 0, 2, 4))
    return moved.transpose(0, 2, 1, 3, 4).reshape(height, breadth, channels)


def to_home(image):
    height, breadth, channels = image.shape
    sy_count = lax.axis_size("sy")
    sx_count = lax.axis_size("sx")
    blocks = image.reshape(sy_count, height // sy_count, sx_count, breadth // sx_count, channels)
    moved = swap_blocks(blocks.transpose(0, 2, 1, 3, 4))
    return moved.transpose(2, 0, 3, 1, 4).reshape(height, breadth, channels)


def exchange_sum(values, axes, axis):
    moved = lax.all_to_all(values.astype(jnp.bfloat16), axes, split_axis=axis, concat_axis=axis, tiled=True)
    return moved.astype(jnp.float32).sum(axis)


def reduce_packed(wide):
    parts = lax.axis_size("rep")
    tiles = lax.axis_size(("sy", "sx"))
    widths = [piece.shape[1] for piece in wide]
    packed = jnp.concatenate(wide, axis=1)
    channels, width = packed.shape
    rows = channels // parts
    piece = rows // tiles
    local = exchange_sum(packed.reshape(parts, tiles, piece, width), ("sy", "sx"), 1)
    local = exchange_sum(local, "rep", 0)
    spread = jnp.broadcast_to(local[None].astype(jnp.bfloat16), (tiles, piece, width))
    total = lax.all_to_all(spread, ("sy", "sx"), split_axis=0, concat_axis=0, tiled=True)
    total = total.astype(jnp.float32).reshape(rows, width)
    cuts = []
    offset = 0
    for size in widths:
        cuts.append(total[:, offset : offset + size])
        offset += size
    return cuts


def pad_lanes(columns):
    joined = jnp.concatenate(columns, axis=1)
    return jnp.pad(joined, ((0, 0), (0, -joined.shape[1] % 128)))


def reduce_grads(grads):
    channels = grads[0].shape[0]
    taps = grads[2].shape[1]
    kernel_cols = taps * grads[2].shape[0] // channels
    small = pad_lanes([grads[2].reshape(channels, -1), grads[0][:, None], grads[4][:, None], grads[7][:, None]])
    cuts = reduce_packed([grads[1], grads[5], grads[6], grads[8], grads[9], grads[3].reshape(channels, -1), small])
    small = cuts[6]
    return (
        small[:, kernel_cols],
        cuts[0],
        small[:, :kernel_cols].reshape(-1, taps),
        cuts[5].reshape(-1, grads[3].shape[1]),
        small[:, kernel_cols + 1],
        cuts[1],
        cuts[2],
        small[:, kernel_cols + 2],
        cuts[3],
        cuts[4],
    )

def body(
    features,
    cotangent,
    gain_conv,
    expand_weight,
    dw_kernel,
    project_weight,
    gain_block,
    block_inward,
    block_outward,
    gain_grid,
    grid_inward,
    grid_outward,
):
    image = features[0]
    height, breadth, channels = image.shape
    expand_units = expand_weight.shape[1]
    window_count = height * breadth // (WIN * WIN)
    zero_width = jnp.zeros((height, breadth, channels), jnp.float32)
    zero_expand = jnp.zeros((height, breadth, expand_units), jnp.float32)
    zero_qkv = jnp.zeros((window_count, WIN * WIN, 3 * channels), jnp.float32)
    widened = image.astype(jnp.float32)

    def conv_front(wide_in, gain_in):
        return layer_norm(wide_in, gain_in).astype(jnp.bfloat16)

    normed, front_back = jax.vjp(conv_front, widened, gain_conv)

    def expand_fn(normed_in, tap_in):
        return jax.nn.gelu(project_rows(normed_in, expand_weight) + tap_in).astype(jnp.bfloat16)

    inner, expand_back = jax.vjp(expand_fn, normed, zero_expand)
    inner_ext = extended_2(inner, (("sy", 0), ("sx", 1)), 1)

    def conv_only(kernel_in):
        return depthwise(inner_ext, kernel_in)

    conv_out, kernel_back = jax.vjp(conv_only, dw_kernel)

    def conv_tail(conv_in, wide_in, tap_in):
        activated_in = jax.nn.gelu(conv_in).astype(jnp.bfloat16)
        return (wide_in + project_rows(activated_in, project_weight) + tap_in, activated_in)

    stream_one, tail_back, activated = jax.vjp(
        conv_tail, conv_out, widened, zero_width, has_aux=True
    )

    def block_layer(stream_in, gain_in, tap_in, tap_out):
        normed_two = layer_norm(stream_in, gain_in).astype(jnp.bfloat16)
        windows = to_windows(normed_two, WIN)
        attended = window_attention(windows, block_inward, tap_in, HEADS)
        attended_home = from_windows(attended, height, breadth, WIN)
        return (
            stream_in + project_rows(attended_home, block_outward) + tap_out,
            (windows, attended_home),
        )

    stream_two, block_back, block_saved = jax.vjp(
        block_layer, stream_one, gain_block, zero_qkv, zero_width, has_aux=True
    )

    def grid_front(stream_in, gain_in):
        return layer_norm(stream_in, gain_in).astype(jnp.bfloat16)

    normed_three, grid_front_back = jax.vjp(grid_front, stream_two, gain_grid)
    grid_windows = to_grid(to_exchanged(normed_three), WIN)

    def grid_core(windows_in, tap_in):
        return window_attention(windows_in, grid_inward, tap_in, HEADS)

    grid_attended, grid_core_back = jax.vjp(grid_core, grid_windows, zero_qkv)
    grid_home = to_home(from_grid(grid_attended, height, breadth, WIN))

    def grid_tail(stream_in, attended_in, tap_in):
        return (stream_in + project_rows(attended_in, grid_outward) + tap_in).astype(jnp.bfloat16)

    output_tile, grid_tail_back = jax.vjp(grid_tail, stream_two, grid_home, zero_width)
    d_stream_two, d_grid_home, tap_grid_out = grid_tail_back(cotangent[0])
    d_grid_attended = to_grid(to_exchanged(d_grid_home), WIN)
    d_grid_windows, tap_grid_in = grid_core_back(d_grid_attended)
    d_normed_three = to_home(from_grid(d_grid_windows, height, breadth, WIN))
    d_stream_extra, d_gain_grid = grid_front_back(d_normed_three)
    d_stream_two = d_stream_two + d_stream_extra
    d_stream_one, d_gain_block, tap_block_in, tap_block_out = block_back(d_stream_two)
    d_conv, d_wide_tail, tap_project = tail_back(d_stream_one)
    d_conv_ext = extended_2(d_conv, (("sy", 0), ("sx", 1)), 1)
    d_kernel = kernel_back(d_conv)[0]
    d_inner = depthwise_back(d_conv_ext, dw_kernel).astype(jnp.bfloat16)
    d_normed, tap_expand = expand_back(d_inner)
    d_wide_front, d_gain_conv = front_back(d_normed)
    token_grad = (d_wide_tail + d_wide_front).astype(jnp.bfloat16)
    local_grads = (
        d_gain_conv,
        outer_sum(normed, tap_expand),
        d_kernel,
        outer_sum(activated, tap_project),
        d_gain_block,
        outer_sum(block_saved[0], tap_block_in),
        outer_sum(block_saved[1], tap_block_out),
        d_gain_grid,
        outer_sum(grid_windows, tap_grid_in),
        outer_sum(grid_home, tap_grid_out),
    )
    summed = reduce_grads(local_grads)
    return (
        output_tile[None],
        token_grad[None],
        summed[0],
        summed[1],
        summed[2],
        summed[3],
        summed[4],
        summed[5],
        summed[6],
        summed[7],
        summed[8],
        summed[9],
    )


def solution(mesh):
    return jax.shard_map(
        body,
        mesh=mesh,
        in_specs=(
            P("rep", "sy", "sx", None),
            P("rep", "sy", "sx", None),
            P(),
            P(),
            P(),
            P(),
            P(),
            P(),
            P(),
            P(),
            P(),
            P(),
        ),
        out_specs=(
            P("rep", "sy", "sx", None),
            P("rep", "sy", "sx", None),
            P("rep"),
            P("rep", None),
            P("rep", None),
            P("rep", None),
            P("rep"),
            P("rep", None),
            P("rep", None),
            P("rep"),
            P("rep", None),
            P("rep", None),
        ),
        check_vma=False,
    )
```

```python
import jax
import jax.numpy as jnp
from jax import lax
from jax.sharding import PartitionSpec as P

HEADS = 8
WIN = 8


EPSILON = 1e-05


def as_sent(value):

    def short(part):
        return part.astype(jnp.bfloat16) if part.dtype == jnp.float32 else part

    return jax.tree.map(short, value)


def extended_2(cells, sides, width):
    height, breadth, channels = cells.shape
    row_count = lax.axis_size("sy")
    col_count = lax.axis_size("sx")
    tiles = row_count * col_count
    row_at = lax.axis_index("sy")
    col_at = lax.axis_index("sx")
    span = max(height, breadth)

    def lay(line):
        return jnp.pad(line, ((0, span - line.shape[0]), (0, 0)))

    sends = (
        ((-1, 0), lay(cells[0])),
        ((1, 0), lay(cells[height - 1])),
        ((0, -1), lay(cells[:, 0])),
        ((0, 1), lay(cells[:, breadth - 1])),
        ((-1, -1), lay(cells[0, :1])),
        ((-1, 1), lay(cells[0, breadth - 1 :])),
        ((1, -1), lay(cells[height - 1, :1])),
        ((1, 1), lay(cells[height - 1, breadth - 1 :])),
    )
    slot = lax.broadcasted_iota(jnp.int32, (tiles, 1, 1), 0)
    row_step = slot // col_count - row_at
    col_step = slot % col_count - col_at
    outgoing = jnp.zeros((tiles, span, channels), cells.dtype)
    for (up, side), line in sends:
        outgoing = jnp.where((row_step == up) & (col_step == side), line[None], outgoing)
    incoming = lax.all_to_all(outgoing, ("sy", "sx"), split_axis=0, concat_axis=0, tiled=True)

    def take(up, side):
        row = row_at + up
        col = col_at + side
        valid = (row >= 0) & (row < row_count) & (col >= 0) & (col < col_count)
        index = jnp.clip(row, 0, row_count - 1) * col_count + jnp.clip(col, 0, col_count - 1)
        line = lax.dynamic_index_in_dim(incoming, index, 0, keepdims=False)
        return jnp.where(valid, line, jnp.zeros_like(line))

    top = jnp.concatenate([take(-1, -1)[:1], take(-1, 0)[:breadth], take(-1, 1)[:1]], axis=0)
    bottom = jnp.concatenate([take(1, -1)[:1], take(1, 0)[:breadth], take(1, 1)[:1]], axis=0)
    middle = jnp.concatenate([take(0, -1)[:height, None], cells, take(0, 1)[:height, None]], axis=1)
    return jnp.concatenate([top[None], middle, bottom[None]], axis=0)

def widen(values):
    return lax.optimization_barrier(values).astype(jnp.float32)


def layer_norm(values, gain):
    row_mean = jnp.mean(values, axis=-1, keepdims=True)
    centred = values - row_mean
    variance = jnp.mean(centred * centred, axis=-1, keepdims=True)
    return centred * lax.rsqrt(variance + EPSILON) * gain


def project_rows(values, weight):
    leading = values.shape[:-1]
    flattened = values.reshape(-1, values.shape[-1])
    product = jnp.dot(flattened, weight, preferred_element_type=jnp.float32)
    return product.reshape(leading + (weight.shape[1],))


def outer_sum(left_side, right_side):
    left_flat = left_side.reshape(-1, left_side.shape[-1])
    right_flat = right_side.reshape(-1, right_side.shape[-1]).astype(jnp.bfloat16)
    return lax.dot_general(
        left_flat, right_flat, (((0,), (0,)), ((), ())), preferred_element_type=jnp.float32
    )


def to_windows(image, side):
    height, breadth, channels = image.shape
    blocks = image.reshape(height // side, side, breadth // side, side, channels)
    return blocks.transpose(0, 2, 1, 3, 4).reshape(-1, side * side, channels)


def from_windows(windows, height, breadth, side):
    channels = windows.shape[-1]
    blocks = windows.reshape(height // side, breadth // side, side, side, channels)
    return blocks.transpose(0, 2, 1, 3, 4).reshape(height, breadth, channels)


def to_grid(image, side):
    height, breadth, channels = image.shape
    blocks = image.reshape(side, height // side, side, breadth // side, channels)
    return blocks.transpose(1, 3, 0, 2, 4).reshape(-1, side * side, channels)


def from_grid(windows, height, breadth, side):
    channels = windows.shape[-1]
    blocks = windows.reshape(height // side, breadth // side, side, side, channels)
    return blocks.transpose(2, 0, 3, 1, 4).reshape(height, breadth, channels)


def window_attention(windows, weight, tap_in, heads):
    count, members, channels = windows.shape
    head_width = channels // heads
    qkv_rows = (project_rows(windows, weight) + tap_in).astype(jnp.bfloat16)
    queries = qkv_rows[..., :channels]
    key_rows = qkv_rows[..., channels : 2 * channels]
    value_rows = qkv_rows[..., 2 * channels :]
    owner = lax.broadcasted_iota(jnp.int32, (heads, channels), 1) // head_width
    mask = (owner == lax.broadcasted_iota(jnp.int32, (heads, channels), 0)).astype(jnp.bfloat16)
    masked = queries[:, None, :, :] * mask[None, :, None, :]
    scores = jnp.einsum(
        "whqc,wkc->whqk", masked, key_rows, preferred_element_type=jnp.float32
    ) * head_width ** (-0.5)
    softmax_out = jax.nn.softmax(scores, axis=-1).astype(jnp.bfloat16)
    spread = jnp.einsum(
        "whqk,wkc->whqc", softmax_out, value_rows, preferred_element_type=jnp.float32
    )
    attended = (spread * mask[None, :, None, :].astype(jnp.float32)).sum(axis=1)
    return attended.astype(jnp.bfloat16)

def depthwise(extended, kernel):
    height = extended.shape[0] - 2
    breadth = extended.shape[1] - 2
    widened = widen(extended)
    summed = jnp.zeros((height, breadth, extended.shape[2]), jnp.float32)
    for tap_index in range(9):
        row_step, col_step = divmod(tap_index, 3)
        summed = (
            summed
            + widened[row_step : row_step + height, col_step : col_step + breadth]
            * kernel[:, tap_index]
        )
    return summed


def depthwise_back(grad_ext, kernel):
    height = grad_ext.shape[0] - 2
    breadth = grad_ext.shape[1] - 2
    summed = jnp.zeros((height, breadth, grad_ext.shape[2]), jnp.float32)
    for tap_index in range(9):
        row_step, col_step = divmod(tap_index, 3)
        summed = (
            summed
            + grad_ext[2 - row_step : 2 - row_step + height, 2 - col_step : 2 - col_step + breadth]
            * kernel[:, tap_index]
        )
    return summed


def swap_blocks(blocks):
    sy_count, sx_count, row_part, col_part, channels = blocks.shape
    flattened = blocks.reshape(sy_count * sx_count, row_part, col_part, channels)
    moved = lax.all_to_all(
        as_sent(flattened), ("sy", "sx"), split_axis=0, concat_axis=0, tiled=True
    ).astype(flattened.dtype)
    return moved.reshape(blocks.shape)


def to_exchanged(image):
    height, breadth, channels = image.shape
    sy_count = lax.axis_size("sy")
    sx_count = lax.axis_size("sx")
    blocks = image.reshape(height // sy_count, sy_count, breadth // sx_count, sx_count, channels)
    moved = swap_blocks(blocks.transpose(1, 3, 0, 2, 4))
    return moved.transpose(0, 2, 1, 3, 4).reshape(height, breadth, channels)


def to_home(image):
    height, breadth, channels = image.shape
    sy_count = lax.axis_size("sy")
    sx_count = lax.axis_size("sx")
    blocks = image.reshape(sy_count, height // sy_count, sx_count, breadth // sx_count, channels)
    moved = swap_blocks(blocks.transpose(0, 2, 1, 3, 4))
    return moved.transpose(2, 0, 3, 1, 4).reshape(height, breadth, channels)


def exchange_sum(values, axes, axis):
    moved = lax.all_to_all(values.astype(jnp.bfloat16), axes, split_axis=axis, concat_axis=axis, tiled=True)
    return moved.astype(jnp.float32).sum(axis)


def reduce_packed(wide):
    parts = lax.axis_size("rep")
    tiles = lax.axis_size(("sy", "sx"))
    widths = [piece.shape[1] for piece in wide]
    packed = jnp.concatenate(wide, axis=1)
    channels, width = packed.shape
    rows = channels // parts
    piece = rows // tiles
    local = exchange_sum(packed.reshape(parts, tiles, piece, width), ("sy", "sx"), 1)
    local = exchange_sum(local, "rep", 0)
    spread = jnp.broadcast_to(local[None].astype(jnp.bfloat16), (tiles, piece, width))
    total = lax.all_to_all(spread, ("sy", "sx"), split_axis=0, concat_axis=0, tiled=True)
    total = total.astype(jnp.float32).reshape(rows, width)
    cuts = []
    offset = 0
    for size in widths:
        cuts.append(total[:, offset : offset + size])
        offset += size
    return cuts


def pad_lanes(columns):
    joined = jnp.concatenate(columns, axis=1)
    return jnp.pad(joined, ((0, 0), (0, -joined.shape[1] % 128)))


def reduce_grads(grads):
    channels = grads[0].shape[0]
    taps = grads[2].shape[1]
    kernel_cols = taps * grads[2].shape[0] // channels
    small = pad_lanes([grads[2].reshape(channels, -1), grads[0][:, None], grads[4][:, None], grads[7][:, None]])
    cuts = reduce_packed([grads[1], grads[5], grads[6], grads[8], grads[9], grads[3].reshape(channels, -1), small])
    small = cuts[6]
    return (
        small[:, kernel_cols],
        cuts[0],
        small[:, :kernel_cols].reshape(-1, taps),
        cuts[5].reshape(-1, grads[3].shape[1]),
        small[:, kernel_cols + 1],
        cuts[1],
        cuts[2],
        small[:, kernel_cols + 2],
        cuts[3],
        cuts[4],
    )

def body(
    features,
    cotangent,
    gain_conv,
    expand_weight,
    dw_kernel,
    project_weight,
    gain_block,
    block_inward,
    block_outward,
    gain_grid,
    grid_inward,
    grid_outward,
):
    image = features[0]
    height, breadth, channels = image.shape
    expand_units = expand_weight.shape[1]
    window_count = height * breadth // (WIN * WIN)
    zero_width = jnp.zeros((height, breadth, channels), jnp.float32)
    zero_expand = jnp.zeros((height, breadth, expand_units), jnp.float32)
    zero_qkv = jnp.zeros((window_count, WIN * WIN, 3 * channels), jnp.float32)
    widened = image.astype(jnp.float32)

    def conv_front(wide_in, gain_in):
        return layer_norm(wide_in, gain_in).astype(jnp.bfloat16)

    normed, front_back = jax.vjp(conv_front, widened, gain_conv)

    def expand_fn(normed_in, tap_in):
        return jax.nn.gelu(project_rows(normed_in, expand_weight) + tap_in).astype(jnp.bfloat16)

    inner, expand_back = jax.vjp(expand_fn, normed, zero_expand)
    inner_ext = extended_2(inner, (("sy", 0), ("sx", 1)), 1)

    def conv_only(kernel_in):
        return depthwise(inner_ext, kernel_in)

    conv_out, kernel_back = jax.vjp(conv_only, dw_kernel)

    def conv_tail(conv_in, wide_in, tap_in):
        activated_in = jax.nn.gelu(conv_in).astype(jnp.bfloat16)
        return (wide_in + project_rows(activated_in, project_weight) + tap_in, activated_in)

    stream_one, tail_back, activated = jax.vjp(
        conv_tail, conv_out, widened, zero_width, has_aux=True
    )

    def block_layer(stream_in, gain_in, tap_in, tap_out):
        normed_two = layer_norm(stream_in, gain_in).astype(jnp.bfloat16)
        windows = to_windows(normed_two, WIN)
        attended = window_attention(windows, block_inward, tap_in, HEADS)
        attended_home = from_windows(attended, height, breadth, WIN)
        return (
            stream_in + project_rows(attended_home, block_outward) + tap_out,
            (windows, attended_home),
        )

    stream_two, block_back, block_saved = jax.vjp(
        block_layer, stream_one, gain_block, zero_qkv, zero_width, has_aux=True
    )

    def grid_front(stream_in, gain_in):
        return layer_norm(stream_in, gain_in).astype(jnp.bfloat16)

    normed_three, grid_front_back = jax.vjp(grid_front, stream_two, gain_grid)
    grid_windows = to_grid(to_exchanged(normed_three), WIN)

    def grid_core(windows_in, tap_in):
        return window_attention(windows_in, grid_inward, tap_in, HEADS)

    grid_attended, grid_core_back = jax.vjp(grid_core, grid_windows, zero_qkv)
    grid_home = to_home(from_grid(grid_attended, height, breadth, WIN))

    def grid_tail(stream_in, attended_in, tap_in):
        return (stream_in + project_rows(attended_in, grid_outward) + tap_in).astype(jnp.bfloat16)

    output_tile, grid_tail_back = jax.vjp(grid_tail, stream_two, grid_home, zero_width)
    d_stream_two, d_grid_home, tap_grid_out = grid_tail_back(cotangent[0])
    d_grid_attended = to_grid(to_exchanged(d_grid_home), WIN)
    d_grid_windows, tap_grid_in = grid_core_back(d_grid_attended)
    d_normed_three = to_home(from_grid(d_grid_windows, height, breadth, WIN))
    d_stream_extra, d_gain_grid = grid_front_back(d_normed_three)
    d_stream_two = d_stream_two + d_stream_extra
    d_stream_one, d_gain_block, tap_block_in, tap_block_out = block_back(d_stream_two)
    d_conv, d_wide_tail, tap_project = tail_back(d_stream_one)
    d_conv_ext = extended_2(d_conv, (("sy", 0), ("sx", 1)), 1)
    d_kernel = kernel_back(d_conv)[0]
    d_inner = depthwise_back(d_conv_ext, dw_kernel).astype(jnp.bfloat16)
    d_normed, tap_expand = expand_back(d_inner)
    d_wide_front, d_gain_conv = front_back(d_normed)
    token_grad = (d_wide_tail + d_wide_front).astype(jnp.bfloat16)
    local_grads = (
        d_gain_conv,
        outer_sum(normed, tap_expand),
        d_kernel,
        outer_sum(activated, tap_project),
        d_gain_block,
        outer_sum(block_saved[0], tap_block_in),
        outer_sum(block_saved[1], tap_block_out),
        d_gain_grid,
        outer_sum(grid_windows, tap_grid_in),
        outer_sum(grid_home, tap_grid_out),
    )
    summed = reduce_grads(local_grads)
    return (
        output_tile[None],
        token_grad[None],
        summed[0],
        summed[1],
        summed[2],
        summed[3],
        summed[4],
        summed[5],
        summed[6],
        summed[7],
        summed[8],
        summed[9],
    )


def solution(mesh):
    return jax.shard_map(
        body,
        mesh=mesh,
        in_specs=(
            P("rep", "sy", "sx", None),
            P("rep", "sy", "sx", None),
            P(),
            P(),
            P(),
            P(),
            P(),
            P(),
            P(),
            P(),
            P(),
            P(),
        ),
        out_specs=(
            P("rep", "sy", "sx", None),
            P("rep", "sy", "sx", None),
            P("rep"),
            P("rep", None),
            P("rep", None),
            P("rep", None),
            P("rep"),
            P("rep", None),
            P("rep", None),
            P("rep"),
            P("rep", None),
            P("rep", None),
        ),
        check_vma=False,
    )
```

```python
import jax
import jax.numpy as jnp
from jax import lax
from jax.sharding import PartitionSpec as P

HEADS = 8
WIN = 8


EPSILON = 1e-05


def as_sent(value):

    def short(part):
        return part.astype(jnp.bfloat16) if part.dtype == jnp.float32 else part

    return jax.tree.map(short, value)


def extended_2(cells, sides, width):
    height, breadth, channels = cells.shape
    row_count = lax.axis_size("sy")
    col_count = lax.axis_size("sx")
    tiles = row_count * col_count
    row_at = lax.axis_index("sy")
    col_at = lax.axis_index("sx")
    span = max(height, breadth)

    def lay(line):
        return jnp.pad(line, ((0, span - line.shape[0]), (0, 0)))

    sends = (
        ((-1, 0), lay(cells[0])),
        ((1, 0), lay(cells[height - 1])),
        ((0, -1), lay(cells[:, 0])),
        ((0, 1), lay(cells[:, breadth - 1])),
        ((-1, -1), lay(cells[0, :1])),
        ((-1, 1), lay(cells[0, breadth - 1 :])),
        ((1, -1), lay(cells[height - 1, :1])),
        ((1, 1), lay(cells[height - 1, breadth - 1 :])),
    )
    slot = lax.broadcasted_iota(jnp.int32, (tiles, 1, 1), 0)
    row_step = slot // col_count - row_at
    col_step = slot % col_count - col_at
    outgoing = jnp.zeros((tiles, span, channels), cells.dtype)
    for (up, side), line in sends:
        outgoing = jnp.where((row_step == up) & (col_step == side), line[None], outgoing)
    incoming = lax.all_to_all(outgoing, ("sy", "sx"), split_axis=0, concat_axis=0, tiled=True)

    def take(up, side):
        row = row_at + up
        col = col_at + side
        valid = (row >= 0) & (row < row_count) & (col >= 0) & (col < col_count)
        index = jnp.clip(row, 0, row_count - 1) * col_count + jnp.clip(col, 0, col_count - 1)
        line = lax.dynamic_index_in_dim(incoming, index, 0, keepdims=False)
        return jnp.where(valid, line, jnp.zeros_like(line))

    top = jnp.concatenate([take(-1, -1)[:1], take(-1, 0)[:breadth], take(-1, 1)[:1]], axis=0)
    bottom = jnp.concatenate([take(1, -1)[:1], take(1, 0)[:breadth], take(1, 1)[:1]], axis=0)
    middle = jnp.concatenate([take(0, -1)[:height, None], cells, take(0, 1)[:height, None]], axis=1)
    return jnp.concatenate([top[None], middle, bottom[None]], axis=0)

def widen(values):
    return lax.optimization_barrier(values).astype(jnp.float32)


def layer_norm(values, gain):
    row_mean = jnp.mean(values, axis=-1, keepdims=True)
    centred = values - row_mean
    variance = jnp.mean(centred * centred, axis=-1, keepdims=True)
    return centred * lax.rsqrt(variance + EPSILON) * gain


def project_rows(values, weight):
    leading = values.shape[:-1]
    flattened = values.reshape(-1, values.shape[-1])
    product = jnp.dot(flattened, weight, preferred_element_type=jnp.float32)
    return product.reshape(leading + (weight.shape[1],))


def outer_sum(left_side, right_side):
    left_flat = left_side.reshape(-1, left_side.shape[-1])
    right_flat = right_side.reshape(-1, right_side.shape[-1]).astype(jnp.bfloat16)
    return lax.dot_general(
        left_flat, right_flat, (((0,), (0,)), ((), ())), preferred_element_type=jnp.float32
    )


def to_windows(image, side):
    height, breadth, channels = image.shape
    blocks = image.reshape(height // side, side, breadth // side, side, channels)
    return blocks.transpose(0, 2, 1, 3, 4).reshape(-1, side * side, channels)


def from_windows(windows, height, breadth, side):
    channels = windows.shape[-1]
    blocks = windows.reshape(height // side, breadth // side, side, side, channels)
    return blocks.transpose(0, 2, 1, 3, 4).reshape(height, breadth, channels)


def to_grid(image, side):
    height, breadth, channels = image.shape
    blocks = image.reshape(side, height // side, side, breadth // side, channels)
    return blocks.transpose(1, 3, 0, 2, 4).reshape(-1, side * side, channels)


def from_grid(windows, height, breadth, side):
    channels = windows.shape[-1]
    blocks = windows.reshape(height // side, breadth // side, side, side, channels)
    return blocks.transpose(2, 0, 3, 1, 4).reshape(height, breadth, channels)


def window_attention(windows, weight, tap_in, heads):
    count, members, channels = windows.shape
    head_width = channels // heads
    qkv_rows = (project_rows(windows, weight) + tap_in).astype(jnp.bfloat16)
    queries = qkv_rows[..., :channels]
    key_rows = qkv_rows[..., channels : 2 * channels]
    value_rows = qkv_rows[..., 2 * channels :]
    owner = lax.broadcasted_iota(jnp.int32, (heads, channels), 1) // head_width
    mask = (owner == lax.broadcasted_iota(jnp.int32, (heads, channels), 0)).astype(jnp.bfloat16)
    masked = queries[:, None, :, :] * mask[None, :, None, :]
    scores = jnp.einsum(
        "whqc,wkc->whqk", masked, key_rows, preferred_element_type=jnp.float32
    ) * head_width ** (-0.5)
    softmax_out = jax.nn.softmax(scores, axis=-1).astype(jnp.bfloat16)
    spread = jnp.einsum(
        "whqk,wkc->whqc", softmax_out, value_rows, preferred_element_type=jnp.float32
    )
    attended = (spread * mask[None, :, None, :].astype(jnp.float32)).sum(axis=1)
    return attended.astype(jnp.bfloat16)

def depthwise(extended, kernel):
    height = extended.shape[0] - 2
    breadth = extended.shape[1] - 2
    widened = widen(extended)
    summed = jnp.zeros((height, breadth, extended.shape[2]), jnp.float32)
    for tap_index in range(9):
        row_step, col_step = divmod(tap_index, 3)
        summed = (
            summed
            + widened[row_step : row_step + height, col_step : col_step + breadth]
            * kernel[:, tap_index]
        )
    return summed


def depthwise_back(grad_ext, kernel):
    height = grad_ext.shape[0] - 2
    breadth = grad_ext.shape[1] - 2
    summed = jnp.zeros((height, breadth, grad_ext.shape[2]), jnp.float32)
    for tap_index in range(9):
        row_step, col_step = divmod(tap_index, 3)
        summed = (
            summed
            + grad_ext[2 - row_step : 2 - row_step + height, 2 - col_step : 2 - col_step + breadth]
            * kernel[:, tap_index]
        )
    return summed


def swap_blocks(blocks):
    sy_count, sx_count, row_part, col_part, channels = blocks.shape
    flattened = blocks.reshape(sy_count * sx_count, row_part, col_part, channels)
    moved = lax.all_to_all(
        as_sent(flattened), ("sy", "sx"), split_axis=0, concat_axis=0, tiled=True
    ).astype(flattened.dtype)
    return moved.reshape(blocks.shape)


def to_exchanged(image):
    height, breadth, channels = image.shape
    sy_count = lax.axis_size("sy")
    sx_count = lax.axis_size("sx")
    blocks = image.reshape(height // sy_count, sy_count, breadth // sx_count, sx_count, channels)
    moved = swap_blocks(blocks.transpose(1, 3, 0, 2, 4))
    return moved.transpose(0, 2, 1, 3, 4).reshape(height, breadth, channels)


def to_home(image):
    height, breadth, channels = image.shape
    sy_count = lax.axis_size("sy")
    sx_count = lax.axis_size("sx")
    blocks = image.reshape(sy_count, height // sy_count, sx_count, breadth // sx_count, channels)
    moved = swap_blocks(blocks.transpose(0, 2, 1, 3, 4))
    return moved.transpose(2, 0, 3, 1, 4).reshape(height, breadth, channels)


def exchange_sum(values, axes, axis):
    moved = lax.all_to_all(values.astype(jnp.bfloat16), axes, split_axis=axis, concat_axis=axis, tiled=True)
    return moved.astype(jnp.float32).sum(axis)


def halve_sum(values, axis, dim):
    count = lax.axis_size(axis)
    at = lax.axis_index(axis)
    bit = 1
    while bit < count:
        bit *= 2
    bit //= 2
    while bit >= 1:
        shape = values.shape
        split = shape[:dim] + (shape[dim] // (2 * bit), 2, bit) + shape[dim + 1 :]
        values = values.reshape(split)
        mine = (at // bit) % 2
        keep = lax.dynamic_index_in_dim(values, mine, dim + 1, keepdims=False)
        send = lax.dynamic_index_in_dim(values, 1 - mine, dim + 1, keepdims=False)
        pairs = [(i, i ^ bit) for i in range(count)]
        came = lax.ppermute(send.astype(jnp.bfloat16), axis, pairs)
        values = keep + came.astype(jnp.float32)
        values = values.reshape(shape[:dim] + (shape[dim] // 2,) + shape[dim + 1 :])
        bit //= 2
    return lax.squeeze(values, (dim,)) if values.shape[dim] == 1 else values


def reduce_packed(wide):
    parts = lax.axis_size("rep")
    tiles = lax.axis_size(("sy", "sx"))
    widths = [piece.shape[1] for piece in wide]
    packed = jnp.concatenate(wide, axis=1)
    channels, width = packed.shape
    rows = channels // parts
    piece = rows // tiles
    local = packed.reshape(parts, lax.axis_size("sy"), lax.axis_size("sx"), piece, width)
    local = halve_sum(local, "sx", 2)
    local = halve_sum(local, "sy", 1)
    local = exchange_sum(local, "rep", 0)
    spread = jnp.broadcast_to(local[None].astype(jnp.bfloat16), (tiles, piece, width))
    total = lax.all_to_all(spread, ("sy", "sx"), split_axis=0, concat_axis=0, tiled=True)
    total = total.astype(jnp.float32).reshape(rows, width)
    cuts = []
    offset = 0
    for size in widths:
        cuts.append(total[:, offset : offset + size])
        offset += size
    return cuts


def pad_lanes(columns):
    joined = jnp.concatenate(columns, axis=1)
    return jnp.pad(joined, ((0, 0), (0, -joined.shape[1] % 128)))


def reduce_grads(grads):
    channels = grads[0].shape[0]
    taps = grads[2].shape[1]
    kernel_cols = taps * grads[2].shape[0] // channels
    small = pad_lanes([grads[2].reshape(channels, -1), grads[0][:, None], grads[4][:, None], grads[7][:, None]])
    cuts = reduce_packed([grads[1], grads[5], grads[6], grads[8], grads[9], grads[3].reshape(channels, -1), small])
    small = cuts[6]
    return (
        small[:, kernel_cols],
        cuts[0],
        small[:, :kernel_cols].reshape(-1, taps),
        cuts[5].reshape(-1, grads[3].shape[1]),
        small[:, kernel_cols + 1],
        cuts[1],
        cuts[2],
        small[:, kernel_cols + 2],
        cuts[3],
        cuts[4],
    )

def body(
    features,
    cotangent,
    gain_conv,
    expand_weight,
    dw_kernel,
    project_weight,
    gain_block,
    block_inward,
    block_outward,
    gain_grid,
    grid_inward,
    grid_outward,
):
    image = features[0]
    height, breadth, channels = image.shape
    expand_units = expand_weight.shape[1]
    window_count = height * breadth // (WIN * WIN)
    zero_width = jnp.zeros((height, breadth, channels), jnp.float32)
    zero_expand = jnp.zeros((height, breadth, expand_units), jnp.float32)
    zero_qkv = jnp.zeros((window_count, WIN * WIN, 3 * channels), jnp.float32)
    widened = image.astype(jnp.float32)

    def conv_front(wide_in, gain_in):
        return layer_norm(wide_in, gain_in).astype(jnp.bfloat16)

    normed, front_back = jax.vjp(conv_front, widened, gain_conv)

    def expand_fn(normed_in, tap_in):
        return jax.nn.gelu(project_rows(normed_in, expand_weight) + tap_in).astype(jnp.bfloat16)

    inner, expand_back = jax.vjp(expand_fn, normed, zero_expand)
    inner_ext = extended_2(inner, (("sy", 0), ("sx", 1)), 1)

    def conv_only(kernel_in):
        return depthwise(inner_ext, kernel_in)

    conv_out, kernel_back = jax.vjp(conv_only, dw_kernel)

    def conv_tail(conv_in, wide_in, tap_in):
        activated_in = jax.nn.gelu(conv_in).astype(jnp.bfloat16)
        return (wide_in + project_rows(activated_in, project_weight) + tap_in, activated_in)

    stream_one, tail_back, activated = jax.vjp(
        conv_tail, conv_out, widened, zero_width, has_aux=True
    )

    def block_layer(stream_in, gain_in, tap_in, tap_out):
        normed_two = layer_norm(stream_in, gain_in).astype(jnp.bfloat16)
        windows = to_windows(normed_two, WIN)
        attended = window_attention(windows, block_inward, tap_in, HEADS)
        attended_home = from_windows(attended, height, breadth, WIN)
        return (
            stream_in + project_rows(attended_home, block_outward) + tap_out,
            (windows, attended_home),
        )

    stream_two, block_back, block_saved = jax.vjp(
        block_layer, stream_one, gain_block, zero_qkv, zero_width, has_aux=True
    )

    def grid_front(stream_in, gain_in):
        return layer_norm(stream_in, gain_in).astype(jnp.bfloat16)

    normed_three, grid_front_back = jax.vjp(grid_front, stream_two, gain_grid)
    grid_windows = to_grid(to_exchanged(normed_three), WIN)

    def grid_core(windows_in, tap_in):
        return window_attention(windows_in, grid_inward, tap_in, HEADS)

    grid_attended, grid_core_back = jax.vjp(grid_core, grid_windows, zero_qkv)
    grid_home = to_home(from_grid(grid_attended, height, breadth, WIN))

    def grid_tail(stream_in, attended_in, tap_in):
        return (stream_in + project_rows(attended_in, grid_outward) + tap_in).astype(jnp.bfloat16)

    output_tile, grid_tail_back = jax.vjp(grid_tail, stream_two, grid_home, zero_width)
    d_stream_two, d_grid_home, tap_grid_out = grid_tail_back(cotangent[0])
    d_grid_attended = to_grid(to_exchanged(d_grid_home), WIN)
    d_grid_windows, tap_grid_in = grid_core_back(d_grid_attended)
    d_normed_three = to_home(from_grid(d_grid_windows, height, breadth, WIN))
    d_stream_extra, d_gain_grid = grid_front_back(d_normed_three)
    d_stream_two = d_stream_two + d_stream_extra
    d_stream_one, d_gain_block, tap_block_in, tap_block_out = block_back(d_stream_two)
    d_conv, d_wide_tail, tap_project = tail_back(d_stream_one)
    d_conv_ext = extended_2(d_conv, (("sy", 0), ("sx", 1)), 1)
    d_kernel = kernel_back(d_conv)[0]
    d_inner = depthwise_back(d_conv_ext, dw_kernel).astype(jnp.bfloat16)
    d_normed, tap_expand = expand_back(d_inner)
    d_wide_front, d_gain_conv = front_back(d_normed)
    token_grad = (d_wide_tail + d_wide_front).astype(jnp.bfloat16)
    local_grads = (
        d_gain_conv,
        outer_sum(normed, tap_expand),
        d_kernel,
        outer_sum(activated, tap_project),
        d_gain_block,
        outer_sum(block_saved[0], tap_block_in),
        outer_sum(block_saved[1], tap_block_out),
        d_gain_grid,
        outer_sum(grid_windows, tap_grid_in),
        outer_sum(grid_home, tap_grid_out),
    )
    summed = reduce_grads(local_grads)
    return (
        output_tile[None],
        token_grad[None],
        summed[0],
        summed[1],
        summed[2],
        summed[3],
        summed[4],
        summed[5],
        summed[6],
        summed[7],
        summed[8],
        summed[9],
    )


def solution(mesh):
    return jax.shard_map(
        body,
        mesh=mesh,
        in_specs=(
            P("rep", "sy", "sx", None),
            P("rep", "sy", "sx", None),
            P(),
            P(),
            P(),
            P(),
            P(),
            P(),
            P(),
            P(),
            P(),
            P(),
        ),
        out_specs=(
            P("rep", "sy", "sx", None),
            P("rep", "sy", "sx", None),
            P("rep"),
            P("rep", None),
            P("rep", None),
            P("rep", None),
            P("rep"),
            P("rep", None),
            P("rep", None),
            P("rep"),
            P("rep", None),
            P("rep", None),
        ),
        check_vma=False,
    )
```

```python
import jax
import jax.numpy as jnp
from jax import lax
from jax.sharding import PartitionSpec as P

HEADS = 8
WIN = 8


EPSILON = 1e-05


def as_sent(value):

    def short(part):
        return part.astype(jnp.bfloat16) if part.dtype == jnp.float32 else part

    return jax.tree.map(short, value)


def extended_2(cells, sides, width):
    height, breadth, channels = cells.shape
    row_count = lax.axis_size("sy")
    col_count = lax.axis_size("sx")
    tiles = row_count * col_count
    row_at = lax.axis_index("sy")
    col_at = lax.axis_index("sx")
    span = max(height, breadth)

    def lay(line):
        return jnp.pad(line, ((0, span - line.shape[0]), (0, 0)))

    sends = (
        ((-1, 0), lay(cells[0])),
        ((1, 0), lay(cells[height - 1])),
        ((0, -1), lay(cells[:, 0])),
        ((0, 1), lay(cells[:, breadth - 1])),
        ((-1, -1), lay(cells[0, :1])),
        ((-1, 1), lay(cells[0, breadth - 1 :])),
        ((1, -1), lay(cells[height - 1, :1])),
        ((1, 1), lay(cells[height - 1, breadth - 1 :])),
    )
    slot = lax.broadcasted_iota(jnp.int32, (tiles, 1, 1), 0)
    row_step = slot // col_count - row_at
    col_step = slot % col_count - col_at
    outgoing = jnp.zeros((tiles, span, channels), cells.dtype)
    for (up, side), line in sends:
        outgoing = jnp.where((row_step == up) & (col_step == side), line[None], outgoing)
    incoming = lax.all_to_all(outgoing, ("sy", "sx"), split_axis=0, concat_axis=0, tiled=True)

    def take(up, side):
        row = row_at + up
        col = col_at + side
        valid = (row >= 0) & (row < row_count) & (col >= 0) & (col < col_count)
        index = jnp.clip(row, 0, row_count - 1) * col_count + jnp.clip(col, 0, col_count - 1)
        line = lax.dynamic_index_in_dim(incoming, index, 0, keepdims=False)
        return jnp.where(valid, line, jnp.zeros_like(line))

    top = jnp.concatenate([take(-1, -1)[:1], take(-1, 0)[:breadth], take(-1, 1)[:1]], axis=0)
    bottom = jnp.concatenate([take(1, -1)[:1], take(1, 0)[:breadth], take(1, 1)[:1]], axis=0)
    middle = jnp.concatenate([take(0, -1)[:height, None], cells, take(0, 1)[:height, None]], axis=1)
    return jnp.concatenate([top[None], middle, bottom[None]], axis=0)

def widen(values):
    return lax.optimization_barrier(values).astype(jnp.float32)


def layer_norm(values, gain):
    row_mean = jnp.mean(values, axis=-1, keepdims=True)
    centred = values - row_mean
    variance = jnp.mean(centred * centred, axis=-1, keepdims=True)
    return centred * lax.rsqrt(variance + EPSILON) * gain


def project_rows(values, weight):
    leading = values.shape[:-1]
    flattened = values.reshape(-1, values.shape[-1])
    product = jnp.dot(flattened, weight, preferred_element_type=jnp.float32)
    return product.reshape(leading + (weight.shape[1],))


def outer_sum(left_side, right_side):
    left_flat = left_side.reshape(-1, left_side.shape[-1])
    right_flat = right_side.reshape(-1, right_side.shape[-1]).astype(jnp.bfloat16)
    return lax.dot_general(
        left_flat, right_flat, (((0,), (0,)), ((), ())), preferred_element_type=jnp.float32
    )


def to_windows(image, side):
    height, breadth, channels = image.shape
    blocks = image.reshape(height // side, side, breadth // side, side, channels)
    return blocks.transpose(0, 2, 1, 3, 4).reshape(-1, side * side, channels)


def from_windows(windows, height, breadth, side):
    channels = windows.shape[-1]
    blocks = windows.reshape(height // side, breadth // side, side, side, channels)
    return blocks.transpose(0, 2, 1, 3, 4).reshape(height, breadth, channels)


def to_grid(image, side):
    height, breadth, channels = image.shape
    blocks = image.reshape(side, height // side, side, breadth // side, channels)
    return blocks.transpose(1, 3, 0, 2, 4).reshape(-1, side * side, channels)


def from_grid(windows, height, breadth, side):
    channels = windows.shape[-1]
    blocks = windows.reshape(height // side, breadth // side, side, side, channels)
    return blocks.transpose(2, 0, 3, 1, 4).reshape(height, breadth, channels)


def window_attention(windows, weight, tap_in, heads):
    count, members, channels = windows.shape
    head_width = channels // heads
    qkv_rows = (project_rows(windows, weight) + tap_in).astype(jnp.bfloat16)
    queries = qkv_rows[..., :channels]
    key_rows = qkv_rows[..., channels : 2 * channels]
    value_rows = qkv_rows[..., 2 * channels :]
    owner = lax.broadcasted_iota(jnp.int32, (heads, channels), 1) // head_width
    mask = (owner == lax.broadcasted_iota(jnp.int32, (heads, channels), 0)).astype(jnp.bfloat16)
    masked = queries[:, None, :, :] * mask[None, :, None, :]
    scores = jnp.einsum(
        "whqc,wkc->whqk", masked, key_rows, preferred_element_type=jnp.float32
    ) * head_width ** (-0.5)
    softmax_out = jax.nn.softmax(scores, axis=-1).astype(jnp.bfloat16)
    spread = jnp.einsum(
        "whqk,wkc->whqc", softmax_out, value_rows, preferred_element_type=jnp.float32
    )
    attended = (spread * mask[None, :, None, :].astype(jnp.float32)).sum(axis=1)
    return attended.astype(jnp.bfloat16)

def depthwise(extended, kernel):
    height = extended.shape[0] - 2
    breadth = extended.shape[1] - 2
    widened = widen(extended)
    summed = jnp.zeros((height, breadth, extended.shape[2]), jnp.float32)
    for tap_index in range(9):
        row_step, col_step = divmod(tap_index, 3)
        summed = (
            summed
            + widened[row_step : row_step + height, col_step : col_step + breadth]
            * kernel[:, tap_index]
        )
    return summed


def depthwise_back(grad_ext, kernel):
    height = grad_ext.shape[0] - 2
    breadth = grad_ext.shape[1] - 2
    summed = jnp.zeros((height, breadth, grad_ext.shape[2]), jnp.float32)
    for tap_index in range(9):
        row_step, col_step = divmod(tap_index, 3)
        summed = (
            summed
            + grad_ext[2 - row_step : 2 - row_step + height, 2 - col_step : 2 - col_step + breadth]
            * kernel[:, tap_index]
        )
    return summed


def swap_blocks(blocks):
    sy_count, sx_count, row_part, col_part, channels = blocks.shape
    flattened = blocks.reshape(sy_count * sx_count, row_part, col_part, channels)
    moved = lax.all_to_all(flattened, ("sy", "sx"), split_axis=0, concat_axis=0, tiled=True)
    return moved.reshape(blocks.shape)


def to_exchanged(image):
    height, breadth, channels = image.shape
    sy_count = lax.axis_size("sy")
    sx_count = lax.axis_size("sx")
    blocks = image.reshape(height // sy_count, sy_count, breadth // sx_count, sx_count, channels)
    moved = swap_blocks(blocks.transpose(1, 3, 0, 2, 4))
    return moved.transpose(0, 2, 1, 3, 4).reshape(height, breadth, channels)


def to_home(image):
    height, breadth, channels = image.shape
    sy_count = lax.axis_size("sy")
    sx_count = lax.axis_size("sx")
    blocks = image.reshape(sy_count, height // sy_count, sx_count, breadth // sx_count, channels)
    moved = swap_blocks(blocks.transpose(0, 2, 1, 3, 4))
    return moved.transpose(2, 0, 3, 1, 4).reshape(height, breadth, channels)


def exchange_sum(values, axes, axis):
    moved = lax.all_to_all(values.astype(jnp.bfloat16), axes, split_axis=axis, concat_axis=axis, tiled=True)
    return moved.astype(jnp.float32).sum(axis)


def reduce_packed(wide):
    parts = lax.axis_size("rep")
    tiles = lax.axis_size(("sy", "sx"))
    widths = [piece.shape[1] for piece in wide]
    packed = jnp.concatenate(wide, axis=1)
    channels, width = packed.shape
    rows = channels // parts
    piece = rows // tiles
    local = exchange_sum(packed.reshape(parts, tiles, piece, width), ("sy", "sx"), 1)
    local = exchange_sum(local, "rep", 0)
    spread = jnp.broadcast_to(local[None].astype(jnp.bfloat16), (tiles, piece, width))
    total = lax.all_to_all(spread, ("sy", "sx"), split_axis=0, concat_axis=0, tiled=True)
    total = total.astype(jnp.float32).reshape(rows, width)
    cuts = []
    offset = 0
    for size in widths:
        cuts.append(total[:, offset : offset + size])
        offset += size
    return cuts


def pad_lanes(columns):
    joined = jnp.concatenate(columns, axis=1)
    return jnp.pad(joined, ((0, 0), (0, -joined.shape[1] % 128)))


def reduce_grads(grads):
    channels = grads[0].shape[0]
    taps = grads[2].shape[1]
    kernel_cols = taps * grads[2].shape[0] // channels
    small = pad_lanes([grads[2].reshape(channels, -1), grads[0][:, None], grads[4][:, None], grads[7][:, None]])
    cuts = reduce_packed([grads[1], grads[5], grads[6], grads[8], grads[9], grads[3].reshape(channels, -1), small])
    small = cuts[6]
    return (
        small[:, kernel_cols],
        cuts[0],
        small[:, :kernel_cols].reshape(-1, taps),
        cuts[5].reshape(-1, grads[3].shape[1]),
        small[:, kernel_cols + 1],
        cuts[1],
        cuts[2],
        small[:, kernel_cols + 2],
        cuts[3],
        cuts[4],
    )

def body(
    features,
    cotangent,
    gain_conv,
    expand_weight,
    dw_kernel,
    project_weight,
    gain_block,
    block_inward,
    block_outward,
    gain_grid,
    grid_inward,
    grid_outward,
):
    image = features[0]
    height, breadth, channels = image.shape
    expand_units = expand_weight.shape[1]
    window_count = height * breadth // (WIN * WIN)
    zero_width = jnp.zeros((height, breadth, channels), jnp.float32)
    zero_expand = jnp.zeros((height, breadth, expand_units), jnp.float32)
    zero_qkv = jnp.zeros((window_count, WIN * WIN, 3 * channels), jnp.float32)
    widened = image.astype(jnp.float32)

    def conv_front(wide_in, gain_in):
        return layer_norm(wide_in, gain_in).astype(jnp.bfloat16)

    normed, front_back = jax.vjp(conv_front, widened, gain_conv)

    def expand_fn(normed_in, tap_in):
        return jax.nn.gelu(project_rows(normed_in, expand_weight) + tap_in).astype(jnp.bfloat16)

    inner, expand_back = jax.vjp(expand_fn, normed, zero_expand)
    inner_ext = extended_2(inner, (("sy", 0), ("sx", 1)), 1)

    def conv_only(kernel_in):
        return depthwise(inner_ext, kernel_in)

    conv_out, kernel_back = jax.vjp(conv_only, dw_kernel)

    def conv_tail(conv_in, wide_in, tap_in):
        activated_in = jax.nn.gelu(conv_in).astype(jnp.bfloat16)
        return (wide_in + project_rows(activated_in, project_weight) + tap_in, activated_in)

    stream_one, tail_back, activated = jax.vjp(
        conv_tail, conv_out, widened, zero_width, has_aux=True
    )

    def block_layer(stream_in, gain_in, tap_in, tap_out):
        normed_two = layer_norm(stream_in, gain_in).astype(jnp.bfloat16)
        windows = to_windows(normed_two, WIN)
        attended = window_attention(windows, block_inward, tap_in, HEADS)
        attended_home = from_windows(attended, height, breadth, WIN)
        return (
            stream_in + project_rows(attended_home, block_outward) + tap_out,
            (windows, attended_home),
        )

    stream_two, block_back, block_saved = jax.vjp(
        block_layer, stream_one, gain_block, zero_qkv, zero_width, has_aux=True
    )

    def grid_front(stream_in, gain_in):
        return layer_norm(stream_in, gain_in).astype(jnp.bfloat16)

    stream_two_grid = to_grid(to_exchanged(stream_two), WIN)
    grid_windows, grid_front_back = jax.vjp(grid_front, stream_two_grid, gain_grid)

    def grid_core(windows_in, tap_in):
        return window_attention(windows_in, grid_inward, tap_in, HEADS)

    grid_attended, grid_core_back = jax.vjp(grid_core, grid_windows, zero_qkv)

    def grid_tail(stream_in, attended_in, tap_in):
        return (stream_in + project_rows(attended_in, grid_outward) + tap_in).astype(jnp.bfloat16)

    zero_grid = jnp.zeros(stream_two_grid.shape, jnp.float32)
    output_grid, grid_tail_back = jax.vjp(grid_tail, stream_two_grid, grid_attended, zero_grid)
    output_tile = to_home(from_grid(output_grid, height, breadth, WIN))
    cotangent_grid = to_grid(to_exchanged(cotangent[0]), WIN)
    d_stream_grid, d_grid_attended, tap_grid_out = grid_tail_back(cotangent_grid)
    d_grid_windows, tap_grid_in = grid_core_back(d_grid_attended)
    d_stream_extra, d_gain_grid = grid_front_back(d_grid_windows)
    d_stream_two = to_home(from_grid(d_stream_grid + d_stream_extra, height, breadth, WIN))
    d_stream_one, d_gain_block, tap_block_in, tap_block_out = block_back(d_stream_two)
    d_conv, d_wide_tail, tap_project = tail_back(d_stream_one)
    d_conv_ext = extended_2(d_conv, (("sy", 0), ("sx", 1)), 1)
    d_kernel = kernel_back(d_conv)[0]
    d_inner = depthwise_back(d_conv_ext, dw_kernel).astype(jnp.bfloat16)
    d_normed, tap_expand = expand_back(d_inner)
    d_wide_front, d_gain_conv = front_back(d_normed)
    token_grad = (d_wide_tail + d_wide_front).astype(jnp.bfloat16)
    local_grads = (
        d_gain_conv,
        outer_sum(normed, tap_expand),
        d_kernel,
        outer_sum(activated, tap_project),
        d_gain_block,
        outer_sum(block_saved[0], tap_block_in),
        outer_sum(block_saved[1], tap_block_out),
        d_gain_grid,
        outer_sum(grid_windows, tap_grid_in),
        outer_sum(grid_attended, tap_grid_out),
    )
    summed = reduce_grads(local_grads)
    return (
        output_tile[None],
        token_grad[None],
        summed[0],
        summed[1],
        summed[2],
        summed[3],
        summed[4],
        summed[5],
        summed[6],
        summed[7],
        summed[8],
        summed[9],
    )


def solution(mesh):
    return jax.shard_map(
        body,
        mesh=mesh,
        in_specs=(
            P("rep", "sy", "sx", None),
            P("rep", "sy", "sx", None),
            P(),
            P(),
            P(),
            P(),
            P(),
            P(),
            P(),
            P(),
            P(),
            P(),
        ),
        out_specs=(
            P("rep", "sy", "sx", None),
            P("rep", "sy", "sx", None),
            P("rep"),
            P("rep", None),
            P("rep", None),
            P("rep", None),
            P("rep"),
            P("rep", None),
            P("rep", None),
            P("rep"),
            P("rep", None),
            P("rep", None),
        ),
        check_vma=False,
    )
```

```python
import jax
import jax.numpy as jnp
from jax import lax
from jax.sharding import PartitionSpec as P

HEADS = 8
WIN = 8


EPSILON = 1e-05


def as_sent(value):

    def short(part):
        return part.astype(jnp.bfloat16) if part.dtype == jnp.float32 else part

    return jax.tree.map(short, value)


def extended_2(cells, sides, width):
    height, breadth, channels = cells.shape
    row_count = lax.axis_size("sy")
    col_count = lax.axis_size("sx")
    tiles = row_count * col_count
    row_at = lax.axis_index("sy")
    col_at = lax.axis_index("sx")
    span = max(height, breadth)

    def lay(line):
        return jnp.pad(line, ((0, span - line.shape[0]), (0, 0)))

    sends = (
        ((-1, 0), lay(cells[0])),
        ((1, 0), lay(cells[height - 1])),
        ((0, -1), lay(cells[:, 0])),
        ((0, 1), lay(cells[:, breadth - 1])),
        ((-1, -1), lay(cells[0, :1])),
        ((-1, 1), lay(cells[0, breadth - 1 :])),
        ((1, -1), lay(cells[height - 1, :1])),
        ((1, 1), lay(cells[height - 1, breadth - 1 :])),
    )
    slot = lax.broadcasted_iota(jnp.int32, (tiles, 1, 1), 0)
    row_step = slot // col_count - row_at
    col_step = slot % col_count - col_at
    outgoing = jnp.zeros((tiles, span, channels), cells.dtype)
    for (up, side), line in sends:
        outgoing = jnp.where((row_step == up) & (col_step == side), line[None], outgoing)
    incoming = lax.all_to_all(outgoing, ("sy", "sx"), split_axis=0, concat_axis=0, tiled=True)

    def take(up, side):
        row = row_at + up
        col = col_at + side
        valid = (row >= 0) & (row < row_count) & (col >= 0) & (col < col_count)
        index = jnp.clip(row, 0, row_count - 1) * col_count + jnp.clip(col, 0, col_count - 1)
        line = lax.dynamic_index_in_dim(incoming, index, 0, keepdims=False)
        return jnp.where(valid, line, jnp.zeros_like(line))

    top = jnp.concatenate([take(-1, -1)[:1], take(-1, 0)[:breadth], take(-1, 1)[:1]], axis=0)
    bottom = jnp.concatenate([take(1, -1)[:1], take(1, 0)[:breadth], take(1, 1)[:1]], axis=0)
    middle = jnp.concatenate([take(0, -1)[:height, None], cells, take(0, 1)[:height, None]], axis=1)
    return jnp.concatenate([top[None], middle, bottom[None]], axis=0)

def widen(values):
    return lax.optimization_barrier(values).astype(jnp.float32)


def layer_norm(values, gain):
    row_mean = jnp.mean(values, axis=-1, keepdims=True)
    centred = values - row_mean
    variance = jnp.mean(centred * centred, axis=-1, keepdims=True)
    return centred * lax.rsqrt(variance + EPSILON) * gain


def project_rows(values, weight):
    leading = values.shape[:-1]
    flattened = values.reshape(-1, values.shape[-1])
    product = jnp.dot(flattened, weight, preferred_element_type=jnp.float32)
    return product.reshape(leading + (weight.shape[1],))


def outer_sum(left_side, right_side):
    left_flat = left_side.reshape(-1, left_side.shape[-1])
    right_flat = right_side.reshape(-1, right_side.shape[-1]).astype(jnp.bfloat16)
    return lax.dot_general(
        left_flat, right_flat, (((0,), (0,)), ((), ())), preferred_element_type=jnp.float32
    )


def to_windows(image, side):
    height, breadth, channels = image.shape
    blocks = image.reshape(height // side, side, breadth // side, side, channels)
    return blocks.transpose(0, 2, 1, 3, 4).reshape(-1, side * side, channels)


def from_windows(windows, height, breadth, side):
    channels = windows.shape[-1]
    blocks = windows.reshape(height // side, breadth // side, side, side, channels)
    return blocks.transpose(0, 2, 1, 3, 4).reshape(height, breadth, channels)


def to_grid(image, side):
    height, breadth, channels = image.shape
    blocks = image.reshape(side, height // side, side, breadth // side, channels)
    return blocks.transpose(1, 3, 0, 2, 4).reshape(-1, side * side, channels)


def from_grid(windows, height, breadth, side):
    channels = windows.shape[-1]
    blocks = windows.reshape(height // side, breadth // side, side, side, channels)
    return blocks.transpose(2, 0, 3, 1, 4).reshape(height, breadth, channels)


def window_attention(windows, weight, tap_in, heads):
    count, members, channels = windows.shape
    head_width = channels // heads
    qkv_rows = (project_rows(windows, weight) + tap_in).astype(jnp.bfloat16)
    queries = qkv_rows[..., :channels]
    key_rows = qkv_rows[..., channels : 2 * channels]
    value_rows = qkv_rows[..., 2 * channels :]
    owner = lax.broadcasted_iota(jnp.int32, (heads, channels), 1) // head_width
    mask = (owner == lax.broadcasted_iota(jnp.int32, (heads, channels), 0)).astype(jnp.bfloat16)
    masked = queries[:, None, :, :] * mask[None, :, None, :]
    scores = jnp.einsum(
        "whqc,wkc->whqk", masked, key_rows, preferred_element_type=jnp.float32
    ) * head_width ** (-0.5)
    softmax_out = jax.nn.softmax(scores, axis=-1).astype(jnp.bfloat16)
    spread = jnp.einsum(
        "whqk,wkc->whqc", softmax_out, value_rows, preferred_element_type=jnp.float32
    )
    attended = (spread * mask[None, :, None, :].astype(jnp.float32)).sum(axis=1)
    return attended.astype(jnp.bfloat16)

def depthwise(extended, kernel):
    height = extended.shape[0] - 2
    breadth = extended.shape[1] - 2
    widened = widen(extended)
    summed = jnp.zeros((height, breadth, extended.shape[2]), jnp.float32)
    for tap_index in range(9):
        row_step, col_step = divmod(tap_index, 3)
        summed = (
            summed
            + widened[row_step : row_step + height, col_step : col_step + breadth]
            * kernel[:, tap_index]
        )
    return summed


def depthwise_back(grad_ext, kernel):
    height = grad_ext.shape[0] - 2
    breadth = grad_ext.shape[1] - 2
    summed = jnp.zeros((height, breadth, grad_ext.shape[2]), jnp.float32)
    for tap_index in range(9):
        row_step, col_step = divmod(tap_index, 3)
        summed = (
            summed
            + grad_ext[2 - row_step : 2 - row_step + height, 2 - col_step : 2 - col_step + breadth]
            * kernel[:, tap_index]
        )
    return summed


def swap_blocks(blocks):
    sy_count, sx_count, row_part, col_part, channels = blocks.shape
    flattened = blocks.reshape(sy_count * sx_count, row_part, col_part, channels)
    moved = lax.all_to_all(
        as_sent(flattened), ("sy", "sx"), split_axis=0, concat_axis=0, tiled=True
    ).astype(flattened.dtype)
    return moved.reshape(blocks.shape)


def to_exchanged(image):
    height, breadth, channels = image.shape
    sy_count = lax.axis_size("sy")
    sx_count = lax.axis_size("sx")
    blocks = image.reshape(height // sy_count, sy_count, breadth // sx_count, sx_count, channels)
    moved = swap_blocks(blocks.transpose(1, 3, 0, 2, 4))
    return moved.transpose(0, 2, 1, 3, 4).reshape(height, breadth, channels)


def to_home(image):
    height, breadth, channels = image.shape
    sy_count = lax.axis_size("sy")
    sx_count = lax.axis_size("sx")
    blocks = image.reshape(sy_count, height // sy_count, sx_count, breadth // sx_count, channels)
    moved = swap_blocks(blocks.transpose(0, 2, 1, 3, 4))
    return moved.transpose(2, 0, 3, 1, 4).reshape(height, breadth, channels)


def exchange_sum(values, axes, axis):
    moved = lax.all_to_all(values.astype(jnp.bfloat16), axes, split_axis=axis, concat_axis=axis, tiled=True)
    return moved.astype(jnp.float32).sum(axis)


def reduce_packed(wide):
    parts = lax.axis_size("rep")
    tiles = lax.axis_size(("sy", "sx"))
    widths = [piece.shape[1] for piece in wide]
    packed = jnp.concatenate(wide, axis=1)
    channels, width = packed.shape
    rows = channels // parts
    piece = rows // tiles
    local = exchange_sum(packed.reshape(parts, tiles, piece, width), ("sy", "sx"), 1)
    local = exchange_sum(local, "rep", 0)
    spread = jnp.broadcast_to(local[None].astype(jnp.bfloat16), (tiles, piece, width))
    total = lax.all_to_all(spread, ("sy", "sx"), split_axis=0, concat_axis=0, tiled=True)
    total = total.astype(jnp.float32).reshape(rows, width)
    cuts = []
    offset = 0
    for size in widths:
        cuts.append(total[:, offset : offset + size])
        offset += size
    return cuts


def pad_lanes(columns):
    joined = jnp.concatenate(columns, axis=1)
    return jnp.pad(joined, ((0, 0), (0, -joined.shape[1] % 128)))


def reduce_grads(grads):
    channels = grads[0].shape[0]
    taps = grads[2].shape[1]
    kernel_cols = taps * grads[2].shape[0] // channels
    small = pad_lanes([grads[2].reshape(channels, -1), grads[0][:, None], grads[4][:, None], grads[7][:, None]])
    cuts = reduce_packed([grads[1], grads[5], grads[6], grads[8], grads[9], grads[3].reshape(channels, -1), small])
    small = cuts[6]
    return (
        small[:, kernel_cols],
        cuts[0],
        small[:, :kernel_cols].reshape(-1, taps),
        cuts[5].reshape(-1, grads[3].shape[1]),
        small[:, kernel_cols + 1],
        cuts[1],
        cuts[2],
        small[:, kernel_cols + 2],
        cuts[3],
        cuts[4],
    )

def body(
    features,
    cotangent,
    gain_conv,
    expand_weight,
    dw_kernel,
    project_weight,
    gain_block,
    block_inward,
    block_outward,
    gain_grid,
    grid_inward,
    grid_outward,
):
    image = features[0]
    height, breadth, channels = image.shape
    expand_units = expand_weight.shape[1]
    window_count = height * breadth // (WIN * WIN)
    zero_width = jnp.zeros((height, breadth, channels), jnp.float32)
    zero_expand = jnp.zeros((height, breadth, expand_units), jnp.float32)
    zero_qkv = jnp.zeros((window_count, WIN * WIN, 3 * channels), jnp.float32)
    widened = image.astype(jnp.float32)

    def conv_front(wide_in, gain_in):
        return layer_norm(wide_in, gain_in).astype(jnp.bfloat16)

    normed, front_back = jax.vjp(conv_front, widened, gain_conv)

    def expand_fn(normed_in, tap_in):
        return jax.nn.gelu(project_rows(normed_in, expand_weight) + tap_in).astype(jnp.bfloat16)

    inner, expand_back = jax.vjp(expand_fn, normed, zero_expand)
    features_ext = extended_2(image, (("sy", 0), ("sx", 1)), 1)
    border = jnp.concatenate(
        [features_ext[0], features_ext[height + 1], features_ext[1 : height + 1, 0], features_ext[1 : height + 1, breadth + 1]],
        axis=0,
    )
    border_normed = conv_front(border.astype(jnp.float32), gain_conv)
    border_inner = expand_fn(border_normed, jnp.zeros((border.shape[0], expand_units), jnp.float32))
    top_inner = border_inner[: breadth + 2]
    bottom_inner = border_inner[breadth + 2 : 2 * breadth + 4]
    left_inner = border_inner[2 * breadth + 4 : 2 * breadth + 4 + height]
    right_inner = border_inner[2 * breadth + 4 + height :]
    inner_ext = jnp.concatenate(
        [top_inner[None], jnp.concatenate([left_inner[:, None], inner, right_inner[:, None]], axis=1), bottom_inner[None]],
        axis=0,
    )

    def conv_only(kernel_in):
        return depthwise(inner_ext, kernel_in)

    conv_out, kernel_back = jax.vjp(conv_only, dw_kernel)

    def conv_tail(conv_in, wide_in, tap_in):
        activated_in = jax.nn.gelu(conv_in).astype(jnp.bfloat16)
        return (wide_in + project_rows(activated_in, project_weight) + tap_in, activated_in)

    stream_one, tail_back, activated = jax.vjp(
        conv_tail, conv_out, widened, zero_width, has_aux=True
    )

    def block_layer(stream_in, gain_in, tap_in, tap_out):
        normed_two = layer_norm(stream_in, gain_in).astype(jnp.bfloat16)
        windows = to_windows(normed_two, WIN)
        attended = window_attention(windows, block_inward, tap_in, HEADS)
        attended_home = from_windows(attended, height, breadth, WIN)
        return (
            stream_in + project_rows(attended_home, block_outward) + tap_out,
            (windows, attended_home),
        )

    stream_two, block_back, block_saved = jax.vjp(
        block_layer, stream_one, gain_block, zero_qkv, zero_width, has_aux=True
    )

    def grid_front(stream_in, gain_in):
        return layer_norm(stream_in, gain_in).astype(jnp.bfloat16)

    normed_three, grid_front_back = jax.vjp(grid_front, stream_two, gain_grid)
    grid_windows = to_grid(to_exchanged(normed_three), WIN)

    def grid_core(windows_in, tap_in):
        return window_attention(windows_in, grid_inward, tap_in, HEADS)

    grid_attended, grid_core_back = jax.vjp(grid_core, grid_windows, zero_qkv)
    grid_home = to_home(from_grid(grid_attended, height, breadth, WIN))

    def grid_tail(stream_in, attended_in, tap_in):
        return (stream_in + project_rows(attended_in, grid_outward) + tap_in).astype(jnp.bfloat16)

    output_tile, grid_tail_back = jax.vjp(grid_tail, stream_two, grid_home, zero_width)
    d_stream_two, d_grid_home, tap_grid_out = grid_tail_back(cotangent[0])
    d_grid_attended = to_grid(to_exchanged(d_grid_home), WIN)
    d_grid_windows, tap_grid_in = grid_core_back(d_grid_attended)
    d_normed_three = to_home(from_grid(d_grid_windows, height, breadth, WIN))
    d_stream_extra, d_gain_grid = grid_front_back(d_normed_three)
    d_stream_two = d_stream_two + d_stream_extra
    d_stream_one, d_gain_block, tap_block_in, tap_block_out = block_back(d_stream_two)
    d_conv, d_wide_tail, tap_project = tail_back(d_stream_one)
    d_conv_ext = extended_2(d_conv, (("sy", 0), ("sx", 1)), 1)
    d_kernel = kernel_back(d_conv)[0]
    d_inner = depthwise_back(d_conv_ext, dw_kernel).astype(jnp.bfloat16)
    d_normed, tap_expand = expand_back(d_inner)
    d_wide_front, d_gain_conv = front_back(d_normed)
    token_grad = (d_wide_tail + d_wide_front).astype(jnp.bfloat16)
    local_grads = (
        d_gain_conv,
        outer_sum(normed, tap_expand),
        d_kernel,
        outer_sum(activated, tap_project),
        d_gain_block,
        outer_sum(block_saved[0], tap_block_in),
        outer_sum(block_saved[1], tap_block_out),
        d_gain_grid,
        outer_sum(grid_windows, tap_grid_in),
        outer_sum(grid_home, tap_grid_out),
    )
    summed = reduce_grads(local_grads)
    return (
        output_tile[None],
        token_grad[None],
        summed[0],
        summed[1],
        summed[2],
        summed[3],
        summed[4],
        summed[5],
        summed[6],
        summed[7],
        summed[8],
        summed[9],
    )


def solution(mesh):
    return jax.shard_map(
        body,
        mesh=mesh,
        in_specs=(
            P("rep", "sy", "sx", None),
            P("rep", "sy", "sx", None),
            P(),
            P(),
            P(),
            P(),
            P(),
            P(),
            P(),
            P(),
            P(),
            P(),
        ),
        out_specs=(
            P("rep", "sy", "sx", None),
            P("rep", "sy", "sx", None),
            P("rep"),
            P("rep", None),
            P("rep", None),
            P("rep", None),
            P("rep"),
            P("rep", None),
            P("rep", None),
            P("rep"),
            P("rep", None),
            P("rep", None),
        ),
        check_vma=False,
    )
```

```python
import jax
import jax.numpy as jnp
from jax import lax
from jax.sharding import PartitionSpec as P

HEADS = 8
WIN = 8


EPSILON = 1e-05


def as_sent(value):

    def short(part):
        return part.astype(jnp.bfloat16) if part.dtype == jnp.float32 else part

    return jax.tree.map(short, value)


def extended_2(cells, sides, width):
    height, breadth, channels = cells.shape
    row_count = lax.axis_size("sy")
    col_count = lax.axis_size("sx")
    tiles = row_count * col_count
    row_at = lax.axis_index("sy")
    col_at = lax.axis_index("sx")
    span = max(height, breadth)

    def lay(line):
        return jnp.pad(line, ((0, span - line.shape[0]), (0, 0)))

    sends = (
        ((-1, 0), lay(cells[0])),
        ((1, 0), lay(cells[height - 1])),
        ((0, -1), lay(cells[:, 0])),
        ((0, 1), lay(cells[:, breadth - 1])),
        ((-1, -1), lay(cells[0, :1])),
        ((-1, 1), lay(cells[0, breadth - 1 :])),
        ((1, -1), lay(cells[height - 1, :1])),
        ((1, 1), lay(cells[height - 1, breadth - 1 :])),
    )
    slot = lax.broadcasted_iota(jnp.int32, (tiles, 1, 1), 0)
    row_step = slot // col_count - row_at
    col_step = slot % col_count - col_at
    outgoing = jnp.zeros((tiles, span, channels), cells.dtype)
    for (up, side), line in sends:
        outgoing = jnp.where((row_step == up) & (col_step == side), line[None], outgoing)
    incoming = lax.all_to_all(outgoing, ("sy", "sx"), split_axis=0, concat_axis=0, tiled=True)

    def take(up, side):
        row = row_at + up
        col = col_at + side
        valid = (row >= 0) & (row < row_count) & (col >= 0) & (col < col_count)
        index = jnp.clip(row, 0, row_count - 1) * col_count + jnp.clip(col, 0, col_count - 1)
        line = lax.dynamic_index_in_dim(incoming, index, 0, keepdims=False)
        return jnp.where(valid, line, jnp.zeros_like(line))

    top = jnp.concatenate([take(-1, -1)[:1], take(-1, 0)[:breadth], take(-1, 1)[:1]], axis=0)
    bottom = jnp.concatenate([take(1, -1)[:1], take(1, 0)[:breadth], take(1, 1)[:1]], axis=0)
    middle = jnp.concatenate([take(0, -1)[:height, None], cells, take(0, 1)[:height, None]], axis=1)
    return jnp.concatenate([top[None], middle, bottom[None]], axis=0)

def widen(values):
    return lax.optimization_barrier(values).astype(jnp.float32)


def layer_norm(values, gain):
    row_mean = jnp.mean(values, axis=-1, keepdims=True)
    centred = values - row_mean
    variance = jnp.mean(centred * centred, axis=-1, keepdims=True)
    return centred * lax.rsqrt(variance + EPSILON) * gain


def project_rows(values, weight):
    leading = values.shape[:-1]
    flattened = values.reshape(-1, values.shape[-1])
    product = jnp.dot(flattened, weight, preferred_element_type=jnp.float32)
    return product.reshape(leading + (weight.shape[1],))


def outer_sum(left_side, right_side):
    left_flat = left_side.reshape(-1, left_side.shape[-1])
    right_flat = right_side.reshape(-1, right_side.shape[-1]).astype(jnp.bfloat16)
    return lax.dot_general(
        left_flat, right_flat, (((0,), (0,)), ((), ())), preferred_element_type=jnp.float32
    )


def to_windows(image, side):
    height, breadth, channels = image.shape
    blocks = image.reshape(height // side, side, breadth // side, side, channels)
    return blocks.transpose(0, 2, 1, 3, 4).reshape(-1, side * side, channels)


def from_windows(windows, height, breadth, side):
    channels = windows.shape[-1]
    blocks = windows.reshape(height // side, breadth // side, side, side, channels)
    return blocks.transpose(0, 2, 1, 3, 4).reshape(height, breadth, channels)


def to_grid(image, side):
    height, breadth, channels = image.shape
    blocks = image.reshape(side, height // side, side, breadth // side, channels)
    return blocks.transpose(1, 3, 0, 2, 4).reshape(-1, side * side, channels)


def from_grid(windows, height, breadth, side):
    channels = windows.shape[-1]
    blocks = windows.reshape(height // side, breadth // side, side, side, channels)
    return blocks.transpose(2, 0, 3, 1, 4).reshape(height, breadth, channels)


def window_attention(windows, weight, tap_in, heads):
    count, members, channels = windows.shape
    head_width = channels // heads
    qkv_rows = (project_rows(windows, weight) + tap_in).astype(jnp.bfloat16)
    queries = qkv_rows[..., :channels]
    key_rows = qkv_rows[..., channels : 2 * channels]
    value_rows = qkv_rows[..., 2 * channels :]
    owner = lax.broadcasted_iota(jnp.int32, (heads, channels), 1) // head_width
    mask = (owner == lax.broadcasted_iota(jnp.int32, (heads, channels), 0)).astype(jnp.bfloat16)
    masked = queries[:, None, :, :] * mask[None, :, None, :]
    scores = jnp.einsum(
        "whqc,wkc->whqk", masked, key_rows, preferred_element_type=jnp.float32
    ) * head_width ** (-0.5)
    softmax_out = jax.nn.softmax(scores, axis=-1).astype(jnp.bfloat16)
    spread = jnp.einsum(
        "whqk,wkc->whqc", softmax_out, value_rows, preferred_element_type=jnp.float32
    )
    attended = (spread * mask[None, :, None, :].astype(jnp.float32)).sum(axis=1)
    return attended.astype(jnp.bfloat16)

def depthwise(extended, kernel):
    height = extended.shape[0] - 2
    breadth = extended.shape[1] - 2
    widened = widen(extended)
    summed = jnp.zeros((height, breadth, extended.shape[2]), jnp.float32)
    for tap_index in range(9):
        row_step, col_step = divmod(tap_index, 3)
        summed = (
            summed
            + widened[row_step : row_step + height, col_step : col_step + breadth]
            * kernel[:, tap_index]
        )
    return summed


def depthwise_back(grad_ext, kernel):
    height = grad_ext.shape[0] - 2
    breadth = grad_ext.shape[1] - 2
    summed = jnp.zeros((height, breadth, grad_ext.shape[2]), jnp.float32)
    for tap_index in range(9):
        row_step, col_step = divmod(tap_index, 3)
        summed = (
            summed
            + grad_ext[2 - row_step : 2 - row_step + height, 2 - col_step : 2 - col_step + breadth]
            * kernel[:, tap_index]
        )
    return summed


def swap_blocks(blocks):
    sy_count, sx_count, row_part, col_part, channels = blocks.shape
    flattened = blocks.reshape(sy_count * sx_count, row_part, col_part, channels)
    moved = lax.all_to_all(
        as_sent(flattened), ("sy", "sx"), split_axis=0, concat_axis=0, tiled=True
    ).astype(flattened.dtype)
    return moved.reshape(blocks.shape)


def to_exchanged(image):
    height, breadth, channels = image.shape
    sy_count = lax.axis_size("sy")
    sx_count = lax.axis_size("sx")
    blocks = image.reshape(height // sy_count, sy_count, breadth // sx_count, sx_count, channels)
    moved = swap_blocks(blocks.transpose(1, 3, 0, 2, 4))
    return moved.transpose(0, 2, 1, 3, 4).reshape(height, breadth, channels)


def to_home(image):
    height, breadth, channels = image.shape
    sy_count = lax.axis_size("sy")
    sx_count = lax.axis_size("sx")
    blocks = image.reshape(sy_count, height // sy_count, sx_count, breadth // sx_count, channels)
    moved = swap_blocks(blocks.transpose(0, 2, 1, 3, 4))
    return moved.transpose(2, 0, 3, 1, 4).reshape(height, breadth, channels)


def exchange_sum(values, axes, axis):
    moved = lax.all_to_all(values.astype(jnp.bfloat16), axes, split_axis=axis, concat_axis=axis, tiled=True)
    return moved.astype(jnp.float32).sum(axis)


def tile_sum(wide):
    parts = lax.axis_size("rep")
    tiles = lax.axis_size(("sy", "sx"))
    packed = jnp.concatenate(wide, axis=1)
    channels, width = packed.shape
    piece = channels // parts // tiles
    return exchange_sum(packed.reshape(parts, tiles, piece, width), ("sy", "sx"), 1)


def reduce_packed(groups):
    tiles = lax.axis_size(("sy", "sx"))
    widths = [piece.shape[1] for wide in groups for piece in wide]
    local = jnp.concatenate([tile_sum(wide) for wide in groups], axis=-1)
    parts, piece, width = local.shape
    local = exchange_sum(local, "rep", 0)
    spread = jnp.broadcast_to(local[None].astype(jnp.bfloat16), (tiles, piece, width))
    total = lax.all_to_all(spread, ("sy", "sx"), split_axis=0, concat_axis=0, tiled=True)
    total = total.astype(jnp.float32).reshape(piece * tiles, width)
    cuts = []
    offset = 0
    for size in widths:
        cuts.append(total[:, offset : offset + size])
        offset += size
    return cuts


def pad_lanes(columns):
    joined = jnp.concatenate(columns, axis=1)
    return jnp.pad(joined, ((0, 0), (0, -joined.shape[1] % 128)))


def reduce_grads(grads):
    channels = grads[0].shape[0]
    taps = grads[2].shape[1]
    kernel_cols = taps * grads[2].shape[0] // channels
    cuts = reduce_packed(
        (
            [grads[5], grads[6], grads[8], grads[9], pad_lanes([grads[4][:, None], grads[7][:, None]])],
            [grads[1], grads[3].reshape(channels, -1), pad_lanes([grads[2].reshape(channels, -1), grads[0][:, None]])],
        )
    )
    return (
        cuts[7][:, kernel_cols],
        cuts[5],
        cuts[7][:, :kernel_cols].reshape(-1, taps),
        cuts[6].reshape(-1, grads[3].shape[1]),
        cuts[4][:, 0],
        cuts[0],
        cuts[1],
        cuts[4][:, 1],
        cuts[2],
        cuts[3],
    )

def body(
    features,
    cotangent,
    gain_conv,
    expand_weight,
    dw_kernel,
    project_weight,
    gain_block,
    block_inward,
    block_outward,
    gain_grid,
    grid_inward,
    grid_outward,
):
    image = features[0]
    height, breadth, channels = image.shape
    expand_units = expand_weight.shape[1]
    window_count = height * breadth // (WIN * WIN)
    zero_width = jnp.zeros((height, breadth, channels), jnp.float32)
    zero_expand = jnp.zeros((height, breadth, expand_units), jnp.float32)
    zero_qkv = jnp.zeros((window_count, WIN * WIN, 3 * channels), jnp.float32)
    widened = image.astype(jnp.float32)

    def conv_front(wide_in, gain_in):
        return layer_norm(wide_in, gain_in).astype(jnp.bfloat16)

    normed, front_back = jax.vjp(conv_front, widened, gain_conv)

    def expand_fn(normed_in, tap_in):
        return jax.nn.gelu(project_rows(normed_in, expand_weight) + tap_in).astype(jnp.bfloat16)

    inner, expand_back = jax.vjp(expand_fn, normed, zero_expand)
    inner_ext = extended_2(inner, (("sy", 0), ("sx", 1)), 1)

    def conv_only(kernel_in):
        return depthwise(inner_ext, kernel_in)

    conv_out, kernel_back = jax.vjp(conv_only, dw_kernel)

    def conv_tail(conv_in, wide_in, tap_in):
        activated_in = jax.nn.gelu(conv_in).astype(jnp.bfloat16)
        return (wide_in + project_rows(activated_in, project_weight) + tap_in, activated_in)

    stream_one, tail_back, activated = jax.vjp(
        conv_tail, conv_out, widened, zero_width, has_aux=True
    )

    def block_layer(stream_in, gain_in, tap_in, tap_out):
        normed_two = layer_norm(stream_in, gain_in).astype(jnp.bfloat16)
        windows = to_windows(normed_two, WIN)
        attended = window_attention(windows, block_inward, tap_in, HEADS)
        attended_home = from_windows(attended, height, breadth, WIN)
        return (
            stream_in + project_rows(attended_home, block_outward) + tap_out,
            (windows, attended_home),
        )

    stream_two, block_back, block_saved = jax.vjp(
        block_layer, stream_one, gain_block, zero_qkv, zero_width, has_aux=True
    )

    def grid_front(stream_in, gain_in):
        return layer_norm(stream_in, gain_in).astype(jnp.bfloat16)

    normed_three, grid_front_back = jax.vjp(grid_front, stream_two, gain_grid)
    grid_windows = to_grid(to_exchanged(normed_three), WIN)

    def grid_core(windows_in, tap_in):
        return window_attention(windows_in, grid_inward, tap_in, HEADS)

    grid_attended, grid_core_back = jax.vjp(grid_core, grid_windows, zero_qkv)
    grid_home = to_home(from_grid(grid_attended, height, breadth, WIN))

    def grid_tail(stream_in, attended_in, tap_in):
        return (stream_in + project_rows(attended_in, grid_outward) + tap_in).astype(jnp.bfloat16)

    output_tile, grid_tail_back = jax.vjp(grid_tail, stream_two, grid_home, zero_width)
    d_stream_two, d_grid_home, tap_grid_out = grid_tail_back(cotangent[0])
    d_grid_attended = to_grid(to_exchanged(d_grid_home), WIN)
    d_grid_windows, tap_grid_in = grid_core_back(d_grid_attended)
    d_normed_three = to_home(from_grid(d_grid_windows, height, breadth, WIN))
    d_stream_extra, d_gain_grid = grid_front_back(d_normed_three)
    d_stream_two = d_stream_two + d_stream_extra
    d_stream_one, d_gain_block, tap_block_in, tap_block_out = block_back(d_stream_two)
    d_conv, d_wide_tail, tap_project = tail_back(d_stream_one)
    d_conv_ext = extended_2(d_conv, (("sy", 0), ("sx", 1)), 1)
    d_kernel = kernel_back(d_conv)[0]
    d_inner = depthwise_back(d_conv_ext, dw_kernel).astype(jnp.bfloat16)
    d_normed, tap_expand = expand_back(d_inner)
    d_wide_front, d_gain_conv = front_back(d_normed)
    token_grad = (d_wide_tail + d_wide_front).astype(jnp.bfloat16)
    local_grads = (
        d_gain_conv,
        outer_sum(normed, tap_expand),
        d_kernel,
        outer_sum(activated, tap_project),
        d_gain_block,
        outer_sum(block_saved[0], tap_block_in),
        outer_sum(block_saved[1], tap_block_out),
        d_gain_grid,
        outer_sum(grid_windows, tap_grid_in),
        outer_sum(grid_home, tap_grid_out),
    )
    summed = reduce_grads(local_grads)
    return (
        output_tile[None],
        token_grad[None],
        summed[0],
        summed[1],
        summed[2],
        summed[3],
        summed[4],
        summed[5],
        summed[6],
        summed[7],
        summed[8],
        summed[9],
    )


def solution(mesh):
    return jax.shard_map(
        body,
        mesh=mesh,
        in_specs=(
            P("rep", "sy", "sx", None),
            P("rep", "sy", "sx", None),
            P(),
            P(),
            P(),
            P(),
            P(),
            P(),
            P(),
            P(),
            P(),
            P(),
        ),
        out_specs=(
            P("rep", "sy", "sx", None),
            P("rep", "sy", "sx", None),
            P("rep"),
            P("rep", None),
            P("rep", None),
            P("rep", None),
            P("rep"),
            P("rep", None),
            P("rep", None),
            P("rep"),
            P("rep", None),
            P("rep", None),
        ),
        check_vma=False,
    )
```

```python
import jax
import jax.numpy as jnp
from jax import lax
from jax.sharding import PartitionSpec as P

HEADS = 8
WIN = 8


EPSILON = 1e-05


def as_sent(value):

    def short(part):
        return part.astype(jnp.bfloat16) if part.dtype == jnp.float32 else part

    return jax.tree.map(short, value)


def extended_2(cells, sides, width):
    height, breadth, channels = cells.shape
    row_count = lax.axis_size("sy")
    col_count = lax.axis_size("sx")
    tiles = row_count * col_count
    row_at = lax.axis_index("sy")
    col_at = lax.axis_index("sx")
    span = max(height, breadth)

    def lay(line):
        return jnp.pad(line, ((0, span - line.shape[0]), (0, 0)))

    sends = (
        ((-1, 0), lay(cells[0])),
        ((1, 0), lay(cells[height - 1])),
        ((0, -1), lay(cells[:, 0])),
        ((0, 1), lay(cells[:, breadth - 1])),
        ((-1, -1), lay(cells[0, :1])),
        ((-1, 1), lay(cells[0, breadth - 1 :])),
        ((1, -1), lay(cells[height - 1, :1])),
        ((1, 1), lay(cells[height - 1, breadth - 1 :])),
    )
    slot = lax.broadcasted_iota(jnp.int32, (tiles, 1, 1), 0)
    row_step = slot // col_count - row_at
    col_step = slot % col_count - col_at
    outgoing = jnp.zeros((tiles, span, channels), cells.dtype)
    for (up, side), line in sends:
        outgoing = jnp.where((row_step == up) & (col_step == side), line[None], outgoing)
    incoming = lax.all_to_all(outgoing, ("sy", "sx"), split_axis=0, concat_axis=0, tiled=True)

    def take(up, side):
        row = row_at + up
        col = col_at + side
        valid = (row >= 0) & (row < row_count) & (col >= 0) & (col < col_count)
        index = jnp.clip(row, 0, row_count - 1) * col_count + jnp.clip(col, 0, col_count - 1)
        line = lax.dynamic_index_in_dim(incoming, index, 0, keepdims=False)
        return jnp.where(valid, line, jnp.zeros_like(line))

    top = jnp.concatenate([take(-1, -1)[:1], take(-1, 0)[:breadth], take(-1, 1)[:1]], axis=0)
    bottom = jnp.concatenate([take(1, -1)[:1], take(1, 0)[:breadth], take(1, 1)[:1]], axis=0)
    middle = jnp.concatenate([take(0, -1)[:height, None], cells, take(0, 1)[:height, None]], axis=1)
    return jnp.concatenate([top[None], middle, bottom[None]], axis=0)

def widen(values):
    return lax.optimization_barrier(values).astype(jnp.float32)


def layer_norm(values, gain):
    row_mean = jnp.mean(values, axis=-1, keepdims=True)
    centred = values - row_mean
    variance = jnp.mean(centred * centred, axis=-1, keepdims=True)
    return centred * lax.rsqrt(variance + EPSILON) * gain


def project_rows(values, weight):
    leading = values.shape[:-1]
    flattened = values.reshape(-1, values.shape[-1])
    product = jnp.dot(flattened, weight, preferred_element_type=jnp.float32)
    return product.reshape(leading + (weight.shape[1],))


def outer_sum(left_side, right_side):
    left_flat = left_side.reshape(-1, left_side.shape[-1])
    right_flat = right_side.reshape(-1, right_side.shape[-1]).astype(jnp.bfloat16)
    return lax.dot_general(
        left_flat, right_flat, (((0,), (0,)), ((), ())), preferred_element_type=jnp.float32
    )


def to_windows(image, side):
    height, breadth, channels = image.shape
    blocks = image.reshape(height // side, side, breadth // side, side, channels)
    return blocks.transpose(0, 2, 1, 3, 4).reshape(-1, side * side, channels)


def from_windows(windows, height, breadth, side):
    channels = windows.shape[-1]
    blocks = windows.reshape(height // side, breadth // side, side, side, channels)
    return blocks.transpose(0, 2, 1, 3, 4).reshape(height, breadth, channels)


def to_grid(image, side):
    height, breadth, channels = image.shape
    blocks = image.reshape(side, height // side, side, breadth // side, channels)
    return blocks.transpose(1, 3, 0, 2, 4).reshape(-1, side * side, channels)


def from_grid(windows, height, breadth, side):
    channels = windows.shape[-1]
    blocks = windows.reshape(height // side, breadth // side, side, side, channels)
    return blocks.transpose(2, 0, 3, 1, 4).reshape(height, breadth, channels)


def window_attention(windows, weight, tap_in, heads):
    count, members, channels = windows.shape
    head_width = channels // heads
    qkv_rows = (project_rows(windows, weight) + tap_in).astype(jnp.bfloat16)
    queries = qkv_rows[..., :channels]
    key_rows = qkv_rows[..., channels : 2 * channels]
    value_rows = qkv_rows[..., 2 * channels :]
    owner = lax.broadcasted_iota(jnp.int32, (heads, channels), 1) // head_width
    mask = (owner == lax.broadcasted_iota(jnp.int32, (heads, channels), 0)).astype(jnp.bfloat16)
    masked = queries[:, None, :, :] * mask[None, :, None, :]
    scores = jnp.einsum(
        "whqc,wkc->whqk", masked, key_rows, preferred_element_type=jnp.float32
    ) * head_width ** (-0.5)
    softmax_out = jax.nn.softmax(scores, axis=-1).astype(jnp.bfloat16)
    spread = jnp.einsum(
        "whqk,wkc->whqc", softmax_out, value_rows, preferred_element_type=jnp.float32
    )
    attended = (spread * mask[None, :, None, :].astype(jnp.float32)).sum(axis=1)
    return attended.astype(jnp.bfloat16)

def depthwise(extended, kernel):
    height = extended.shape[0] - 2
    breadth = extended.shape[1] - 2
    widened = widen(extended)
    summed = jnp.zeros((height, breadth, extended.shape[2]), jnp.float32)
    for tap_index in range(9):
        row_step, col_step = divmod(tap_index, 3)
        summed = (
            summed
            + widened[row_step : row_step + height, col_step : col_step + breadth]
            * kernel[:, tap_index]
        )
    return summed


def depthwise_back(grad_ext, kernel):
    height = grad_ext.shape[0] - 2
    breadth = grad_ext.shape[1] - 2
    summed = jnp.zeros((height, breadth, grad_ext.shape[2]), jnp.float32)
    for tap_index in range(9):
        row_step, col_step = divmod(tap_index, 3)
        summed = (
            summed
            + grad_ext[2 - row_step : 2 - row_step + height, 2 - col_step : 2 - col_step + breadth]
            * kernel[:, tap_index]
        )
    return summed


def swap_blocks(blocks):
    sy_count, sx_count, row_part, col_part, channels = blocks.shape
    flattened = blocks.reshape(sy_count * sx_count, row_part, col_part, channels)
    moved = lax.all_to_all(
        as_sent(flattened), ("sy", "sx"), split_axis=0, concat_axis=0, tiled=True
    ).astype(flattened.dtype)
    return moved.reshape(blocks.shape)


def to_exchanged(image):
    height, breadth, channels = image.shape
    sy_count = lax.axis_size("sy")
    sx_count = lax.axis_size("sx")
    blocks = image.reshape(height // sy_count, sy_count, breadth // sx_count, sx_count, channels)
    moved = swap_blocks(blocks.transpose(1, 3, 0, 2, 4))
    return moved.transpose(0, 2, 1, 3, 4).reshape(height, breadth, channels)


def to_home(image):
    height, breadth, channels = image.shape
    sy_count = lax.axis_size("sy")
    sx_count = lax.axis_size("sx")
    blocks = image.reshape(sy_count, height // sy_count, sx_count, breadth // sx_count, channels)
    moved = swap_blocks(blocks.transpose(0, 2, 1, 3, 4))
    return moved.transpose(2, 0, 3, 1, 4).reshape(height, breadth, channels)


def exchange_sum(values, axes, axis):
    moved = lax.all_to_all(values.astype(jnp.bfloat16), axes, split_axis=axis, concat_axis=axis, tiled=True)
    return moved.astype(jnp.float32).sum(axis)


def tile_sum(wide):
    parts = lax.axis_size("rep")
    tiles = lax.axis_size(("sy", "sx"))
    packed = jnp.concatenate(wide, axis=1)
    channels, width = packed.shape
    piece = channels // parts // tiles
    return exchange_sum(packed.reshape(parts, tiles, piece, width), ("sy", "sx"), 1)


def reduce_packed(groups):
    tiles = lax.axis_size(("sy", "sx"))
    widths = [piece.shape[1] for wide in groups for piece in wide]
    local = jnp.concatenate([tile_sum(wide) for wide in groups], axis=-1)
    parts, piece, width = local.shape
    local = exchange_sum(local, "rep", 0)
    spread = jnp.broadcast_to(local[None].astype(jnp.bfloat16), (tiles, piece, width))
    total = lax.all_to_all(spread, ("sy", "sx"), split_axis=0, concat_axis=0, tiled=True)
    total = total.astype(jnp.float32).reshape(piece * tiles, width)
    cuts = []
    offset = 0
    for size in widths:
        cuts.append(total[:, offset : offset + size])
        offset += size
    return cuts


def pad_lanes(columns):
    joined = jnp.concatenate(columns, axis=1)
    return jnp.pad(joined, ((0, 0), (0, -joined.shape[1] % 128)))


def reduce_grads(grads):
    channels = grads[0].shape[0]
    taps = grads[2].shape[1]
    kernel_cols = taps * grads[2].shape[0] // channels
    cuts = reduce_packed(
        (
            [grads[5], grads[6], grads[8], grads[9], grads[3].reshape(channels, -1), pad_lanes([grads[4][:, None], grads[7][:, None]])],
            [grads[1], pad_lanes([grads[2].reshape(channels, -1), grads[0][:, None]])],
        )
    )
    return (
        cuts[7][:, kernel_cols],
        cuts[6],
        cuts[7][:, :kernel_cols].reshape(-1, taps),
        cuts[4].reshape(-1, grads[3].shape[1]),
        cuts[5][:, 0],
        cuts[0],
        cuts[1],
        cuts[5][:, 1],
        cuts[2],
        cuts[3],
    )

def body(
    features,
    cotangent,
    gain_conv,
    expand_weight,
    dw_kernel,
    project_weight,
    gain_block,
    block_inward,
    block_outward,
    gain_grid,
    grid_inward,
    grid_outward,
):
    image = features[0]
    height, breadth, channels = image.shape
    expand_units = expand_weight.shape[1]
    window_count = height * breadth // (WIN * WIN)
    zero_width = jnp.zeros((height, breadth, channels), jnp.float32)
    zero_expand = jnp.zeros((height, breadth, expand_units), jnp.float32)
    zero_qkv = jnp.zeros((window_count, WIN * WIN, 3 * channels), jnp.float32)
    widened = image.astype(jnp.float32)

    def conv_front(wide_in, gain_in):
        return layer_norm(wide_in, gain_in).astype(jnp.bfloat16)

    normed, front_back = jax.vjp(conv_front, widened, gain_conv)

    def expand_fn(normed_in, tap_in):
        return jax.nn.gelu(project_rows(normed_in, expand_weight) + tap_in).astype(jnp.bfloat16)

    inner, expand_back = jax.vjp(expand_fn, normed, zero_expand)
    inner_ext = extended_2(inner, (("sy", 0), ("sx", 1)), 1)

    def conv_only(kernel_in):
        return depthwise(inner_ext, kernel_in)

    conv_out, kernel_back = jax.vjp(conv_only, dw_kernel)

    def conv_tail(conv_in, wide_in, tap_in):
        activated_in = jax.nn.gelu(conv_in).astype(jnp.bfloat16)
        return (wide_in + project_rows(activated_in, project_weight) + tap_in, activated_in)

    stream_one, tail_back, activated = jax.vjp(
        conv_tail, conv_out, widened, zero_width, has_aux=True
    )

    def block_layer(stream_in, gain_in, tap_in, tap_out):
        normed_two = layer_norm(stream_in, gain_in).astype(jnp.bfloat16)
        windows = to_windows(normed_two, WIN)
        attended = window_attention(windows, block_inward, tap_in, HEADS)
        attended_home = from_windows(attended, height, breadth, WIN)
        return (
            stream_in + project_rows(attended_home, block_outward) + tap_out,
            (windows, attended_home),
        )

    stream_two, block_back, block_saved = jax.vjp(
        block_layer, stream_one, gain_block, zero_qkv, zero_width, has_aux=True
    )

    def grid_front(stream_in, gain_in):
        return layer_norm(stream_in, gain_in).astype(jnp.bfloat16)

    normed_three, grid_front_back = jax.vjp(grid_front, stream_two, gain_grid)
    grid_windows = to_grid(to_exchanged(normed_three), WIN)

    def grid_core(windows_in, tap_in):
        return window_attention(windows_in, grid_inward, tap_in, HEADS)

    grid_attended, grid_core_back = jax.vjp(grid_core, grid_windows, zero_qkv)
    grid_home = to_home(from_grid(grid_attended, height, breadth, WIN))

    def grid_tail(stream_in, attended_in, tap_in):
        return (stream_in + project_rows(attended_in, grid_outward) + tap_in).astype(jnp.bfloat16)

    output_tile, grid_tail_back = jax.vjp(grid_tail, stream_two, grid_home, zero_width)
    d_stream_two, d_grid_home, tap_grid_out = grid_tail_back(cotangent[0])
    d_grid_attended = to_grid(to_exchanged(d_grid_home), WIN)
    d_grid_windows, tap_grid_in = grid_core_back(d_grid_attended)
    d_normed_three = to_home(from_grid(d_grid_windows, height, breadth, WIN))
    d_stream_extra, d_gain_grid = grid_front_back(d_normed_three)
    d_stream_two = d_stream_two + d_stream_extra
    d_stream_one, d_gain_block, tap_block_in, tap_block_out = block_back(d_stream_two)
    d_conv, d_wide_tail, tap_project = tail_back(d_stream_one)
    d_conv_ext = extended_2(d_conv.astype(jnp.bfloat16), (("sy", 0), ("sx", 1)), 1)
    d_conv_ext = d_conv_ext.astype(jnp.float32).at[1:-1, 1:-1].set(d_conv)
    d_kernel = kernel_back(d_conv)[0]
    d_inner = depthwise_back(d_conv_ext, dw_kernel).astype(jnp.bfloat16)
    d_normed, tap_expand = expand_back(d_inner)
    d_wide_front, d_gain_conv = front_back(d_normed)
    token_grad = (d_wide_tail + d_wide_front).astype(jnp.bfloat16)
    local_grads = (
        d_gain_conv,
        outer_sum(normed, tap_expand),
        d_kernel,
        outer_sum(activated, tap_project),
        d_gain_block,
        outer_sum(block_saved[0], tap_block_in),
        outer_sum(block_saved[1], tap_block_out),
        d_gain_grid,
        outer_sum(grid_windows, tap_grid_in),
        outer_sum(grid_home, tap_grid_out),
    )
    summed = reduce_grads(local_grads)
    return (
        output_tile[None],
        token_grad[None],
        summed[0],
        summed[1],
        summed[2],
        summed[3],
        summed[4],
        summed[5],
        summed[6],
        summed[7],
        summed[8],
        summed[9],
    )


def solution(mesh):
    return jax.shard_map(
        body,
        mesh=mesh,
        in_specs=(
            P("rep", "sy", "sx", None),
            P("rep", "sy", "sx", None),
            P(),
            P(),
            P(),
            P(),
            P(),
            P(),
            P(),
            P(),
            P(),
            P(),
        ),
        out_specs=(
            P("rep", "sy", "sx", None),
            P("rep", "sy", "sx", None),
            P("rep"),
            P("rep", None),
            P("rep", None),
            P("rep", None),
            P("rep"),
            P("rep", None),
            P("rep", None),
            P("rep"),
            P("rep", None),
            P("rep", None),
        ),
        check_vma=False,
    )
```

```python
import jax
import jax.numpy as jnp
from jax import lax
from jax.sharding import PartitionSpec as P

HEADS = 8
WIN = 8


EPSILON = 1e-05


def as_sent(value):

    def short(part):
        return part.astype(jnp.bfloat16) if part.dtype == jnp.float32 else part

    return jax.tree.map(short, value)


def extended_2(cells, sides, width):
    height, breadth, channels = cells.shape
    row_count = lax.axis_size("sy")
    col_count = lax.axis_size("sx")
    tiles = row_count * col_count
    row_at = lax.axis_index("sy")
    col_at = lax.axis_index("sx")
    span = max(height, breadth)

    def lay(line):
        return jnp.pad(line, ((0, span - line.shape[0]), (0, 0)))

    sends = (
        ((-1, 0), lay(cells[0])),
        ((1, 0), lay(cells[height - 1])),
        ((0, -1), lay(cells[:, 0])),
        ((0, 1), lay(cells[:, breadth - 1])),
        ((-1, -1), lay(cells[0, :1])),
        ((-1, 1), lay(cells[0, breadth - 1 :])),
        ((1, -1), lay(cells[height - 1, :1])),
        ((1, 1), lay(cells[height - 1, breadth - 1 :])),
    )
    slot = lax.broadcasted_iota(jnp.int32, (tiles, 1, 1), 0)
    row_step = slot // col_count - row_at
    col_step = slot % col_count - col_at
    outgoing = jnp.zeros((tiles, span, channels), cells.dtype)
    for (up, side), line in sends:
        outgoing = jnp.where((row_step == up) & (col_step == side), line[None], outgoing)
    incoming = lax.all_to_all(outgoing, ("sy", "sx"), split_axis=0, concat_axis=0, tiled=True)

    def take(up, side):
        row = row_at + up
        col = col_at + side
        valid = (row >= 0) & (row < row_count) & (col >= 0) & (col < col_count)
        index = jnp.clip(row, 0, row_count - 1) * col_count + jnp.clip(col, 0, col_count - 1)
        line = lax.dynamic_index_in_dim(incoming, index, 0, keepdims=False)
        return jnp.where(valid, line, jnp.zeros_like(line))

    top = jnp.concatenate([take(-1, -1)[:1], take(-1, 0)[:breadth], take(-1, 1)[:1]], axis=0)
    bottom = jnp.concatenate([take(1, -1)[:1], take(1, 0)[:breadth], take(1, 1)[:1]], axis=0)
    middle = jnp.concatenate([take(0, -1)[:height, None], cells, take(0, 1)[:height, None]], axis=1)
    return jnp.concatenate([top[None], middle, bottom[None]], axis=0)

def widen(values):
    return lax.optimization_barrier(values).astype(jnp.float32)


def layer_norm(values, gain):
    row_mean = jnp.mean(values, axis=-1, keepdims=True)
    centred = values - row_mean
    variance = jnp.mean(centred * centred, axis=-1, keepdims=True)
    return centred * lax.rsqrt(variance + EPSILON) * gain


def project_rows(values, weight):
    leading = values.shape[:-1]
    flattened = values.reshape(-1, values.shape[-1])
    product = jnp.dot(flattened, weight, preferred_element_type=jnp.float32)
    return product.reshape(leading + (weight.shape[1],))


def outer_sum(left_side, right_side):
    left_flat = left_side.reshape(-1, left_side.shape[-1])
    right_flat = right_side.reshape(-1, right_side.shape[-1]).astype(jnp.bfloat16)
    return lax.dot_general(
        left_flat, right_flat, (((0,), (0,)), ((), ())), preferred_element_type=jnp.float32
    )


def to_windows(image, side):
    height, breadth, channels = image.shape
    blocks = image.reshape(height // side, side, breadth // side, side, channels)
    return blocks.transpose(0, 2, 1, 3, 4).reshape(-1, side * side, channels)


def from_windows(windows, height, breadth, side):
    channels = windows.shape[-1]
    blocks = windows.reshape(height // side, breadth // side, side, side, channels)
    return blocks.transpose(0, 2, 1, 3, 4).reshape(height, breadth, channels)


def to_grid(image, side):
    height, breadth, channels = image.shape
    blocks = image.reshape(side, height // side, side, breadth // side, channels)
    return blocks.transpose(1, 3, 0, 2, 4).reshape(-1, side * side, channels)


def from_grid(windows, height, breadth, side):
    channels = windows.shape[-1]
    blocks = windows.reshape(height // side, breadth // side, side, side, channels)
    return blocks.transpose(2, 0, 3, 1, 4).reshape(height, breadth, channels)


def window_attention(windows, weight, tap_in, heads):
    count, members, channels = windows.shape
    head_width = channels // heads
    qkv_rows = (project_rows(windows, weight) + tap_in).astype(jnp.bfloat16)
    queries = qkv_rows[..., :channels]
    key_rows = qkv_rows[..., channels : 2 * channels]
    value_rows = qkv_rows[..., 2 * channels :]
    owner = lax.broadcasted_iota(jnp.int32, (heads, channels), 1) // head_width
    mask = (owner == lax.broadcasted_iota(jnp.int32, (heads, channels), 0)).astype(jnp.bfloat16)
    masked = queries[:, None, :, :] * mask[None, :, None, :]
    scores = jnp.einsum(
        "whqc,wkc->whqk", masked, key_rows, preferred_element_type=jnp.float32
    ) * head_width ** (-0.5)
    softmax_out = jax.nn.softmax(scores, axis=-1).astype(jnp.bfloat16)
    spread = jnp.einsum(
        "whqk,wkc->whqc", softmax_out, value_rows, preferred_element_type=jnp.float32
    )
    attended = (spread * mask[None, :, None, :].astype(jnp.float32)).sum(axis=1)
    return attended.astype(jnp.bfloat16)

def depthwise(extended, kernel):
    height = extended.shape[0] - 2
    breadth = extended.shape[1] - 2
    widened = widen(extended)
    summed = jnp.zeros((height, breadth, extended.shape[2]), jnp.float32)
    for tap_index in range(9):
        row_step, col_step = divmod(tap_index, 3)
        summed = (
            summed
            + widened[row_step : row_step + height, col_step : col_step + breadth]
            * kernel[:, tap_index]
        )
    return summed


def depthwise_back(grad_ext, kernel):
    height = grad_ext.shape[0] - 2
    breadth = grad_ext.shape[1] - 2
    summed = jnp.zeros((height, breadth, grad_ext.shape[2]), jnp.float32)
    for tap_index in range(9):
        row_step, col_step = divmod(tap_index, 3)
        summed = (
            summed
            + grad_ext[2 - row_step : 2 - row_step + height, 2 - col_step : 2 - col_step + breadth]
            * kernel[:, tap_index]
        )
    return summed


def swap_blocks(blocks):
    sy_count, sx_count, row_part, col_part, channels = blocks.shape
    flattened = blocks.reshape(sy_count * sx_count, row_part, col_part, channels)
    moved = lax.all_to_all(
        as_sent(flattened), ("sy", "sx"), split_axis=0, concat_axis=0, tiled=True
    ).astype(flattened.dtype)
    return moved.reshape(blocks.shape)


def to_exchanged(image):
    height, breadth, channels = image.shape
    sy_count = lax.axis_size("sy")
    sx_count = lax.axis_size("sx")
    blocks = image.reshape(height // sy_count, sy_count, breadth // sx_count, sx_count, channels)
    moved = swap_blocks(blocks.transpose(1, 3, 0, 2, 4))
    return moved.transpose(0, 2, 1, 3, 4).reshape(height, breadth, channels)


def to_home(image):
    height, breadth, channels = image.shape
    sy_count = lax.axis_size("sy")
    sx_count = lax.axis_size("sx")
    blocks = image.reshape(sy_count, height // sy_count, sx_count, breadth // sx_count, channels)
    moved = swap_blocks(blocks.transpose(0, 2, 1, 3, 4))
    return moved.transpose(2, 0, 3, 1, 4).reshape(height, breadth, channels)


def exchange_sum(values, axes, axis):
    moved = lax.all_to_all(values.astype(jnp.bfloat16), axes, split_axis=axis, concat_axis=axis, tiled=True)
    return moved.astype(jnp.float32).sum(axis)


def tile_sum(wide):
    parts = lax.axis_size("rep")
    tiles = lax.axis_size(("sy", "sx"))
    packed = jnp.concatenate(wide, axis=1)
    channels, width = packed.shape
    piece = channels // parts // tiles
    return exchange_sum(packed.reshape(parts, tiles, piece, width), ("sy", "sx"), 1)


def reduce_packed(groups):
    tiles = lax.axis_size(("sy", "sx"))
    widths = [piece.shape[1] for wide in groups for piece in wide]
    local = jnp.concatenate([tile_sum(wide) for wide in groups], axis=-1)
    parts, piece, width = local.shape
    local = exchange_sum(local, "rep", 0)
    spread = jnp.broadcast_to(local[None].astype(jnp.bfloat16), (tiles, piece, width))
    total = lax.all_to_all(spread, ("sy", "sx"), split_axis=0, concat_axis=0, tiled=True)
    total = total.astype(jnp.float32).reshape(piece * tiles, width)
    cuts = []
    offset = 0
    for size in widths:
        cuts.append(total[:, offset : offset + size])
        offset += size
    return cuts


def pad_lanes(columns):
    joined = jnp.concatenate(columns, axis=1)
    return jnp.pad(joined, ((0, 0), (0, -joined.shape[1] % 128)))


def reduce_grads(grads):
    channels = grads[0].shape[0]
    taps = grads[2].shape[1]
    kernel_cols = taps * grads[2].shape[0] // channels
    cuts = reduce_packed(
        (
            [grads[5], grads[6], grads[8], grads[9], pad_lanes([grads[4][:, None], grads[7][:, None]])],
            [grads[1], grads[3].reshape(channels, -1), pad_lanes([grads[2].reshape(channels, -1), grads[0][:, None]])],
        )
    )
    return (
        cuts[7][:, kernel_cols],
        cuts[5],
        cuts[7][:, :kernel_cols].reshape(-1, taps),
        cuts[6].reshape(-1, grads[3].shape[1]),
        cuts[4][:, 0],
        cuts[0],
        cuts[1],
        cuts[4][:, 1],
        cuts[2],
        cuts[3],
    )

def body(
    features,
    cotangent,
    gain_conv,
    expand_weight,
    dw_kernel,
    project_weight,
    gain_block,
    block_inward,
    block_outward,
    gain_grid,
    grid_inward,
    grid_outward,
):
    image = features[0]
    height, breadth, channels = image.shape
    expand_units = expand_weight.shape[1]
    window_count = height * breadth // (WIN * WIN)
    zero_width = jnp.zeros((height, breadth, channels), jnp.float32)
    zero_expand = jnp.zeros((height, breadth, expand_units), jnp.float32)
    zero_qkv = jnp.zeros((window_count, WIN * WIN, 3 * channels), jnp.float32)
    widened = image.astype(jnp.float32)

    def conv_front(wide_in, gain_in):
        return layer_norm(wide_in, gain_in).astype(jnp.bfloat16)

    normed, front_back = jax.vjp(conv_front, widened, gain_conv)

    def expand_fn(normed_in, tap_in):
        return jax.nn.gelu(project_rows(normed_in, expand_weight) + tap_in).astype(jnp.bfloat16)

    inner, expand_back = jax.vjp(expand_fn, normed, zero_expand)
    inner_ext = extended_2(inner, (("sy", 0), ("sx", 1)), 1)

    def conv_only(kernel_in):
        return depthwise(inner_ext, kernel_in)

    conv_out, kernel_back = jax.vjp(conv_only, dw_kernel)

    def conv_tail(conv_in, wide_in, tap_in):
        activated_in = jax.nn.gelu(conv_in).astype(jnp.bfloat16)
        return (wide_in + project_rows(activated_in, project_weight) + tap_in, activated_in)

    stream_one, tail_back, activated = jax.vjp(
        conv_tail, conv_out, widened, zero_width, has_aux=True
    )

    def block_layer(stream_in, gain_in, tap_in, tap_out):
        normed_two = layer_norm(stream_in, gain_in).astype(jnp.bfloat16)
        windows = to_windows(normed_two, WIN)
        attended = window_attention(windows, block_inward, tap_in, HEADS)
        attended_home = from_windows(attended, height, breadth, WIN)
        return (
            stream_in + project_rows(attended_home, block_outward) + tap_out,
            (windows, attended_home),
        )

    stream_two, block_back, block_saved = jax.vjp(
        block_layer, stream_one, gain_block, zero_qkv, zero_width, has_aux=True
    )

    def grid_front(stream_in, gain_in):
        return layer_norm(stream_in, gain_in).astype(jnp.bfloat16)

    normed_three, grid_front_back = jax.vjp(grid_front, stream_two, gain_grid)
    grid_windows = to_grid(to_exchanged(normed_three), WIN)

    def grid_core(windows_in, tap_in):
        return window_attention(windows_in, grid_inward, tap_in, HEADS)

    grid_attended, grid_core_back = jax.vjp(grid_core, grid_windows, zero_qkv)
    grid_home = to_home(from_grid(grid_attended, height, breadth, WIN))

    def grid_tail(stream_in, attended_in, tap_in):
        return (stream_in + project_rows(attended_in, grid_outward) + tap_in).astype(jnp.bfloat16)

    output_tile, grid_tail_back = jax.vjp(grid_tail, stream_two, grid_home, zero_width)
    d_stream_two, d_grid_home, tap_grid_out = grid_tail_back(cotangent[0])
    d_grid_attended = to_grid(to_exchanged(d_grid_home), WIN)
    d_grid_windows, tap_grid_in = grid_core_back(d_grid_attended)
    d_normed_three = to_home(from_grid(d_grid_windows, height, breadth, WIN))
    d_stream_extra, d_gain_grid = grid_front_back(d_normed_three)
    d_stream_two = d_stream_two + d_stream_extra
    d_stream_one, d_gain_block, tap_block_in, tap_block_out = block_back(d_stream_two)
    d_conv, d_wide_tail, tap_project = tail_back(d_stream_one)
    d_conv_ext = extended_2(d_conv.astype(jnp.bfloat16), (("sy", 0), ("sx", 1)), 1)
    d_conv_ext = d_conv_ext.astype(jnp.float32).at[1:-1, 1:-1].set(d_conv)
    d_kernel = kernel_back(d_conv)[0]
    d_inner = depthwise_back(d_conv_ext, dw_kernel).astype(jnp.bfloat16)
    d_normed, tap_expand = expand_back(d_inner)
    d_wide_front, d_gain_conv = front_back(d_normed)
    token_grad = (d_wide_tail + d_wide_front).astype(jnp.bfloat16)
    local_grads = (
        d_gain_conv,
        outer_sum(normed, tap_expand),
        d_kernel,
        outer_sum(activated, tap_project),
        d_gain_block,
        outer_sum(block_saved[0], tap_block_in),
        outer_sum(block_saved[1], tap_block_out),
        d_gain_grid,
        outer_sum(grid_windows, tap_grid_in),
        outer_sum(grid_home, tap_grid_out),
    )
    summed = reduce_grads(local_grads)
    return (
        output_tile[None],
        token_grad[None],
        summed[0],
        summed[1],
        summed[2],
        summed[3],
        summed[4],
        summed[5],
        summed[6],
        summed[7],
        summed[8],
        summed[9],
    )


def solution(mesh):
    return jax.shard_map(
        body,
        mesh=mesh,
        in_specs=(
            P("rep", "sy", "sx", None),
            P("rep", "sy", "sx", None),
            P(),
            P(),
            P(),
            P(),
            P(),
            P(),
            P(),
            P(),
            P(),
            P(),
        ),
        out_specs=(
            P("rep", "sy", "sx", None),
            P("rep", "sy", "sx", None),
            P("rep"),
            P("rep", None),
            P("rep", None),
            P("rep", None),
            P("rep"),
            P("rep", None),
            P("rep", None),
            P("rep"),
            P("rep", None),
            P("rep", None),
        ),
        check_vma=False,
    )
```

```python
import jax
import jax.numpy as jnp
from jax import lax
from jax.sharding import PartitionSpec as P

HEADS = 8
WIN = 8


EPSILON = 1e-05


def as_sent(value):

    def short(part):
        return part.astype(jnp.bfloat16) if part.dtype == jnp.float32 else part

    return jax.tree.map(short, value)


def extended_2(cells, sides, width):
    height, breadth, channels = cells.shape
    row_count = lax.axis_size("sy")
    col_count = lax.axis_size("sx")
    tiles = row_count * col_count
    row_at = lax.axis_index("sy")
    col_at = lax.axis_index("sx")
    span = max(height, breadth)

    def lay(line):
        return jnp.pad(line, ((0, span - line.shape[0]), (0, 0)))

    sends = (
        ((-1, 0), lay(cells[0])),
        ((1, 0), lay(cells[height - 1])),
        ((0, -1), lay(cells[:, 0])),
        ((0, 1), lay(cells[:, breadth - 1])),
        ((-1, -1), lay(cells[0, :1])),
        ((-1, 1), lay(cells[0, breadth - 1 :])),
        ((1, -1), lay(cells[height - 1, :1])),
        ((1, 1), lay(cells[height - 1, breadth - 1 :])),
    )
    slot = lax.broadcasted_iota(jnp.int32, (tiles, 1, 1), 0)
    row_step = slot // col_count - row_at
    col_step = slot % col_count - col_at
    outgoing = jnp.zeros((tiles, span, channels), cells.dtype)
    for (up, side), line in sends:
        outgoing = jnp.where((row_step == up) & (col_step == side), line[None], outgoing)
    incoming = lax.all_to_all(outgoing, ("sy", "sx"), split_axis=0, concat_axis=0, tiled=True)

    def take(up, side):
        row = row_at + up
        col = col_at + side
        valid = (row >= 0) & (row < row_count) & (col >= 0) & (col < col_count)
        index = jnp.clip(row, 0, row_count - 1) * col_count + jnp.clip(col, 0, col_count - 1)
        line = lax.dynamic_index_in_dim(incoming, index, 0, keepdims=False)
        return jnp.where(valid, line, jnp.zeros_like(line))

    top = jnp.concatenate([take(-1, -1)[:1], take(-1, 0)[:breadth], take(-1, 1)[:1]], axis=0)
    bottom = jnp.concatenate([take(1, -1)[:1], take(1, 0)[:breadth], take(1, 1)[:1]], axis=0)
    middle = jnp.concatenate([take(0, -1)[:height, None], cells, take(0, 1)[:height, None]], axis=1)
    return jnp.concatenate([top[None], middle, bottom[None]], axis=0)

def widen(values):
    return lax.optimization_barrier(values).astype(jnp.float32)


def layer_norm(values, gain):
    row_mean = jnp.mean(values, axis=-1, keepdims=True)
    centred = values - row_mean
    variance = jnp.mean(centred * centred, axis=-1, keepdims=True)
    return centred * lax.rsqrt(variance + EPSILON) * gain


def project_rows(values, weight):
    leading = values.shape[:-1]
    flattened = values.reshape(-1, values.shape[-1])
    product = jnp.dot(flattened, weight, preferred_element_type=jnp.float32)
    return product.reshape(leading + (weight.shape[1],))


def outer_sum(left_side, right_side):
    left_flat = left_side.reshape(-1, left_side.shape[-1])
    right_flat = right_side.reshape(-1, right_side.shape[-1]).astype(jnp.bfloat16)
    return lax.dot_general(
        left_flat, right_flat, (((0,), (0,)), ((), ())), preferred_element_type=jnp.float32
    )


def to_windows(image, side):
    height, breadth, channels = image.shape
    blocks = image.reshape(height // side, side, breadth // side, side, channels)
    return blocks.transpose(0, 2, 1, 3, 4).reshape(-1, side * side, channels)


def from_windows(windows, height, breadth, side):
    channels = windows.shape[-1]
    blocks = windows.reshape(height // side, breadth // side, side, side, channels)
    return blocks.transpose(0, 2, 1, 3, 4).reshape(height, breadth, channels)


def to_grid(image, side):
    height, breadth, channels = image.shape
    blocks = image.reshape(side, height // side, side, breadth // side, channels)
    return blocks.transpose(1, 3, 0, 2, 4).reshape(-1, side * side, channels)


def from_grid(windows, height, breadth, side):
    channels = windows.shape[-1]
    blocks = windows.reshape(height // side, breadth // side, side, side, channels)
    return blocks.transpose(2, 0, 3, 1, 4).reshape(height, breadth, channels)


def window_attention(windows, weight, tap_in, heads):
    count, members, channels = windows.shape
    head_width = channels // heads
    qkv_rows = (project_rows(windows, weight) + tap_in).astype(jnp.bfloat16)
    queries = qkv_rows[..., :channels]
    key_rows = qkv_rows[..., channels : 2 * channels]
    value_rows = qkv_rows[..., 2 * channels :]
    owner = lax.broadcasted_iota(jnp.int32, (heads, channels), 1) // head_width
    mask = (owner == lax.broadcasted_iota(jnp.int32, (heads, channels), 0)).astype(jnp.bfloat16)
    masked = queries[:, None, :, :] * mask[None, :, None, :]
    scores = jnp.einsum(
        "whqc,wkc->whqk", masked, key_rows, preferred_element_type=jnp.float32
    ) * head_width ** (-0.5)
    softmax_out = jax.nn.softmax(scores, axis=-1).astype(jnp.bfloat16)
    spread = jnp.einsum(
        "whqk,wkc->whqc", softmax_out, value_rows, preferred_element_type=jnp.float32
    )
    attended = (spread * mask[None, :, None, :].astype(jnp.float32)).sum(axis=1)
    return attended.astype(jnp.bfloat16)

def depthwise(extended, kernel):
    height = extended.shape[0] - 2
    breadth = extended.shape[1] - 2
    widened = widen(extended)
    summed = jnp.zeros((height, breadth, extended.shape[2]), jnp.float32)
    for tap_index in range(9):
        row_step, col_step = divmod(tap_index, 3)
        summed = (
            summed
            + widened[row_step : row_step + height, col_step : col_step + breadth]
            * kernel[:, tap_index]
        )
    return summed


def depthwise_back(grad_ext, kernel):
    height = grad_ext.shape[0] - 2
    breadth = grad_ext.shape[1] - 2
    summed = jnp.zeros((height, breadth, grad_ext.shape[2]), jnp.float32)
    for tap_index in range(9):
        row_step, col_step = divmod(tap_index, 3)
        summed = (
            summed
            + grad_ext[2 - row_step : 2 - row_step + height, 2 - col_step : 2 - col_step + breadth]
            * kernel[:, tap_index]
        )
    return summed


def swap_blocks(blocks):
    sy_count, sx_count, row_part, col_part, channels = blocks.shape
    flattened = blocks.reshape(sy_count * sx_count, row_part, col_part, channels)
    moved = lax.all_to_all(
        as_sent(flattened), ("sy", "sx"), split_axis=0, concat_axis=0, tiled=True
    ).astype(flattened.dtype)
    return moved.reshape(blocks.shape)


def to_exchanged(image):
    height, breadth, channels = image.shape
    sy_count = lax.axis_size("sy")
    sx_count = lax.axis_size("sx")
    blocks = image.reshape(height // sy_count, sy_count, breadth // sx_count, sx_count, channels)
    moved = swap_blocks(blocks.transpose(1, 3, 0, 2, 4))
    return moved.transpose(0, 2, 1, 3, 4).reshape(height, breadth, channels)


def to_home(image):
    height, breadth, channels = image.shape
    sy_count = lax.axis_size("sy")
    sx_count = lax.axis_size("sx")
    blocks = image.reshape(sy_count, height // sy_count, sx_count, breadth // sx_count, channels)
    moved = swap_blocks(blocks.transpose(0, 2, 1, 3, 4))
    return moved.transpose(2, 0, 3, 1, 4).reshape(height, breadth, channels)


def exchange_sum(values, axes, axis):
    moved = lax.all_to_all(values.astype(jnp.bfloat16), axes, split_axis=axis, concat_axis=axis, tiled=True)
    return moved.astype(jnp.float32).sum(axis)


def tile_sum(wide):
    parts = lax.axis_size("rep")
    tiles = lax.axis_size(("sy", "sx"))
    packed = jnp.concatenate(wide, axis=1)
    channels, width = packed.shape
    piece = channels // parts // tiles
    return exchange_sum(packed.reshape(parts, tiles, piece, width), ("sy", "sx"), 1)


def reduce_packed(groups):
    tiles = lax.axis_size(("sy", "sx"))
    widths = [piece.shape[1] for wide in groups for piece in wide]
    sums = []
    for wide in groups:
        if sums:
            sums[-1], wide = lax.optimization_barrier((sums[-1], wide))
        sums.append(tile_sum(wide))
    local = jnp.concatenate(sums, axis=-1)
    parts, piece, width = local.shape
    local = exchange_sum(local, "rep", 0)
    spread = jnp.broadcast_to(local[None].astype(jnp.bfloat16), (tiles, piece, width))
    total = lax.all_to_all(spread, ("sy", "sx"), split_axis=0, concat_axis=0, tiled=True)
    total = total.astype(jnp.float32).reshape(piece * tiles, width)
    cuts = []
    offset = 0
    for size in widths:
        cuts.append(total[:, offset : offset + size])
        offset += size
    return cuts


def pad_lanes(columns):
    joined = jnp.concatenate(columns, axis=1)
    return jnp.pad(joined, ((0, 0), (0, -joined.shape[1] % 128)))


def reduce_grads(grads):
    channels = grads[0].shape[0]
    taps = grads[2].shape[1]
    kernel_cols = taps * grads[2].shape[0] // channels
    cuts = reduce_packed(
        (
            [grads[5], grads[6], grads[8], grads[9], grads[3].reshape(channels, -1), pad_lanes([grads[4][:, None], grads[7][:, None]])],
            [grads[1], pad_lanes([grads[2].reshape(channels, -1), grads[0][:, None]])],
        )
    )
    return (
        cuts[7][:, kernel_cols],
        cuts[6],
        cuts[7][:, :kernel_cols].reshape(-1, taps),
        cuts[4].reshape(-1, grads[3].shape[1]),
        cuts[5][:, 0],
        cuts[0],
        cuts[1],
        cuts[5][:, 1],
        cuts[2],
        cuts[3],
    )

def body(
    features,
    cotangent,
    gain_conv,
    expand_weight,
    dw_kernel,
    project_weight,
    gain_block,
    block_inward,
    block_outward,
    gain_grid,
    grid_inward,
    grid_outward,
):
    image = features[0]
    height, breadth, channels = image.shape
    expand_units = expand_weight.shape[1]
    window_count = height * breadth // (WIN * WIN)
    zero_width = jnp.zeros((height, breadth, channels), jnp.float32)
    zero_expand = jnp.zeros((height, breadth, expand_units), jnp.float32)
    zero_qkv = jnp.zeros((window_count, WIN * WIN, 3 * channels), jnp.float32)
    widened = image.astype(jnp.float32)

    def conv_front(wide_in, gain_in):
        return layer_norm(wide_in, gain_in).astype(jnp.bfloat16)

    normed, front_back = jax.vjp(conv_front, widened, gain_conv)

    def expand_fn(normed_in, tap_in):
        return jax.nn.gelu(project_rows(normed_in, expand_weight) + tap_in).astype(jnp.bfloat16)

    inner, expand_back = jax.vjp(expand_fn, normed, zero_expand)
    inner_ext = extended_2(inner, (("sy", 0), ("sx", 1)), 1)

    def conv_only(kernel_in):
        return depthwise(inner_ext, kernel_in)

    conv_out, kernel_back = jax.vjp(conv_only, dw_kernel)

    def conv_tail(conv_in, wide_in, tap_in):
        activated_in = jax.nn.gelu(conv_in).astype(jnp.bfloat16)
        return (wide_in + project_rows(activated_in, project_weight) + tap_in, activated_in)

    stream_one, tail_back, activated = jax.vjp(
        conv_tail, conv_out, widened, zero_width, has_aux=True
    )

    def block_layer(stream_in, gain_in, tap_in, tap_out):
        normed_two = layer_norm(stream_in, gain_in).astype(jnp.bfloat16)
        windows = to_windows(normed_two, WIN)
        attended = window_attention(windows, block_inward, tap_in, HEADS)
        attended_home = from_windows(attended, height, breadth, WIN)
        return (
            stream_in + project_rows(attended_home, block_outward) + tap_out,
            (windows, attended_home),
        )

    stream_two, block_back, block_saved = jax.vjp(
        block_layer, stream_one, gain_block, zero_qkv, zero_width, has_aux=True
    )

    def grid_front(stream_in, gain_in):
        return layer_norm(stream_in, gain_in).astype(jnp.bfloat16)

    normed_three, grid_front_back = jax.vjp(grid_front, stream_two, gain_grid)
    grid_windows = to_grid(to_exchanged(normed_three), WIN)

    def grid_core(windows_in, tap_in):
        return window_attention(windows_in, grid_inward, tap_in, HEADS)

    grid_attended, grid_core_back = jax.vjp(grid_core, grid_windows, zero_qkv)
    grid_home = to_home(from_grid(grid_attended, height, breadth, WIN))

    def grid_tail(stream_in, attended_in, tap_in):
        return (stream_in + project_rows(attended_in, grid_outward) + tap_in).astype(jnp.bfloat16)

    output_tile, grid_tail_back = jax.vjp(grid_tail, stream_two, grid_home, zero_width)
    d_stream_two, d_grid_home, tap_grid_out = grid_tail_back(cotangent[0])
    d_grid_attended = to_grid(to_exchanged(d_grid_home), WIN)
    d_grid_windows, tap_grid_in = grid_core_back(d_grid_attended)
    d_normed_three = to_home(from_grid(d_grid_windows, height, breadth, WIN))
    d_stream_extra, d_gain_grid = grid_front_back(d_normed_three)
    d_stream_two = d_stream_two + d_stream_extra
    d_stream_one, d_gain_block, tap_block_in, tap_block_out = block_back(d_stream_two)
    d_conv, d_wide_tail, tap_project = tail_back(d_stream_one)
    d_conv_ext = extended_2(d_conv, (("sy", 0), ("sx", 1)), 1)
    d_kernel = kernel_back(d_conv)[0]
    d_inner = depthwise_back(d_conv_ext, dw_kernel).astype(jnp.bfloat16)
    d_normed, tap_expand = expand_back(d_inner)
    d_wide_front, d_gain_conv = front_back(d_normed)
    token_grad = (d_wide_tail + d_wide_front).astype(jnp.bfloat16)
    local_grads = (
        d_gain_conv,
        outer_sum(normed, tap_expand),
        d_kernel,
        outer_sum(activated, tap_project),
        d_gain_block,
        outer_sum(block_saved[0], tap_block_in),
        outer_sum(block_saved[1], tap_block_out),
        d_gain_grid,
        outer_sum(grid_windows, tap_grid_in),
        outer_sum(grid_home, tap_grid_out),
    )
    summed = reduce_grads(local_grads)
    return (
        output_tile[None],
        token_grad[None],
        summed[0],
        summed[1],
        summed[2],
        summed[3],
        summed[4],
        summed[5],
        summed[6],
        summed[7],
        summed[8],
        summed[9],
    )


def solution(mesh):
    return jax.shard_map(
        body,
        mesh=mesh,
        in_specs=(
            P("rep", "sy", "sx", None),
            P("rep", "sy", "sx", None),
            P(),
            P(),
            P(),
            P(),
            P(),
            P(),
            P(),
            P(),
            P(),
            P(),
        ),
        out_specs=(
            P("rep", "sy", "sx", None),
            P("rep", "sy", "sx", None),
            P("rep"),
            P("rep", None),
            P("rep", None),
            P("rep", None),
            P("rep"),
            P("rep", None),
            P("rep", None),
            P("rep"),
            P("rep", None),
            P("rep", None),
        ),
        check_vma=False,
    )
```

```python
import jax
import jax.numpy as jnp
from jax import lax
from jax.sharding import PartitionSpec as P

HEADS = 8
WIN = 8


EPSILON = 1e-05


def as_sent(value):

    def short(part):
        return part.astype(jnp.bfloat16) if part.dtype == jnp.float32 else part

    return jax.tree.map(short, value)


def extended_2(cells, sides, width):
    height, breadth, channels = cells.shape
    row_count = lax.axis_size("sy")
    col_count = lax.axis_size("sx")
    tiles = row_count * col_count
    row_at = lax.axis_index("sy")
    col_at = lax.axis_index("sx")
    span = max(height, breadth)

    def lay(line):
        return jnp.pad(line, ((0, span - line.shape[0]), (0, 0)))

    sends = (
        ((-1, 0), lay(cells[0])),
        ((1, 0), lay(cells[height - 1])),
        ((0, -1), lay(cells[:, 0])),
        ((0, 1), lay(cells[:, breadth - 1])),
        ((-1, -1), lay(cells[0, :1])),
        ((-1, 1), lay(cells[0, breadth - 1 :])),
        ((1, -1), lay(cells[height - 1, :1])),
        ((1, 1), lay(cells[height - 1, breadth - 1 :])),
    )
    slot = lax.broadcasted_iota(jnp.int32, (tiles, 1, 1), 0)
    row_step = slot // col_count - row_at
    col_step = slot % col_count - col_at
    outgoing = jnp.zeros((tiles, span, channels), cells.dtype)
    for (up, side), line in sends:
        outgoing = jnp.where((row_step == up) & (col_step == side), line[None], outgoing)
    incoming = lax.all_to_all(outgoing, ("sy", "sx"), split_axis=0, concat_axis=0, tiled=True)

    def take(up, side):
        row = row_at + up
        col = col_at + side
        valid = (row >= 0) & (row < row_count) & (col >= 0) & (col < col_count)
        index = jnp.clip(row, 0, row_count - 1) * col_count + jnp.clip(col, 0, col_count - 1)
        line = lax.dynamic_index_in_dim(incoming, index, 0, keepdims=False)
        return jnp.where(valid, line, jnp.zeros_like(line))

    top = jnp.concatenate([take(-1, -1)[:1], take(-1, 0)[:breadth], take(-1, 1)[:1]], axis=0)
    bottom = jnp.concatenate([take(1, -1)[:1], take(1, 0)[:breadth], take(1, 1)[:1]], axis=0)
    middle = jnp.concatenate([take(0, -1)[:height, None], cells, take(0, 1)[:height, None]], axis=1)
    return jnp.concatenate([top[None], middle, bottom[None]], axis=0)

def widen(values):
    return lax.optimization_barrier(values).astype(jnp.float32)


def layer_norm(values, gain):
    row_mean = jnp.mean(values, axis=-1, keepdims=True)
    centred = values - row_mean
    variance = jnp.mean(centred * centred, axis=-1, keepdims=True)
    return centred * lax.rsqrt(variance + EPSILON) * gain


def project_rows(values, weight):
    leading = values.shape[:-1]
    flattened = values.reshape(-1, values.shape[-1])
    product = jnp.dot(flattened, weight, preferred_element_type=jnp.float32)
    return product.reshape(leading + (weight.shape[1],))


def outer_sum(left_side, right_side):
    left_flat = left_side.reshape(-1, left_side.shape[-1])
    right_flat = right_side.reshape(-1, right_side.shape[-1]).astype(jnp.bfloat16)
    return lax.dot_general(
        left_flat, right_flat, (((0,), (0,)), ((), ())), preferred_element_type=jnp.float32
    )


def to_windows(image, side):
    height, breadth, channels = image.shape
    blocks = image.reshape(height // side, side, breadth // side, side, channels)
    return blocks.transpose(0, 2, 1, 3, 4).reshape(-1, side * side, channels)


def from_windows(windows, height, breadth, side):
    channels = windows.shape[-1]
    blocks = windows.reshape(height // side, breadth // side, side, side, channels)
    return blocks.transpose(0, 2, 1, 3, 4).reshape(height, breadth, channels)


def to_grid(image, side):
    height, breadth, channels = image.shape
    blocks = image.reshape(side, height // side, side, breadth // side, channels)
    return blocks.transpose(1, 3, 0, 2, 4).reshape(-1, side * side, channels)


def from_grid(windows, height, breadth, side):
    channels = windows.shape[-1]
    blocks = windows.reshape(height // side, breadth // side, side, side, channels)
    return blocks.transpose(2, 0, 3, 1, 4).reshape(height, breadth, channels)


def window_attention(windows, weight, tap_in, heads):
    count, members, channels = windows.shape
    head_width = channels // heads
    qkv_rows = (project_rows(windows, weight) + tap_in).astype(jnp.bfloat16)
    queries = qkv_rows[..., :channels]
    key_rows = qkv_rows[..., channels : 2 * channels]
    value_rows = qkv_rows[..., 2 * channels :]
    owner = lax.broadcasted_iota(jnp.int32, (heads, channels), 1) // head_width
    mask = (owner == lax.broadcasted_iota(jnp.int32, (heads, channels), 0)).astype(jnp.bfloat16)
    masked = queries[:, None, :, :] * mask[None, :, None, :]
    scores = jnp.einsum(
        "whqc,wkc->whqk", masked, key_rows, preferred_element_type=jnp.float32
    ) * head_width ** (-0.5)
    softmax_out = jax.nn.softmax(scores, axis=-1).astype(jnp.bfloat16)
    spread = jnp.einsum(
        "whqk,wkc->whqc", softmax_out, value_rows, preferred_element_type=jnp.float32
    )
    attended = (spread * mask[None, :, None, :].astype(jnp.float32)).sum(axis=1)
    return attended.astype(jnp.bfloat16)

def depthwise(extended, kernel):
    height = extended.shape[0] - 2
    breadth = extended.shape[1] - 2
    widened = widen(extended)
    summed = jnp.zeros((height, breadth, extended.shape[2]), jnp.float32)
    for tap_index in range(9):
        row_step, col_step = divmod(tap_index, 3)
        summed = (
            summed
            + widened[row_step : row_step + height, col_step : col_step + breadth]
            * kernel[:, tap_index]
        )
    return summed


def depthwise_back(grad_ext, kernel):
    height = grad_ext.shape[0] - 2
    breadth = grad_ext.shape[1] - 2
    summed = jnp.zeros((height, breadth, grad_ext.shape[2]), jnp.float32)
    for tap_index in range(9):
        row_step, col_step = divmod(tap_index, 3)
        summed = (
            summed
            + grad_ext[2 - row_step : 2 - row_step + height, 2 - col_step : 2 - col_step + breadth]
            * kernel[:, tap_index]
        )
    return summed


def swap_blocks(blocks):
    sy_count, sx_count, row_part, col_part, channels = blocks.shape
    flattened = blocks.reshape(sy_count * sx_count, row_part, col_part, channels)
    moved = lax.all_to_all(
        as_sent(flattened), ("sy", "sx"), split_axis=0, concat_axis=0, tiled=True
    ).astype(flattened.dtype)
    return moved.reshape(blocks.shape)


def to_exchanged(image):
    height, breadth, channels = image.shape
    sy_count = lax.axis_size("sy")
    sx_count = lax.axis_size("sx")
    blocks = image.reshape(height // sy_count, sy_count, breadth // sx_count, sx_count, channels)
    moved = swap_blocks(blocks.transpose(1, 3, 0, 2, 4))
    return moved.transpose(0, 2, 1, 3, 4).reshape(height, breadth, channels)


def to_home(image):
    height, breadth, channels = image.shape
    sy_count = lax.axis_size("sy")
    sx_count = lax.axis_size("sx")
    blocks = image.reshape(sy_count, height // sy_count, sx_count, breadth // sx_count, channels)
    moved = swap_blocks(blocks.transpose(0, 2, 1, 3, 4))
    return moved.transpose(2, 0, 3, 1, 4).reshape(height, breadth, channels)


def home_with_sums(image, grads):
    height, breadth, channels = image.shape
    sy_count = lax.axis_size("sy")
    sx_count = lax.axis_size("sx")
    tiles = sy_count * sx_count
    parts = lax.axis_size("rep")
    blocks = image.reshape(sy_count, height // sy_count, sx_count, breadth // sx_count, channels)
    blocks = blocks.transpose(0, 2, 1, 3, 4)
    block_shape = blocks.shape
    rows, width = grads.shape
    piece = rows // parts // tiles
    pieces = grads.reshape(parts, tiles, piece, width).transpose(1, 0, 2, 3)
    joined = jnp.concatenate(
        [blocks.reshape(tiles, -1), pieces.astype(jnp.bfloat16).reshape(tiles, -1)], axis=1
    )
    moved = lax.all_to_all(joined, ("sy", "sx"), split_axis=0, concat_axis=0, tiled=True)
    image_part = moved[:, : blocks.size // tiles].reshape(block_shape)
    home = image_part.transpose(2, 0, 3, 1, 4).reshape(height, breadth, channels)
    sums = moved[:, blocks.size // tiles :].reshape(tiles, parts, piece, width)
    return home, sums.astype(jnp.float32).sum(0)


def exchange_sum(values, axes, axis):
    moved = lax.all_to_all(values.astype(jnp.bfloat16), axes, split_axis=axis, concat_axis=axis, tiled=True)
    return moved.astype(jnp.float32).sum(axis)


def tile_sum(wide):
    parts = lax.axis_size("rep")
    tiles = lax.axis_size(("sy", "sx"))
    packed = jnp.concatenate(wide, axis=1)
    channels, width = packed.shape
    piece = channels // parts // tiles
    return exchange_sum(packed.reshape(parts, tiles, piece, width), ("sy", "sx"), 1)


def reduce_packed(groups):
    tiles = lax.axis_size(("sy", "sx"))
    widths = [piece.shape[-1] for wide in groups for piece in wide]
    local = jnp.concatenate(
        [wide[0] if wide[0].ndim == 3 else tile_sum(wide) for wide in groups], axis=-1
    )
    parts, piece, width = local.shape
    local = exchange_sum(local, "rep", 0)
    spread = jnp.broadcast_to(local[None].astype(jnp.bfloat16), (tiles, piece, width))
    total = lax.all_to_all(spread, ("sy", "sx"), split_axis=0, concat_axis=0, tiled=True)
    total = total.astype(jnp.float32).reshape(piece * tiles, width)
    cuts = []
    offset = 0
    for size in widths:
        cuts.append(total[:, offset : offset + size])
        offset += size
    return cuts


def pad_lanes(columns):
    joined = jnp.concatenate(columns, axis=1)
    return jnp.pad(joined, ((0, 0), (0, -joined.shape[1] % 128)))


def reduce_grads(grads):
    channels = grads[0].shape[0]
    taps = grads[2].shape[1]
    kernel_cols = taps * grads[2].shape[0] // channels
    cuts = reduce_packed(
        (
            [grads[9]],
            [grads[5], grads[6], pad_lanes([grads[4][:, None], grads[7][:, None]])],
            [grads[1], grads[3].reshape(channels, -1), pad_lanes([grads[2].reshape(channels, -1), grads[0][:, None]])],
        )
    )
    return (
        cuts[6][:, kernel_cols],
        cuts[4],
        cuts[6][:, :kernel_cols].reshape(-1, taps),
        cuts[5].reshape(-1, grads[3].shape[1]),
        cuts[3][:, 0],
        cuts[1],
        cuts[2],
        cuts[3][:, 1],
        cuts[0][:, : grads[5].shape[1]],
        cuts[0][:, grads[5].shape[1] :],
    )

def body(
    features,
    cotangent,
    gain_conv,
    expand_weight,
    dw_kernel,
    project_weight,
    gain_block,
    block_inward,
    block_outward,
    gain_grid,
    grid_inward,
    grid_outward,
):
    image = features[0]
    height, breadth, channels = image.shape
    expand_units = expand_weight.shape[1]
    window_count = height * breadth // (WIN * WIN)
    zero_width = jnp.zeros((height, breadth, channels), jnp.float32)
    zero_expand = jnp.zeros((height, breadth, expand_units), jnp.float32)
    zero_qkv = jnp.zeros((window_count, WIN * WIN, 3 * channels), jnp.float32)
    widened = image.astype(jnp.float32)

    def conv_front(wide_in, gain_in):
        return layer_norm(wide_in, gain_in).astype(jnp.bfloat16)

    normed, front_back = jax.vjp(conv_front, widened, gain_conv)

    def expand_fn(normed_in, tap_in):
        return jax.nn.gelu(project_rows(normed_in, expand_weight) + tap_in).astype(jnp.bfloat16)

    inner, expand_back = jax.vjp(expand_fn, normed, zero_expand)
    inner_ext = extended_2(inner, (("sy", 0), ("sx", 1)), 1)

    def conv_only(kernel_in):
        return depthwise(inner_ext, kernel_in)

    conv_out, kernel_back = jax.vjp(conv_only, dw_kernel)

    def conv_tail(conv_in, wide_in, tap_in):
        activated_in = jax.nn.gelu(conv_in).astype(jnp.bfloat16)
        return (wide_in + project_rows(activated_in, project_weight) + tap_in, activated_in)

    stream_one, tail_back, activated = jax.vjp(
        conv_tail, conv_out, widened, zero_width, has_aux=True
    )

    def block_layer(stream_in, gain_in, tap_in, tap_out):
        normed_two = layer_norm(stream_in, gain_in).astype(jnp.bfloat16)
        windows = to_windows(normed_two, WIN)
        attended = window_attention(windows, block_inward, tap_in, HEADS)
        attended_home = from_windows(attended, height, breadth, WIN)
        return (
            stream_in + project_rows(attended_home, block_outward) + tap_out,
            (windows, attended_home),
        )

    stream_two, block_back, block_saved = jax.vjp(
        block_layer, stream_one, gain_block, zero_qkv, zero_width, has_aux=True
    )

    def grid_front(stream_in, gain_in):
        return layer_norm(stream_in, gain_in).astype(jnp.bfloat16)

    normed_three, grid_front_back = jax.vjp(grid_front, stream_two, gain_grid)
    grid_windows = to_grid(to_exchanged(normed_three), WIN)

    def grid_core(windows_in, tap_in):
        return window_attention(windows_in, grid_inward, tap_in, HEADS)

    grid_attended, grid_core_back = jax.vjp(grid_core, grid_windows, zero_qkv)
    grid_home = to_home(from_grid(grid_attended, height, breadth, WIN))

    def grid_tail(stream_in, attended_in, tap_in):
        return (stream_in + project_rows(attended_in, grid_outward) + tap_in).astype(jnp.bfloat16)

    output_tile, grid_tail_back = jax.vjp(grid_tail, stream_two, grid_home, zero_width)
    d_stream_two, d_grid_home, tap_grid_out = grid_tail_back(cotangent[0])
    d_grid_attended = to_grid(to_exchanged(d_grid_home), WIN)
    d_grid_windows, tap_grid_in = grid_core_back(d_grid_attended)
    grid_weight_grads = jnp.concatenate(
        [outer_sum(grid_windows, tap_grid_in), outer_sum(grid_home, tap_grid_out)], axis=1
    )
    d_normed_three, grid_tile_sum = home_with_sums(
        from_grid(d_grid_windows, height, breadth, WIN), grid_weight_grads
    )
    d_stream_extra, d_gain_grid = grid_front_back(d_normed_three)
    d_stream_two = d_stream_two + d_stream_extra
    d_stream_one, d_gain_block, tap_block_in, tap_block_out = block_back(d_stream_two)
    d_conv, d_wide_tail, tap_project = tail_back(d_stream_one)
    d_conv_ext = extended_2(d_conv, (("sy", 0), ("sx", 1)), 1)
    d_kernel = kernel_back(d_conv)[0]
    d_inner = depthwise_back(d_conv_ext, dw_kernel).astype(jnp.bfloat16)
    d_normed, tap_expand = expand_back(d_inner)
    d_wide_front, d_gain_conv = front_back(d_normed)
    token_grad = (d_wide_tail + d_wide_front).astype(jnp.bfloat16)
    local_grads = (
        d_gain_conv,
        outer_sum(normed, tap_expand),
        d_kernel,
        outer_sum(activated, tap_project),
        d_gain_block,
        outer_sum(block_saved[0], tap_block_in),
        outer_sum(block_saved[1], tap_block_out),
        d_gain_grid,
        grid_weight_grads,
        grid_tile_sum,
    )
    summed = reduce_grads(local_grads)
    return (
        output_tile[None],
        token_grad[None],
        summed[0],
        summed[1],
        summed[2],
        summed[3],
        summed[4],
        summed[5],
        summed[6],
        summed[7],
        summed[8],
        summed[9],
    )


def solution(mesh):
    return jax.shard_map(
        body,
        mesh=mesh,
        in_specs=(
            P("rep", "sy", "sx", None),
            P("rep", "sy", "sx", None),
            P(),
            P(),
            P(),
            P(),
            P(),
            P(),
            P(),
            P(),
            P(),
            P(),
        ),
        out_specs=(
            P("rep", "sy", "sx", None),
            P("rep", "sy", "sx", None),
            P("rep"),
            P("rep", None),
            P("rep", None),
            P("rep", None),
            P("rep"),
            P("rep", None),
            P("rep", None),
            P("rep"),
            P("rep", None),
            P("rep", None),
        ),
        check_vma=False,
    )
```

```python
import jax
import jax.numpy as jnp
from jax import lax
from jax.sharding import PartitionSpec as P

HEADS = 8
WIN = 8


EPSILON = 1e-05


def as_sent(value):

    def short(part):
        return part.astype(jnp.bfloat16) if part.dtype == jnp.float32 else part

    return jax.tree.map(short, value)


def extended_2(cells, sides, width):
    height, breadth, channels = cells.shape
    row_count = lax.axis_size("sy")
    col_count = lax.axis_size("sx")
    tiles = row_count * col_count
    row_at = lax.axis_index("sy")
    col_at = lax.axis_index("sx")
    span = max(height, breadth)

    def lay(line):
        return jnp.pad(line, ((0, span - line.shape[0]), (0, 0)))

    sends = (
        ((-1, 0), lay(cells[0])),
        ((1, 0), lay(cells[height - 1])),
        ((0, -1), lay(cells[:, 0])),
        ((0, 1), lay(cells[:, breadth - 1])),
        ((-1, -1), lay(cells[0, :1])),
        ((-1, 1), lay(cells[0, breadth - 1 :])),
        ((1, -1), lay(cells[height - 1, :1])),
        ((1, 1), lay(cells[height - 1, breadth - 1 :])),
    )
    slot = lax.broadcasted_iota(jnp.int32, (tiles, 1, 1), 0)
    row_step = slot // col_count - row_at
    col_step = slot % col_count - col_at
    outgoing = jnp.zeros((tiles, span, channels), cells.dtype)
    for (up, side), line in sends:
        outgoing = jnp.where((row_step == up) & (col_step == side), line[None], outgoing)
    incoming = lax.all_to_all(outgoing, ("sy", "sx"), split_axis=0, concat_axis=0, tiled=True)

    def take(up, side):
        row = row_at + up
        col = col_at + side
        valid = (row >= 0) & (row < row_count) & (col >= 0) & (col < col_count)
        index = jnp.clip(row, 0, row_count - 1) * col_count + jnp.clip(col, 0, col_count - 1)
        line = lax.dynamic_index_in_dim(incoming, index, 0, keepdims=False)
        return jnp.where(valid, line, jnp.zeros_like(line))

    top = jnp.concatenate([take(-1, -1)[:1], take(-1, 0)[:breadth], take(-1, 1)[:1]], axis=0)
    bottom = jnp.concatenate([take(1, -1)[:1], take(1, 0)[:breadth], take(1, 1)[:1]], axis=0)
    middle = jnp.concatenate([take(0, -1)[:height, None], cells, take(0, 1)[:height, None]], axis=1)
    return jnp.concatenate([top[None], middle, bottom[None]], axis=0)

def widen(values):
    return lax.optimization_barrier(values).astype(jnp.float32)


def layer_norm(values, gain):
    row_mean = jnp.mean(values, axis=-1, keepdims=True)
    centred = values - row_mean
    variance = jnp.mean(centred * centred, axis=-1, keepdims=True)
    return centred * lax.rsqrt(variance + EPSILON) * gain


def project_rows(values, weight):
    leading = values.shape[:-1]
    flattened = values.reshape(-1, values.shape[-1])
    product = jnp.dot(flattened, weight, preferred_element_type=jnp.float32)
    return product.reshape(leading + (weight.shape[1],))


def outer_sum(left_side, right_side):
    left_flat = left_side.reshape(-1, left_side.shape[-1])
    right_flat = right_side.reshape(-1, right_side.shape[-1]).astype(jnp.bfloat16)
    return lax.dot_general(
        left_flat, right_flat, (((0,), (0,)), ((), ())), preferred_element_type=jnp.float32
    )


def to_windows(image, side):
    height, breadth, channels = image.shape
    blocks = image.reshape(height // side, side, breadth // side, side, channels)
    return blocks.transpose(0, 2, 1, 3, 4).reshape(-1, side * side, channels)


def from_windows(windows, height, breadth, side):
    channels = windows.shape[-1]
    blocks = windows.reshape(height // side, breadth // side, side, side, channels)
    return blocks.transpose(0, 2, 1, 3, 4).reshape(height, breadth, channels)


def to_grid(image, side):
    height, breadth, channels = image.shape
    blocks = image.reshape(side, height // side, side, breadth // side, channels)
    return blocks.transpose(1, 3, 0, 2, 4).reshape(-1, side * side, channels)


def from_grid(windows, height, breadth, side):
    channels = windows.shape[-1]
    blocks = windows.reshape(height // side, breadth // side, side, side, channels)
    return blocks.transpose(2, 0, 3, 1, 4).reshape(height, breadth, channels)


def window_attention(windows, weight, tap_in, heads):
    count, members, channels = windows.shape
    head_width = channels // heads
    qkv_rows = (project_rows(windows, weight) + tap_in).astype(jnp.bfloat16)
    queries = qkv_rows[..., :channels]
    key_rows = qkv_rows[..., channels : 2 * channels]
    value_rows = qkv_rows[..., 2 * channels :]
    owner = lax.broadcasted_iota(jnp.int32, (heads, channels), 1) // head_width
    mask = (owner == lax.broadcasted_iota(jnp.int32, (heads, channels), 0)).astype(jnp.bfloat16)
    masked = queries[:, None, :, :] * mask[None, :, None, :]
    scores = jnp.einsum(
        "whqc,wkc->whqk", masked, key_rows, preferred_element_type=jnp.float32
    ) * head_width ** (-0.5)
    softmax_out = jax.nn.softmax(scores, axis=-1).astype(jnp.bfloat16)
    spread = jnp.einsum(
        "whqk,wkc->whqc", softmax_out, value_rows, preferred_element_type=jnp.float32
    )
    attended = (spread * mask[None, :, None, :].astype(jnp.float32)).sum(axis=1)
    return attended.astype(jnp.bfloat16)

def depthwise(extended, kernel):
    height = extended.shape[0] - 2
    breadth = extended.shape[1] - 2
    widened = widen(extended)
    summed = jnp.zeros((height, breadth, extended.shape[2]), jnp.float32)
    for tap_index in range(9):
        row_step, col_step = divmod(tap_index, 3)
        summed = (
            summed
            + widened[row_step : row_step + height, col_step : col_step + breadth]
            * kernel[:, tap_index]
        )
    return summed


def depthwise_back(grad_ext, kernel):
    height = grad_ext.shape[0] - 2
    breadth = grad_ext.shape[1] - 2
    summed = jnp.zeros((height, breadth, grad_ext.shape[2]), jnp.float32)
    for tap_index in range(9):
        row_step, col_step = divmod(tap_index, 3)
        summed = (
            summed
            + grad_ext[2 - row_step : 2 - row_step + height, 2 - col_step : 2 - col_step + breadth]
            * kernel[:, tap_index]
        )
    return summed


def swap_blocks(blocks):
    sy_count, sx_count, row_part, col_part, channels = blocks.shape
    flattened = blocks.reshape(sy_count * sx_count, row_part, col_part, channels)
    moved = lax.all_to_all(
        as_sent(flattened), ("sy", "sx"), split_axis=0, concat_axis=0, tiled=True
    ).astype(flattened.dtype)
    return moved.reshape(blocks.shape)


def to_exchanged(image):
    height, breadth, channels = image.shape
    sy_count = lax.axis_size("sy")
    sx_count = lax.axis_size("sx")
    blocks = image.reshape(height // sy_count, sy_count, breadth // sx_count, sx_count, channels)
    moved = swap_blocks(blocks.transpose(1, 3, 0, 2, 4))
    return moved.transpose(0, 2, 1, 3, 4).reshape(height, breadth, channels)


def to_home(image):
    height, breadth, channels = image.shape
    sy_count = lax.axis_size("sy")
    sx_count = lax.axis_size("sx")
    blocks = image.reshape(sy_count, height // sy_count, sx_count, breadth // sx_count, channels)
    moved = swap_blocks(blocks.transpose(0, 2, 1, 3, 4))
    return moved.transpose(2, 0, 3, 1, 4).reshape(height, breadth, channels)


def grid_split(image):
    height, breadth, channels = image.shape
    rows = lax.axis_size("sy")
    cols = lax.axis_size("sx")
    row_part, col_part = height // rows, breadth // cols
    row_class, col_class = height // WIN, breadth // WIN
    return rows, cols, row_part, col_part, row_class, col_class


def grid_from_home(image):
    height, breadth, channels = image.shape
    rows, cols, row_part, col_part, row_class, col_class = grid_split(image)
    if row_part % row_class or col_part % col_class:
        return to_grid(to_exchanged(image), WIN)
    blocks = image.reshape(row_part, rows, col_part, cols, channels)
    moved = swap_blocks(blocks.transpose(1, 3, 0, 2, 4))
    moved = moved.reshape(rows, cols, row_part // row_class, row_class, col_part // col_class, col_class, channels)
    return moved.transpose(3, 5, 0, 2, 1, 4, 6).reshape(row_class * col_class, -1, channels)


def grid_to_home(windows, height, breadth):
    channels = windows.shape[-1]
    rows, cols, row_part, col_part, row_class, col_class = grid_split(jax.ShapeDtypeStruct((height, breadth, channels), windows.dtype))
    if row_part % row_class or col_part % col_class:
        return to_home(from_grid(windows, height, breadth, WIN))
    parts = windows.reshape(row_class, col_class, rows, row_part // row_class, cols, col_part // col_class, channels)
    blocks = parts.transpose(2, 4, 3, 0, 5, 1, 6).reshape(rows, cols, row_part, col_part, channels)
    moved = swap_blocks(blocks)
    return moved.transpose(2, 0, 3, 1, 4).reshape(height, breadth, channels)


def exchange_sum(values, axes, axis):
    moved = lax.all_to_all(values.astype(jnp.bfloat16), axes, split_axis=axis, concat_axis=axis, tiled=True)
    return moved.astype(jnp.float32).sum(axis)


def tile_sum(wide):
    parts = lax.axis_size("rep")
    tiles = lax.axis_size(("sy", "sx"))
    packed = jnp.concatenate(wide, axis=1)
    channels, width = packed.shape
    piece = channels // parts // tiles
    return exchange_sum(packed.reshape(parts, tiles, piece, width), ("sy", "sx"), 1)


def reduce_packed(groups):
    tiles = lax.axis_size(("sy", "sx"))
    widths = [piece.shape[1] for wide in groups for piece in wide]
    local = jnp.concatenate([tile_sum(wide) for wide in groups], axis=-1)
    parts, piece, width = local.shape
    local = exchange_sum(local, "rep", 0)
    spread = jnp.broadcast_to(local[None].astype(jnp.bfloat16), (tiles, piece, width))
    total = lax.all_to_all(spread, ("sy", "sx"), split_axis=0, concat_axis=0, tiled=True)
    total = total.astype(jnp.float32).reshape(piece * tiles, width)
    cuts = []
    offset = 0
    for size in widths:
        cuts.append(total[:, offset : offset + size])
        offset += size
    return cuts


def pad_lanes(columns):
    joined = jnp.concatenate(columns, axis=1)
    return jnp.pad(joined, ((0, 0), (0, -joined.shape[1] % 128)))


def reduce_grads(grads):
    channels = grads[0].shape[0]
    taps = grads[2].shape[1]
    kernel_cols = taps * grads[2].shape[0] // channels
    cuts = reduce_packed(
        (
            [grads[5], grads[6], grads[8], grads[9], pad_lanes([grads[4][:, None], grads[7][:, None]])],
            [grads[1], grads[3].reshape(channels, -1), pad_lanes([grads[2].reshape(channels, -1), grads[0][:, None]])],
        )
    )
    return (
        cuts[7][:, kernel_cols],
        cuts[5],
        cuts[7][:, :kernel_cols].reshape(-1, taps),
        cuts[6].reshape(-1, grads[3].shape[1]),
        cuts[4][:, 0],
        cuts[0],
        cuts[1],
        cuts[4][:, 1],
        cuts[2],
        cuts[3],
    )

def body(
    features,
    cotangent,
    gain_conv,
    expand_weight,
    dw_kernel,
    project_weight,
    gain_block,
    block_inward,
    block_outward,
    gain_grid,
    grid_inward,
    grid_outward,
):
    image = features[0]
    height, breadth, channels = image.shape
    expand_units = expand_weight.shape[1]
    window_count = height * breadth // (WIN * WIN)
    zero_width = jnp.zeros((height, breadth, channels), jnp.float32)
    zero_expand = jnp.zeros((height, breadth, expand_units), jnp.float32)
    zero_qkv = jnp.zeros((window_count, WIN * WIN, 3 * channels), jnp.float32)
    widened = image.astype(jnp.float32)

    def conv_front(wide_in, gain_in):
        return layer_norm(wide_in, gain_in).astype(jnp.bfloat16)

    normed, front_back = jax.vjp(conv_front, widened, gain_conv)

    def expand_fn(normed_in, tap_in):
        return jax.nn.gelu(project_rows(normed_in, expand_weight) + tap_in).astype(jnp.bfloat16)

    inner, expand_back = jax.vjp(expand_fn, normed, zero_expand)
    inner_ext = extended_2(inner, (("sy", 0), ("sx", 1)), 1)

    def conv_only(kernel_in):
        return depthwise(inner_ext, kernel_in)

    conv_out, kernel_back = jax.vjp(conv_only, dw_kernel)

    def conv_tail(conv_in, wide_in, tap_in):
        activated_in = jax.nn.gelu(conv_in).astype(jnp.bfloat16)
        return (wide_in + project_rows(activated_in, project_weight) + tap_in, activated_in)

    stream_one, tail_back, activated = jax.vjp(
        conv_tail, conv_out, widened, zero_width, has_aux=True
    )

    def block_layer(stream_in, gain_in, tap_in, tap_out):
        normed_two = layer_norm(stream_in, gain_in).astype(jnp.bfloat16)
        windows = to_windows(normed_two, WIN)
        attended = window_attention(windows, block_inward, tap_in, HEADS)
        attended_home = from_windows(attended, height, breadth, WIN)
        return (
            stream_in + project_rows(attended_home, block_outward) + tap_out,
            (windows, attended_home),
        )

    stream_two, block_back, block_saved = jax.vjp(
        block_layer, stream_one, gain_block, zero_qkv, zero_width, has_aux=True
    )

    def grid_front(stream_in, gain_in):
        return layer_norm(stream_in, gain_in).astype(jnp.bfloat16)

    normed_three, grid_front_back = jax.vjp(grid_front, stream_two, gain_grid)
    grid_windows = grid_from_home(normed_three)

    def grid_core(windows_in, tap_in):
        return window_attention(windows_in, grid_inward, tap_in, HEADS)

    grid_attended, grid_core_back = jax.vjp(grid_core, grid_windows, zero_qkv)
    grid_home = grid_to_home(grid_attended, height, breadth)

    def grid_tail(stream_in, attended_in, tap_in):
        return (stream_in + project_rows(attended_in, grid_outward) + tap_in).astype(jnp.bfloat16)

    output_tile, grid_tail_back = jax.vjp(grid_tail, stream_two, grid_home, zero_width)
    d_stream_two, d_grid_home, tap_grid_out = grid_tail_back(cotangent[0])
    d_grid_attended = grid_from_home(d_grid_home)
    d_grid_windows, tap_grid_in = grid_core_back(d_grid_attended)
    d_normed_three = grid_to_home(d_grid_windows, height, breadth)
    d_stream_extra, d_gain_grid = grid_front_back(d_normed_three)
    d_stream_two = d_stream_two + d_stream_extra
    d_stream_one, d_gain_block, tap_block_in, tap_block_out = block_back(d_stream_two)
    d_conv, d_wide_tail, tap_project = tail_back(d_stream_one)
    d_conv_ext = extended_2(d_conv, (("sy", 0), ("sx", 1)), 1)
    d_kernel = kernel_back(d_conv)[0]
    d_inner = depthwise_back(d_conv_ext, dw_kernel).astype(jnp.bfloat16)
    d_normed, tap_expand = expand_back(d_inner)
    d_wide_front, d_gain_conv = front_back(d_normed)
    token_grad = (d_wide_tail + d_wide_front).astype(jnp.bfloat16)
    local_grads = (
        d_gain_conv,
        outer_sum(normed, tap_expand),
        d_kernel,
        outer_sum(activated, tap_project),
        d_gain_block,
        outer_sum(block_saved[0], tap_block_in),
        outer_sum(block_saved[1], tap_block_out),
        d_gain_grid,
        outer_sum(grid_windows, tap_grid_in),
        outer_sum(grid_home, tap_grid_out),
    )
    summed = reduce_grads(local_grads)
    return (
        output_tile[None],
        token_grad[None],
        summed[0],
        summed[1],
        summed[2],
        summed[3],
        summed[4],
        summed[5],
        summed[6],
        summed[7],
        summed[8],
        summed[9],
    )


def solution(mesh):
    return jax.shard_map(
        body,
        mesh=mesh,
        in_specs=(
            P("rep", "sy", "sx", None),
            P("rep", "sy", "sx", None),
            P(),
            P(),
            P(),
            P(),
            P(),
            P(),
            P(),
            P(),
            P(),
            P(),
        ),
        out_specs=(
            P("rep", "sy", "sx", None),
            P("rep", "sy", "sx", None),
            P("rep"),
            P("rep", None),
            P("rep", None),
            P("rep", None),
            P("rep"),
            P("rep", None),
            P("rep", None),
            P("rep"),
            P("rep", None),
            P("rep", None),
        ),
        check_vma=False,
    )
```
